32 devices in a mesh: rep: 2 (over x), span: 2 (over core), tp: 8 (over z, y).
Axes of the slice: x: 2, y: 2, z: 4, core: 2. Of those that a mesh axis runs over, the one named last changes fastest.
Arguments:
- hidden_in: bfloat16 [16, 128, 6144], P(('rep', 'span'), None, 'tp'), parts along dimension 0, may hold values from -6 to 6
- levels: int32 [16], P(('rep', 'span')), parts along dimension 0, may hold values from 0 to 3
- order: int32 [16], P('rep'), parts along dimension 0, may hold values from 0 to 7, each once
- cache_mask: int32 [16, 8], P('rep'), parts along dimension 0, may hold values 0 or 1
- finished: int32 [2], P('rep'), parts along dimension 0, may hold values from 0 to 7
- cache_kv: bfloat16 [16, 128, 2, 1024], P(('rep', 'span'), None, None, 'tp'), parts along dimension 0, may hold values from -300 to 300
- modulation: bfloat16 [4, 6, 6144], replicated, may hold values from 0.5 to 1.5
- w_qkv: bfloat16 [6144, 3, 1024], P(None, None, 'tp'), may hold values from -0.109375 to 0.109375
- w_out: bfloat16 [1024, 6144], P('tp'), may hold values from -0.375 to 0.375
- w_up: bfloat16 [6144, 4096], P(None, ('span', 'tp')), may hold values from -0.078125 to 0.078125
- w_down: bfloat16 [4096, 6144], P(('span', 'tp')), may hold values from -0.09375 to 0.09375
Outputs:
- layer_out: bfloat16 [16, 128, 6144], P(('rep', 'span'), None, 'tp'), parts along dimension 0
The draws below stay inside these ranges and needn't reach their ends.
There are 2 independent parts, one for each index of `rep`. The reference program is written for one: setup_inputs(seed, part) draws one part's arguments, and reference() takes and returns one part's arrays. A program takes and returns all parts, laid end to end along the dimension named above; an argument that names none is the same for every part. Nothing has to cross between parts.
All inputs are finite; a program needn't handle non-finite values.
Results may differ from the reference program's by a relative error of at most 0.025.
The reference program's roundings to bfloat16 on the way (of `attn_in`, `projected`, `weights`, `attended`, `mlp_in` and `hidden_units`) count: a program that leaves them out, or rounds other values in their place, can miss the bound.
Values may be sent and summed in bfloat16 or wider, within the bound.
No kernel may reach another device: no remote copies, remote signals or barrier semaphores. Data moves between devices by JAX's collectives and lax.ppermute only.
A program may use at most 128 MiB of HBM per device.

```python
import math
import jax
import jax.numpy as jnp
from jax import lax

D = 6144
HEAD_DIM = 128
LEVELS = 4
ROWS = 128
SPANS = 8
HEADS = 8
FF = 4096
N_TP = 8


def draw_cache_kv(key, part):
    key_base = jax.random.fold_in(key, 11)
    base = jax.random.normal(key_base, (SPANS, ROWS, 2, HEADS * HEAD_DIM), jnp.float32)
    return jnp.clip(base, -300.0, 300.0).astype(jnp.bfloat16)


def place_ends(array, own_key, smallest, high):
    longest = array.shape.index(max(array.shape))
    spots = []
    for shift in (0, 1):
        where = [jax.random.randint(jax.random.fold_in(own_key, axis), (), 0, length) for axis, length in enumerate(array.shape)]
        where[longest] = (where[longest] + shift) % array.shape[longest]
        spots.append(tuple(where))
    return array.at[spots[0]].set(smallest).at[spots[1]].set(high)


def level_of(rng, extent, shards, smallest, high):
    def one(axis_at, parts):
        steps = jax.random.uniform(jax.random.fold_in(jax.random.fold_in(rng, 6), axis_at), (parts,), jnp.float32, smallest / len(shards), high / len(shards))
        return jnp.repeat(jnp.exp(steps), extent[axis_at] // parts).reshape((-1,) + (1,) * (len(extent) - axis_at - 1))

    level = one(*shards[0])
    for cut in shards[1:]:
        level = level * one(*cut)
    return level


def bell_draw(own_key, extent, width, limit, split=(), kind=jnp.bfloat16):
    level = level_of(own_key, extent, split, -0.22, 0.18) if split else 1.0
    array = jax.random.normal(own_key, extent, jnp.float32) * width * level
    return jnp.minimum(jnp.maximum(array, -limit), limit).astype(kind)


def setup_inputs(seed: int = 0, part: int = 0) -> dict:
    streams_of = jax.random.split(jax.random.key(seed), 12)
    part_splits = jax.random.split(jax.random.fold_in(streams_of[11], part), 12)
    return {
        "hidden_in": bell_draw(part_splits[0], (SPANS, ROWS, D), 1.0, 6.0, ((0, 2), (2, 8))),
        "levels": place_ends(jax.random.randint(part_splits[1], (SPANS,), 0, LEVELS), jax.random.fold_in(part_splits[1], 1), 0, LEVELS - 1).astype(jnp.int32),
        "order": jax.random.permutation(part_splits[2], SPANS).astype(jnp.int32),
        "cache_mask": place_ends((jax.random.randint(part_splits[3], (SPANS, SPANS), 0, 4) < 1).astype(jnp.int32), jax.random.fold_in(part_splits[3], 1), 0, 1),
        "finished": jax.random.randint(part_splits[4], (1,), 0, SPANS).astype(jnp.int32),
        "cache_kv": draw_cache_kv(jax.random.fold_in(jax.random.fold_in(streams_of[11], part), 71), part),
        "modulation": jnp.clip(jax.random.uniform(streams_of[6], (LEVELS, 6, D), jnp.float32, 0.5, 1.5), 0.5, 1.5).astype(jnp.bfloat16),
        "w_qkv": bell_draw(streams_of[7], (D, 3, HEADS * HEAD_DIM), (D // 2) ** -0.5, 0.109375, ((2, 8),)),
        "w_out": bell_draw(streams_of[8], (HEADS * HEAD_DIM, D), (HEADS * HEAD_DIM // 4) ** -0.5, 0.375, ((0, 8),)),
        "w_up": bell_draw(streams_of[9], (D, FF), D ** -0.5, 0.078125, ((1, 16),)),
        "w_down": bell_draw(streams_of[10], (FF, D), FF ** -0.5, 0.09375, ((0, 16),)),
    }


EPSILON = 1e-06
NEGATIVE = -1e+30

def normalize(values):
    return values * lax.rsqrt(lax.optimization_barrier(jnp.mean(values * values, axis=-1, keepdims=True)) + EPSILON)

def grouped_sum(left, right, groups):
    left_groups = left.reshape(left.shape[0], groups, -1)
    right_groups = right.reshape(groups, -1, right.shape[1])

    def add_group(group, running):
        term = jnp.dot(left_groups[:, group], right_groups[group], preferred_element_type=jnp.float32)
        rounded = lax.optimization_barrier(term.astype(jnp.bfloat16))
        return running + rounded.astype(jnp.float32)
    return lax.fori_loop(0, groups, add_group, jnp.zeros((left.shape[0], right.shape[1]), jnp.float32))

def split_sum(left, right, groups):
    half_width = left.shape[1] // (2 * groups)
    left_parts = left.reshape(left.shape[0], 2, groups, half_width)
    right_parts = right.reshape(2, groups, half_width, right.shape[1])

    def add_group(group, running):
        left_block = left_parts[:, :, group].reshape(left.shape[0], 2 * half_width)
        right_block = right_parts[:, group].reshape(2 * half_width, right.shape[1])
        term = jnp.dot(left_block, right_block, preferred_element_type=jnp.float32)
        rounded = lax.optimization_barrier(term.astype(jnp.bfloat16))
        return running + rounded.astype(jnp.float32)
    return lax.fori_loop(0, groups, add_group, jnp.zeros((left.shape[0], right.shape[1]), jnp.float32))

def reference(hidden_in, levels, order, cache_mask, finished, cache_kv, modulation, w_qkv, w_out, w_up, w_down):
    mod_rows = modulation.astype(jnp.float32)[levels][:, :, None, :]
    start_x = hidden_in.astype(jnp.float32)
    attn_in = (normalize(start_x) * mod_rows[:, 1] + mod_rows[:, 0]).astype(jnp.bfloat16)
    projected = jnp.dot(attn_in.reshape(SPANS * ROWS, D), w_qkv.reshape(D, 3 * HEADS * HEAD_DIM), preferred_element_type=jnp.float32).astype(jnp.bfloat16)
    projected = projected.reshape(SPANS, ROWS, 3, HEADS, HEAD_DIM)
    queries = projected[:, :, 0]
    cache_heads = cache_kv.reshape(SPANS * ROWS, 2, HEADS, HEAD_DIM)
    keys = jnp.concatenate([cache_heads[:, 0], projected[:, :, 1].reshape(SPANS * ROWS, HEADS, HEAD_DIM)], axis=0)
    values = jnp.concatenate([cache_heads[:, 1], projected[:, :, 2].reshape(SPANS * ROWS, HEADS, HEAD_DIM)], axis=0)
    positions = jnp.arange(SPANS, dtype=jnp.int32)
    cache_seen = (cache_mask == 1) | (positions[None, :] == finished[0])
    fresh_seen = order[None, :] <= order[:, None]
    seen = jnp.concatenate([jnp.repeat(cache_seen, ROWS, axis=1), jnp.repeat(fresh_seen, ROWS, axis=1)], axis=1)
    scores = jnp.einsum('cqhd,khd->chqk', queries.astype(jnp.float32), keys.astype(jnp.float32))
    scores = scores * (1.0 / math.sqrt(HEAD_DIM))
    scores = jnp.where(seen[:, None, None, :], scores, NEGATIVE)
    row_max = lax.optimization_barrier(jnp.max(scores, axis=3, keepdims=True))
    exp_terms = jnp.exp(scores - row_max)
    weights = (exp_terms / lax.optimization_barrier(jnp.sum(exp_terms, axis=3, keepdims=True))).astype(jnp.bfloat16)
    attended = jnp.einsum('chqk,khd->cqhd', weights.astype(jnp.float32), values.astype(jnp.float32))
    attended = attended.astype(jnp.bfloat16).reshape(SPANS * ROWS, HEADS * HEAD_DIM)
    attn_out = grouped_sum(attended, w_out, N_TP).reshape(SPANS, ROWS, D)
    residual = start_x + mod_rows[:, 2] * attn_out
    mlp_in = (normalize(residual) * mod_rows[:, 4] + mod_rows[:, 3]).astype(jnp.bfloat16)
    hidden_units = jax.nn.gelu(jnp.dot(mlp_in.reshape(SPANS * ROWS, D), w_up, preferred_element_type=jnp.float32)).astype(jnp.bfloat16)
    mlp_out = split_sum(hidden_units, w_down, N_TP).reshape(SPANS, ROWS, D)
    return (residual + mod_rows[:, 5] * mlp_out).astype(jnp.bfloat16)
```

```python
import math

import jax
import jax.numpy as jnp
from jax import lax
from jax.sharding import PartitionSpec as P

HEAD_DIM = 128


EPSILON = 1e-06
NEGATIVE = -1e30
WEIGHT_GATHER_BYTES = 24 * 2**20


def normalize(values):
    return values * lax.rsqrt(jnp.mean(values * values, axis=-1, keepdims=True) + EPSILON)


def select_row(source, target):
    matches = jnp.arange(source.shape[0], dtype=jnp.int32) == target
    return jnp.sum(jnp.where(matches.reshape((-1,) + (1,) * (source.ndim - 1)), source, 0), axis=0)


def attend(queries, cache_all, fresh_all, cache_seen, fresh_seen):
    row_count, head_count, head_size = queries.shape
    cache_keys = cache_all[:, :, 0].reshape(-1, head_count, head_size)
    cache_vals = cache_all[:, :, 1].reshape(-1, head_count, head_size)
    fresh_keys = fresh_all[:, :, 0].reshape(-1, head_count, head_size)
    fresh_vals = fresh_all[:, :, 1].reshape(-1, head_count, head_size)
    score_scale = 1.0 / math.sqrt(head_size)
    cache_scores = (
        jnp.einsum("qhd,khd->hqk", queries, cache_keys, preferred_element_type=jnp.float32)
        * score_scale
    )
    fresh_scores = (
        jnp.einsum("qhd,khd->hqk", queries, fresh_keys, preferred_element_type=jnp.float32)
        * score_scale
    )
    cache_scores = jnp.where(cache_seen[None, None, :], cache_scores, NEGATIVE)
    fresh_scores = jnp.where(fresh_seen[None, None, :], fresh_scores, NEGATIVE)
    scores = jnp.concatenate([cache_scores, fresh_scores], axis=2)
    row_max = jnp.max(scores, axis=2, keepdims=True)
    exp_terms = jnp.exp(scores - row_max)
    weights = (exp_terms / jnp.sum(exp_terms, axis=2, keepdims=True)).astype(jnp.bfloat16)
    split_at = cache_keys.shape[0]
    attended = jnp.einsum(
        "hqk,khd->qhd", weights[:, :, :split_at], cache_vals, preferred_element_type=jnp.float32
    )
    attended = attended + jnp.einsum(
        "hqk,khd->qhd", weights[:, :, split_at:], fresh_vals, preferred_element_type=jnp.float32
    )
    return attended.astype(jnp.bfloat16).reshape(row_count, head_count * head_size)


def local(
    hidden_in, levels, order, cache_mask, finished, cache_kv, modulation, w_qkv, w_out, w_up, w_down
):
    span_index = lax.axis_index("span")
    tp_rank = lax.axis_index("tp")
    span_count = lax.psum(1, "span")
    tp_count = lax.psum(1, "tp")
    model_width = modulation.shape[2]
    share_width = hidden_in.shape[2]
    local_count = hidden_in.shape[0]
    row_count = hidden_in.shape[1]
    token_count = local_count * row_count
    gathered = lax.all_gather(hidden_in, "tp", axis=2, tiled=True).astype(jnp.float32)
    gather_weights = tp_count * w_out.size * w_out.dtype.itemsize <= WEIGHT_GATHER_BYTES
    if gather_weights:
        column_part = model_width // span_count
        w_out_part = lax.dynamic_slice_in_dim(w_out, span_index * column_part, column_part, 1)
        w_out_full = lax.all_gather(
            lax.all_gather(w_out_part, "tp", axis=0, tiled=True), "span", axis=1, tiled=True
        )
    up_full, down_full = (
        lax.all_gather(w_up, "span", axis=1, tiled=True),
        lax.all_gather(w_down, "span", axis=0, tiled=True),
    )
    mod_table = modulation.reshape(modulation.shape[0], -1)
    picker = (jnp.arange(mod_table.shape[0], dtype=jnp.int32)[None, :] == levels[:, None]).astype(
        jnp.bfloat16
    )
    mod_rows = jnp.dot(picker, mod_table, preferred_element_type=jnp.float32).reshape(
        local_count, 6, model_width
    )
    attn_in = (normalize(gathered) * mod_rows[:, 1][:, None] + mod_rows[:, 0][:, None]).astype(
        jnp.bfloat16
    )
    per_device = w_qkv.shape[2]
    projected = jnp.dot(
        attn_in.reshape(token_count, model_width),
        w_qkv.reshape(model_width, -1),
        preferred_element_type=jnp.float32,
    )
    projected = projected.astype(jnp.bfloat16).reshape(local_count, row_count, 3, per_device)
    queries = projected[:, :, 0].reshape(local_count, row_count, -1, HEAD_DIM)
    fresh_kv = projected[:, :, 1:]
    cache_all, fresh_all = (
        lax.all_gather(cache_kv, "span", axis=0, tiled=True),
        lax.all_gather(fresh_kv, "span", axis=0, tiled=True),
    )
    positions = jnp.arange(cache_mask.shape[0], dtype=jnp.int32)
    my_spans = span_index * local_count + jnp.arange(local_count, dtype=jnp.int32)
    mask_rows = jax.vmap(lambda target: select_row(cache_mask, target))(my_spans)
    my_order = jax.vmap(lambda target: select_row(order, target))(my_spans)
    cache_seen = jnp.repeat(
        (mask_rows == 1) | (positions[None, :] == finished[0]), row_count, axis=1
    )
    fresh_seen = jnp.repeat(order[None, :] <= my_order[:, None], row_count, axis=1)
    attended = jax.vmap(
        lambda q_rows, c_seen, f_seen: attend(q_rows, cache_all, fresh_all, c_seen, f_seen)
    )(queries, cache_seen, fresh_seen)
    if gather_weights:
        attended_all = lax.all_gather(
            attended.reshape(token_count, per_device), "tp", axis=1, tiled=True
        )
        def add_group(group, running):
            term = jnp.dot(
                lax.dynamic_slice_in_dim(attended_all, group * per_device, per_device, 1),
                lax.dynamic_slice_in_dim(w_out_full, group * per_device, per_device, 0),
                preferred_element_type=jnp.float32,
            )
            return running + term.astype(jnp.bfloat16).astype(jnp.float32)

        attn_out = lax.fori_loop(
            0, tp_count, add_group, jnp.zeros((token_count, model_width), jnp.float32)
        )
        attn_out = attn_out.reshape(local_count, row_count, model_width)
        residual_full = gathered + mod_rows[:, 2][:, None] * attn_out
        mlp_in = (
            normalize(residual_full) * mod_rows[:, 4][:, None] + mod_rows[:, 3][:, None]
        ).astype(jnp.bfloat16)
    else:
        partial_value = jnp.dot(
            attended.reshape(token_count, -1), w_out, preferred_element_type=jnp.float32
        ).reshape(local_count, row_count, model_width)
        attn_part = lax.psum_scatter(
            partial_value.astype(jnp.bfloat16), "tp", scatter_dimension=2, tiled=True
        ).astype(jnp.float32)
        mod_share = lax.dynamic_slice_in_dim(mod_rows, tp_rank * share_width, share_width, 2)
        residual = hidden_in.astype(jnp.float32) + mod_share[:, 2][:, None] * attn_part
        squares = lax.psum(jnp.sum(residual * residual, axis=2), "tp")
        scaled = residual * lax.rsqrt(squares / model_width + EPSILON)[:, :, None]
        mlp_part = (scaled * mod_share[:, 4][:, None] + mod_share[:, 3][:, None]).astype(
            jnp.bfloat16
        )
        mlp_in = lax.all_gather(mlp_part, "tp", axis=2, tiled=True)
    pre_act = jnp.dot(mlp_in, up_full, preferred_element_type=jnp.float32)
    hidden_units = jax.nn.gelu(pre_act).astype(jnp.bfloat16)
    down_terms = jnp.dot(hidden_units, down_full, preferred_element_type=jnp.float32)
    mlp_out = lax.psum_scatter(
        down_terms.astype(jnp.bfloat16), "tp", scatter_dimension=2, tiled=True
    ).astype(jnp.float32)
    if gather_weights:
        residual = lax.dynamic_slice_in_dim(residual_full, tp_rank * share_width, share_width, 2)
        mod_share = lax.dynamic_slice_in_dim(mod_rows, tp_rank * share_width, share_width, 2)
    result = residual + mod_share[:, 5][:, None] * mlp_out
    return result.astype(jnp.bfloat16)


def solution(mesh):
    placed = (
        P(("rep", "span"), None, "tp"),
        P(("rep", "span")),
        P("rep"),
        P("rep", None),
        P("rep"),
        P(("rep", "span"), None, None, "tp"),
        P(),
        P(None, None, "tp"),
        P("tp", None),
        P(None, ("span", "tp")),
        P(("span", "tp"), None),
    )
    return jax.shard_map(
        local, mesh=mesh, in_specs=placed, out_specs=P(("rep", "span"), None, "tp"), check_vma=False
    )
```

```python
import functools
import math

import jax
import jax.numpy as jnp
from jax import lax
from jax.experimental import pallas as pl
from jax.experimental.pallas import tpu as pltpu
from jax.sharding import PartitionSpec as P

HEAD_DIM = 128


EPSILON = 1e-06
NEGATIVE = -1e30
WEIGHT_GATHER_BYTES = 24 * 2**20


def normalize(values):
    return values * lax.rsqrt(jnp.mean(values * values, axis=-1, keepdims=True) + EPSILON)


def snake_cycle(count):
    return list(range(0, count, 2)) + list(range(count - 1, 0, -2)) if count % 2 == 0 else list(range(count))


def ring_gather(block, axis_name, count):
    cycle = snake_cycle(count)
    ahead = [(cycle[p], cycle[(p + 1) % count]) for p in range(count)]
    behind = [(cycle[p], cycle[(p - 1) % count]) for p in range(count)]
    blocks = [block]
    forward = block
    for _ in range(count // 2):
        forward = lax.ppermute(forward, axis_name, ahead)
        blocks.append(forward)
    backward = block
    for _ in range((count - 1) // 2):
        backward = lax.ppermute(backward, axis_name, behind)
        blocks.append(backward)
    return blocks


def out_proj_kernel(group_count, tiles_per_half, span_ref, *refs):
    att_refs = refs[:group_count]
    mine_refs = refs[group_count:2 * group_count]
    other_refs = refs[2 * group_count:3 * group_count]
    out_ref = refs[3 * group_count]
    tile = pl.program_id(0)

    def accumulate(w_refs):
        total = None
        for group in range(group_count):
            term = jnp.dot(att_refs[group][...], w_refs[group][...], preferred_element_type=jnp.float32)
            term = term.astype(jnp.bfloat16).astype(jnp.float32)
            total = term if total is None else total + term
        out_ref[...] = total

    @pl.when(tile < tiles_per_half)
    def _():
        accumulate(mine_refs)

    @pl.when(tile >= tiles_per_half)
    def _():
        accumulate(other_refs)


def grouped_out_proj(span_index, att_blocks, mine_blocks, other_blocks, tile_width=512):
    group_count = len(att_blocks)
    token_count, head_width = att_blocks[0].shape
    half_width = mine_blocks[0].shape[1]
    tile_width = min(tile_width, half_width)
    tiles_per_half = half_width // tile_width
    att_spec = pl.BlockSpec((token_count, head_width), lambda n, s: (0, 0))
    mine_spec = pl.BlockSpec(
        (head_width, tile_width), lambda n, s: (0, jnp.minimum(n, tiles_per_half - 1))
    )
    other_spec = pl.BlockSpec(
        (head_width, tile_width), lambda n, s: (0, jnp.maximum(n - tiles_per_half, 0))
    )
    out_spec = pl.BlockSpec(
        (token_count, tile_width),
        lambda n, s: (0, ((n // tiles_per_half + s[0]) % 2) * tiles_per_half + n % tiles_per_half),
    )
    flops = 2 * token_count * head_width * group_count * half_width * 2
    moved = 2 * (group_count * token_count * head_width + 2 * group_count * head_width * half_width)
    return pl.pallas_call(
        functools.partial(out_proj_kernel, group_count, tiles_per_half),
        out_shape=jax.ShapeDtypeStruct((token_count, 2 * half_width), jnp.float32),
        grid_spec=pltpu.PrefetchScalarGridSpec(
            num_scalar_prefetch=1,
            grid=(2 * tiles_per_half,),
            in_specs=[att_spec] * group_count + [mine_spec] * group_count + [other_spec] * group_count,
            out_specs=out_spec,
        ),
        cost_estimate=pl.CostEstimate(
            flops=flops, bytes_accessed=moved + token_count * 2 * half_width * 4, transcendentals=0
        ),
    )(jnp.reshape(span_index, (1,)).astype(jnp.int32), *att_blocks, *mine_blocks, *other_blocks)


def select_row(source, target):
    matches = jnp.arange(source.shape[0], dtype=jnp.int32) == target
    return jnp.sum(jnp.where(matches.reshape((-1,) + (1,) * (source.ndim - 1)), source, 0), axis=0)


def attend(queries, cache_all, fresh_all, cache_seen, fresh_seen):
    row_count, head_count, head_size = queries.shape
    cache_keys = cache_all[:, :, 0].reshape(-1, head_count, head_size)
    cache_vals = cache_all[:, :, 1].reshape(-1, head_count, head_size)
    fresh_keys = fresh_all[:, :, 0].reshape(-1, head_count, head_size)
    fresh_vals = fresh_all[:, :, 1].reshape(-1, head_count, head_size)
    score_scale = 1.0 / math.sqrt(head_size)
    cache_scores = (
        jnp.einsum("qhd,khd->hqk", queries, cache_keys, preferred_element_type=jnp.float32)
        * score_scale
    )
    fresh_scores = (
        jnp.einsum("qhd,khd->hqk", queries, fresh_keys, preferred_element_type=jnp.float32)
        * score_scale
    )
    cache_scores = jnp.where(cache_seen[None, None, :], cache_scores, NEGATIVE)
    fresh_scores = jnp.where(fresh_seen[None, None, :], fresh_scores, NEGATIVE)
    scores = jnp.concatenate([cache_scores, fresh_scores], axis=2)
    row_max = jnp.max(scores, axis=2, keepdims=True)
    exp_terms = jnp.exp(scores - row_max)
    weights = (exp_terms / jnp.sum(exp_terms, axis=2, keepdims=True)).astype(jnp.bfloat16)
    split_at = cache_keys.shape[0]
    attended = jnp.einsum(
        "hqk,khd->qhd", weights[:, :, :split_at], cache_vals, preferred_element_type=jnp.float32
    )
    attended = attended + jnp.einsum(
        "hqk,khd->qhd", weights[:, :, split_at:], fresh_vals, preferred_element_type=jnp.float32
    )
    return attended.astype(jnp.bfloat16).reshape(row_count, head_count * head_size)


def local(
    hidden_in, levels, order, cache_mask, finished, cache_kv, modulation, w_qkv, w_out, w_up, w_down
):
    span_index = lax.axis_index("span")
    tp_rank = lax.axis_index("tp")
    span_count = lax.psum(1, "span")
    tp_count = lax.psum(1, "tp")
    model_width = modulation.shape[2]
    share_width = hidden_in.shape[2]
    local_count = hidden_in.shape[0]
    row_count = hidden_in.shape[1]
    token_count = local_count * row_count
    gathered = lax.all_gather(hidden_in, "tp", axis=2, tiled=True).astype(jnp.float32)
    gather_weights = (
        tp_count * w_out.size * w_out.dtype.itemsize <= WEIGHT_GATHER_BYTES and span_count == 2
    )
    if gather_weights:
        column_part = model_width // span_count
        w_out_part = lax.dynamic_slice_in_dim(w_out, span_index * column_part, column_part, 1)
        mine_blocks = ring_gather(w_out_part, "tp", tp_count)
        other_blocks = [lax.ppermute(b, "span", [(0, 1), (1, 0)]) for b in mine_blocks]
    up_full, down_full = (
        lax.all_gather(w_up, "span", axis=1, tiled=True),
        lax.all_gather(w_down, "span", axis=0, tiled=True),
    )
    mod_table = modulation.reshape(modulation.shape[0], -1)
    picker = (jnp.arange(mod_table.shape[0], dtype=jnp.int32)[None, :] == levels[:, None]).astype(
        jnp.bfloat16
    )
    mod_rows = jnp.dot(picker, mod_table, preferred_element_type=jnp.float32).reshape(
        local_count, 6, model_width
    )
    attn_in = (normalize(gathered) * mod_rows[:, 1][:, None] + mod_rows[:, 0][:, None]).astype(
        jnp.bfloat16
    )
    per_device = w_qkv.shape[2]
    projected = jnp.dot(
        attn_in.reshape(token_count, model_width),
        w_qkv.reshape(model_width, -1),
        preferred_element_type=jnp.float32,
    )
    projected = projected.astype(jnp.bfloat16).reshape(local_count, row_count, 3, per_device)
    queries = projected[:, :, 0].reshape(local_count, row_count, -1, HEAD_DIM)
    fresh_kv = projected[:, :, 1:]
    cache_all, fresh_all = (
        lax.all_gather(cache_kv, "span", axis=0, tiled=True),
        lax.all_gather(fresh_kv, "span", axis=0, tiled=True),
    )
    positions = jnp.arange(cache_mask.shape[0], dtype=jnp.int32)
    my_spans = span_index * local_count + jnp.arange(local_count, dtype=jnp.int32)
    mask_rows = jax.vmap(lambda target: select_row(cache_mask, target))(my_spans)
    my_order = jax.vmap(lambda target: select_row(order, target))(my_spans)
    cache_seen = jnp.repeat(
        (mask_rows == 1) | (positions[None, :] == finished[0]), row_count, axis=1
    )
    fresh_seen = jnp.repeat(order[None, :] <= my_order[:, None], row_count, axis=1)
    attended = jax.vmap(
        lambda q_rows, c_seen, f_seen: attend(q_rows, cache_all, fresh_all, c_seen, f_seen)
    )(queries, cache_seen, fresh_seen)
    if gather_weights:
        att_blocks = ring_gather(attended.reshape(token_count, per_device), "tp", tp_count)
        attn_out = grouped_out_proj(span_index, att_blocks, mine_blocks, other_blocks)
        attn_out = attn_out.reshape(local_count, row_count, model_width)
        residual_full = gathered + mod_rows[:, 2][:, None] * attn_out
        mlp_in = (
            normalize(residual_full) * mod_rows[:, 4][:, None] + mod_rows[:, 3][:, None]
        ).astype(jnp.bfloat16)
    else:
        partial_value = jnp.dot(
            attended.reshape(token_count, -1), w_out, preferred_element_type=jnp.float32
        ).reshape(local_count, row_count, model_width)
        attn_part = lax.psum_scatter(
            partial_value.astype(jnp.bfloat16), "tp", scatter_dimension=2, tiled=True
        ).astype(jnp.float32)
        mod_share = lax.dynamic_slice_in_dim(mod_rows, tp_rank * share_width, share_width, 2)
        residual = hidden_in.astype(jnp.float32) + mod_share[:, 2][:, None] * attn_part
        squares = lax.psum(jnp.sum(residual * residual, axis=2), "tp")
        scaled = residual * lax.rsqrt(squares / model_width + EPSILON)[:, :, None]
        mlp_part = (scaled * mod_share[:, 4][:, None] + mod_share[:, 3][:, None]).astype(
            jnp.bfloat16
        )
        mlp_in = lax.all_gather(mlp_part, "tp", axis=2, tiled=True)
    pre_act = jnp.dot(mlp_in, up_full, preferred_element_type=jnp.float32)
    hidden_units = jax.nn.gelu(pre_act).astype(jnp.bfloat16)
    down_terms = jnp.dot(hidden_units, down_full, preferred_element_type=jnp.float32)
    mlp_out = lax.psum_scatter(
        down_terms.astype(jnp.bfloat16), "tp", scatter_dimension=2, tiled=True
    ).astype(jnp.float32)
    if gather_weights:
        residual = lax.dynamic_slice_in_dim(residual_full, tp_rank * share_width, share_width, 2)
        mod_share = lax.dynamic_slice_in_dim(mod_rows, tp_rank * share_width, share_width, 2)
    result = residual + mod_share[:, 5][:, None] * mlp_out
    return result.astype(jnp.bfloat16)


def solution(mesh):
    placed = (
        P(("rep", "span"), None, "tp"),
        P(("rep", "span")),
        P("rep"),
        P("rep", None),
        P("rep"),
        P(("rep", "span"), None, None, "tp"),
        P(),
        P(None, None, "tp"),
        P("tp", None),
        P(None, ("span", "tp")),
        P(("span", "tp"), None),
    )
    return jax.shard_map(
        local, mesh=mesh, in_specs=placed, out_specs=P(("rep", "span"), None, "tp"), check_vma=False
    )
```

```python
import functools
import math

import jax
import jax.numpy as jnp
from jax import lax
from jax.experimental import pallas as pl
from jax.experimental.pallas import tpu as pltpu
from jax.sharding import PartitionSpec as P

HEAD_DIM = 128


EPSILON = 1e-06
NEGATIVE = -1e30
WEIGHT_GATHER_BYTES = 24 * 2**20


def normalize(values):
    return values * lax.rsqrt(jnp.mean(values * values, axis=-1, keepdims=True) + EPSILON)


def snake_cycle(count):
    return list(range(0, count, 2)) + list(range(count - 1, 0, -2)) if count % 2 == 0 else list(range(count))


def ring_gather(block, axis_name, count):
    cycle = snake_cycle(count)
    ahead = [(cycle[p], cycle[(p + 1) % count]) for p in range(count)]
    behind = [(cycle[p], cycle[(p - 1) % count]) for p in range(count)]
    blocks = [block]
    forward = block
    for _ in range(count // 2):
        forward = lax.ppermute(forward, axis_name, ahead)
        blocks.append(forward)
    backward = block
    for _ in range((count - 1) // 2):
        backward = lax.ppermute(backward, axis_name, behind)
        blocks.append(backward)
    return blocks


def out_proj_kernel(group_count, set_count, tiles_per_set, place_ref, *refs):
    att_refs = refs[:group_count]
    out_ref = refs[-1]
    tile = pl.program_id(0)

    def accumulate(w_refs):
        total = None
        for group in range(group_count):
            term = jnp.dot(att_refs[group][...], w_refs[group][...], preferred_element_type=jnp.float32)
            term = term.astype(jnp.bfloat16).astype(jnp.float32)
            total = term if total is None else total + term
        out_ref[...] = total

    for which in range(set_count):
        w_refs = refs[group_count * (which + 1):group_count * (which + 2)]

        @pl.when(tile // tiles_per_set == which)
        def _():
            accumulate(w_refs)


def grouped_out_proj(placement, att_blocks, weight_sets, tile_width=512):
    group_count = len(att_blocks)
    set_count = len(weight_sets)
    token_count, head_width = att_blocks[0].shape
    set_width = weight_sets[0][0].shape[1]
    tile_width = min(tile_width, set_width)
    tiles_per_set = set_width // tile_width
    att_spec = pl.BlockSpec((token_count, head_width), lambda n, p: (0, 0))

    def weight_spec(which):
        return pl.BlockSpec(
            (head_width, tile_width),
            lambda n, p: (0, jnp.clip(n - which * tiles_per_set, 0, tiles_per_set - 1)),
        )

    out_spec = pl.BlockSpec(
        (token_count, tile_width),
        lambda n, p: (0, p[n // tiles_per_set] * tiles_per_set + n % tiles_per_set),
    )
    in_specs = [att_spec] * group_count
    for which in range(set_count):
        in_specs += [weight_spec(which)] * group_count
    width = set_count * set_width
    flops = 2 * token_count * head_width * group_count * width
    moved = 2 * group_count * token_count * head_width + 2 * group_count * head_width * width
    return pl.pallas_call(
        functools.partial(out_proj_kernel, group_count, set_count, tiles_per_set),
        out_shape=jax.ShapeDtypeStruct((token_count, width), jnp.float32),
        grid_spec=pltpu.PrefetchScalarGridSpec(
            num_scalar_prefetch=1,
            grid=(set_count * tiles_per_set,),
            in_specs=in_specs,
            out_specs=out_spec,
        ),
        cost_estimate=pl.CostEstimate(
            flops=flops, bytes_accessed=moved + token_count * width * 4, transcendentals=0
        ),
    )(placement, *att_blocks, *[b for blocks in weight_sets for b in blocks])


def select_row(source, target):
    matches = jnp.arange(source.shape[0], dtype=jnp.int32) == target
    return jnp.sum(jnp.where(matches.reshape((-1,) + (1,) * (source.ndim - 1)), source, 0), axis=0)


def attend(queries, cache_all, fresh_all, cache_seen, fresh_seen):
    row_count, head_count, head_size = queries.shape
    cache_keys = cache_all[:, :, 0].reshape(-1, head_count, head_size)
    cache_vals = cache_all[:, :, 1].reshape(-1, head_count, head_size)
    fresh_keys = fresh_all[:, :, 0].reshape(-1, head_count, head_size)
    fresh_vals = fresh_all[:, :, 1].reshape(-1, head_count, head_size)
    score_scale = 1.0 / math.sqrt(head_size)
    cache_scores = (
        jnp.einsum("qhd,khd->hqk", queries, cache_keys, preferred_element_type=jnp.float32)
        * score_scale
    )
    fresh_scores = (
        jnp.einsum("qhd,khd->hqk", queries, fresh_keys, preferred_element_type=jnp.float32)
        * score_scale
    )
    cache_scores = jnp.where(cache_seen[None, None, :], cache_scores, NEGATIVE)
    fresh_scores = jnp.where(fresh_seen[None, None, :], fresh_scores, NEGATIVE)
    scores = jnp.concatenate([cache_scores, fresh_scores], axis=2)
    row_max = jnp.max(scores, axis=2, keepdims=True)
    exp_terms = jnp.exp(scores - row_max)
    weights = (exp_terms / jnp.sum(exp_terms, axis=2, keepdims=True)).astype(jnp.bfloat16)
    split_at = cache_keys.shape[0]
    attended = jnp.einsum(
        "hqk,khd->qhd", weights[:, :, :split_at], cache_vals, preferred_element_type=jnp.float32
    )
    attended = attended + jnp.einsum(
        "hqk,khd->qhd", weights[:, :, split_at:], fresh_vals, preferred_element_type=jnp.float32
    )
    return attended.astype(jnp.bfloat16).reshape(row_count, head_count * head_size)


def local(
    hidden_in, levels, order, cache_mask, finished, cache_kv, modulation, w_qkv, w_out, w_up, w_down
):
    span_index = lax.axis_index("span")
    tp_rank = lax.axis_index("tp")
    span_count = lax.psum(1, "span")
    rep_count = lax.psum(1, "rep")
    tp_count = lax.psum(1, "tp")
    model_width = modulation.shape[2]
    share_width = hidden_in.shape[2]
    local_count = hidden_in.shape[0]
    row_count = hidden_in.shape[1]
    token_count = local_count * row_count
    gathered = lax.all_gather(hidden_in, "tp", axis=2, tiled=True).astype(jnp.float32)
    gather_weights = (
        tp_count * w_out.size * w_out.dtype.itemsize <= WEIGHT_GATHER_BYTES and span_count == 2
        and rep_count == 2
    )
    if gather_weights:
        rep_index = lax.axis_index("rep")
        column_part = model_width // (rep_count * span_count)
        slot = rep_index * span_count + span_index
        w_out_part = lax.dynamic_slice_in_dim(w_out, slot * column_part, column_part, 1)
        mine_blocks = ring_gather(w_out_part, "tp", tp_count)
        swap = [(0, 1), (1, 0)]
        rep_blocks = [lax.ppermute(b, "rep", swap) for b in mine_blocks]
        weight_sets = [
            mine_blocks,
            rep_blocks,
            [lax.ppermute(b, "span", swap) for b in mine_blocks],
            [lax.ppermute(b, "span", swap) for b in rep_blocks],
        ]
        placement = jnp.stack(
            [
                ((rep_index + dr) % 2) * span_count + (span_index + ds) % 2
                for ds in (0, 1)
                for dr in (0, 1)
            ]
        ).astype(jnp.int32)
    up_full, down_full = (
        lax.all_gather(w_up, "span", axis=1, tiled=True),
        lax.all_gather(w_down, "span", axis=0, tiled=True),
    )
    mod_table = modulation.reshape(modulation.shape[0], -1)
    picker = (jnp.arange(mod_table.shape[0], dtype=jnp.int32)[None, :] == levels[:, None]).astype(
        jnp.bfloat16
    )
    mod_rows = jnp.dot(picker, mod_table, preferred_element_type=jnp.float32).reshape(
        local_count, 6, model_width
    )
    attn_in = (normalize(gathered) * mod_rows[:, 1][:, None] + mod_rows[:, 0][:, None]).astype(
        jnp.bfloat16
    )
    per_device = w_qkv.shape[2]
    projected = jnp.dot(
        attn_in.reshape(token_count, model_width),
        w_qkv.reshape(model_width, -1),
        preferred_element_type=jnp.float32,
    )
    projected = projected.astype(jnp.bfloat16).reshape(local_count, row_count, 3, per_device)
    queries = projected[:, :, 0].reshape(local_count, row_count, -1, HEAD_DIM)
    fresh_kv = projected[:, :, 1:]
    cache_all, fresh_all = (
        lax.all_gather(cache_kv, "span", axis=0, tiled=True),
        lax.all_gather(fresh_kv, "span", axis=0, tiled=True),
    )
    positions = jnp.arange(cache_mask.shape[0], dtype=jnp.int32)
    my_spans = span_index * local_count + jnp.arange(local_count, dtype=jnp.int32)
    mask_rows = jax.vmap(lambda target: select_row(cache_mask, target))(my_spans)
    my_order = jax.vmap(lambda target: select_row(order, target))(my_spans)
    cache_seen = jnp.repeat(
        (mask_rows == 1) | (positions[None, :] == finished[0]), row_count, axis=1
    )
    fresh_seen = jnp.repeat(order[None, :] <= my_order[:, None], row_count, axis=1)
    attended = jax.vmap(
        lambda q_rows, c_seen, f_seen: attend(q_rows, cache_all, fresh_all, c_seen, f_seen)
    )(queries, cache_seen, fresh_seen)
    if gather_weights:
        att_blocks = ring_gather(attended.reshape(token_count, per_device), "tp", tp_count)
        attn_out = grouped_out_proj(placement, att_blocks, weight_sets)
        attn_out = attn_out.reshape(local_count, row_count, model_width)
        residual_full = gathered + mod_rows[:, 2][:, None] * attn_out
        mlp_in = (
            normalize(residual_full) * mod_rows[:, 4][:, None] + mod_rows[:, 3][:, None]
        ).astype(jnp.bfloat16)
    else:
        partial_value = jnp.dot(
            attended.reshape(token_count, -1), w_out, preferred_element_type=jnp.float32
        ).reshape(local_count, row_count, model_width)
        attn_part = lax.psum_scatter(
            partial_value.astype(jnp.bfloat16), "tp", scatter_dimension=2, tiled=True
        ).astype(jnp.float32)
        mod_share = lax.dynamic_slice_in_dim(mod_rows, tp_rank * share_width, share_width, 2)
        residual = hidden_in.astype(jnp.float32) + mod_share[:, 2][:, None] * attn_part
        squares = lax.psum(jnp.sum(residual * residual, axis=2), "tp")
        scaled = residual * lax.rsqrt(squares / model_width + EPSILON)[:, :, None]
        mlp_part = (scaled * mod_share[:, 4][:, None] + mod_share[:, 3][:, None]).astype(
            jnp.bfloat16
        )
        mlp_in = lax.all_gather(mlp_part, "tp", axis=2, tiled=True)
    pre_act = jnp.dot(mlp_in, up_full, preferred_element_type=jnp.float32)
    hidden_units = jax.nn.gelu(pre_act).astype(jnp.bfloat16)
    down_terms = jnp.dot(hidden_units, down_full, preferred_element_type=jnp.float32)
    mlp_out = lax.psum_scatter(
        down_terms.astype(jnp.bfloat16), "tp", scatter_dimension=2, tiled=True
    ).astype(jnp.float32)
    if gather_weights:
        residual = lax.dynamic_slice_in_dim(residual_full, tp_rank * share_width, share_width, 2)
        mod_share = lax.dynamic_slice_in_dim(mod_rows, tp_rank * share_width, share_width, 2)
    result = residual + mod_share[:, 5][:, None] * mlp_out
    return result.astype(jnp.bfloat16)


def solution(mesh):
    placed = (
        P(("rep", "span"), None, "tp"),
        P(("rep", "span")),
        P("rep"),
        P("rep", None),
        P("rep"),
        P(("rep", "span"), None, None, "tp"),
        P(),
        P(None, None, "tp"),
        P("tp", None),
        P(None, ("span", "tp")),
        P(("span", "tp"), None),
    )
    return jax.shard_map(
        local, mesh=mesh, in_specs=placed, out_specs=P(("rep", "span"), None, "tp"), check_vma=False
    )
```

```python
import functools
import math

import jax
import jax.numpy as jnp
from jax import lax
from jax.experimental import pallas as pl
from jax.experimental.pallas import tpu as pltpu
from jax.sharding import PartitionSpec as P

HEAD_DIM = 128


EPSILON = 1e-06
NEGATIVE = -1e30
WEIGHT_GATHER_BYTES = 24 * 2**20


def normalize(values):
    return values * lax.rsqrt(jnp.mean(values * values, axis=-1, keepdims=True) + EPSILON)


def snake_cycle(count):
    return list(range(0, count, 2)) + list(range(count - 1, 0, -2)) if count % 2 == 0 else list(range(count))


def ring_gather(block, axis_name, count):
    cycle = snake_cycle(count)
    ahead = [(cycle[p], cycle[(p + 1) % count]) for p in range(count)]
    behind = [(cycle[p], cycle[(p - 1) % count]) for p in range(count)]
    blocks = [block]
    forward = block
    for _ in range(count // 2):
        forward = lax.ppermute(forward, axis_name, ahead)
        blocks.append(forward)
    backward = block
    for _ in range((count - 1) // 2):
        backward = lax.ppermute(backward, axis_name, behind)
        blocks.append(backward)
    return blocks


def direct_gather(block, axis_name, count):
    cycle = snake_cycle(count)
    shifts = list(range(1, count // 2 + 1)) + [-k for k in range(1, (count - 1) // 2 + 1)]
    blocks = [block]
    for shift in shifts:
        pairs = [(cycle[(p - shift) % count], cycle[p]) for p in range(count)]
        blocks.append(lax.ppermute(block, axis_name, pairs))
    return blocks


def out_proj_kernel(group_count, set_count, tiles_per_set, table_ref, *refs):
    att_refs = refs[:group_count]
    out_ref = refs[-1]
    tile = pl.program_id(0)

    def accumulate(w_ref):
        total = None
        for group in range(group_count):
            term = jnp.dot(att_refs[group][...], w_ref[group], preferred_element_type=jnp.float32)
            term = term.astype(jnp.bfloat16).astype(jnp.float32)
            total = term if total is None else total + term
        out_ref[...] = total

    for which in range(set_count):
        w_ref = refs[group_count + which]

        @pl.when(tile // tiles_per_set == which)
        def _():
            accumulate(w_ref)


def grouped_out_proj(table, att_all, weight_sets, tile_width=512):
    set_count = len(weight_sets)
    group_count, head_width, set_width = weight_sets[0].shape
    token_count = att_all.shape[0]
    tile_width = min(tile_width, set_width)
    tiles_per_set = set_width // tile_width

    def att_spec(group):
        return pl.BlockSpec((token_count, head_width), lambda n, p: (0, p[set_count + group]))

    def weight_spec(which):
        return pl.BlockSpec(
            (group_count, head_width, tile_width),
            lambda n, p: (0, 0, jnp.clip(n - which * tiles_per_set, 0, tiles_per_set - 1)),
        )

    out_spec = pl.BlockSpec(
        (token_count, tile_width),
        lambda n, p: (0, p[n // tiles_per_set] * tiles_per_set + n % tiles_per_set),
    )
    in_specs = [att_spec(g) for g in range(group_count)] + [weight_spec(k) for k in range(set_count)]
    width = set_count * set_width
    flops = 2 * token_count * head_width * group_count * width
    moved = 2 * token_count * head_width * group_count + 2 * group_count * head_width * width
    return pl.pallas_call(
        functools.partial(out_proj_kernel, group_count, set_count, tiles_per_set),
        out_shape=jax.ShapeDtypeStruct((token_count, width), jnp.float32),
        grid_spec=pltpu.PrefetchScalarGridSpec(
            num_scalar_prefetch=1,
            grid=(set_count * tiles_per_set,),
            in_specs=in_specs,
            out_specs=out_spec,
        ),
        cost_estimate=pl.CostEstimate(
            flops=flops, bytes_accessed=moved + token_count * width * 4, transcendentals=0
        ),
    )(table, *([att_all] * group_count), *weight_sets)


def select_row(source, target):
    matches = jnp.arange(source.shape[0], dtype=jnp.int32) == target
    return jnp.sum(jnp.where(matches.reshape((-1,) + (1,) * (source.ndim - 1)), source, 0), axis=0)


def attend(queries, cache_all, fresh_all, cache_seen, fresh_seen):
    row_count, head_count, head_size = queries.shape
    cache_keys = cache_all[:, :, 0].reshape(-1, head_count, head_size)
    cache_vals = cache_all[:, :, 1].reshape(-1, head_count, head_size)
    fresh_keys = fresh_all[:, :, 0].reshape(-1, head_count, head_size)
    fresh_vals = fresh_all[:, :, 1].reshape(-1, head_count, head_size)
    score_scale = 1.0 / math.sqrt(head_size)
    cache_scores = (
        jnp.einsum("qhd,khd->hqk", queries, cache_keys, preferred_element_type=jnp.float32)
        * score_scale
    )
    fresh_scores = (
        jnp.einsum("qhd,khd->hqk", queries, fresh_keys, preferred_element_type=jnp.float32)
        * score_scale
    )
    cache_scores = jnp.where(cache_seen[None, None, :], cache_scores, NEGATIVE)
    fresh_scores = jnp.where(fresh_seen[None, None, :], fresh_scores, NEGATIVE)
    scores = jnp.concatenate([cache_scores, fresh_scores], axis=2)
    row_max = jnp.max(scores, axis=2, keepdims=True)
    exp_terms = jnp.exp(scores - row_max)
    weights = (exp_terms / jnp.sum(exp_terms, axis=2, keepdims=True)).astype(jnp.bfloat16)
    split_at = cache_keys.shape[0]
    attended = jnp.einsum(
        "hqk,khd->qhd", weights[:, :, :split_at], cache_vals, preferred_element_type=jnp.float32
    )
    attended = attended + jnp.einsum(
        "hqk,khd->qhd", weights[:, :, split_at:], fresh_vals, preferred_element_type=jnp.float32
    )
    return attended.astype(jnp.bfloat16).reshape(row_count, head_count * head_size)


def local(
    hidden_in, levels, order, cache_mask, finished, cache_kv, modulation, w_qkv, w_out, w_up, w_down
):
    span_index = lax.axis_index("span")
    tp_rank = lax.axis_index("tp")
    span_count = lax.psum(1, "span")
    rep_count = lax.psum(1, "rep")
    tp_count = lax.psum(1, "tp")
    model_width = modulation.shape[2]
    share_width = hidden_in.shape[2]
    local_count = hidden_in.shape[0]
    row_count = hidden_in.shape[1]
    token_count = local_count * row_count
    gathered = lax.all_gather(hidden_in, "tp", axis=2, tiled=True).astype(jnp.float32)
    gather_weights = (
        tp_count * w_out.size * w_out.dtype.itemsize <= WEIGHT_GATHER_BYTES and span_count == 2
        and rep_count == 2
    )
    if gather_weights:
        rep_index = lax.axis_index("rep")
        column_part = model_width // (rep_count * span_count)
        slot = rep_index * span_count + span_index
        w_out_part = lax.dynamic_slice_in_dim(w_out, slot * column_part, column_part, 1)
        mine = jnp.stack(ring_gather(w_out_part, "tp", tp_count))
        swap = [(0, 1), (1, 0)]
        from_rep = lax.ppermute(mine, "rep", swap)
        from_span = lax.ppermute(jnp.stack([mine, from_rep]), "span", swap)
        weight_sets = [mine, from_rep, from_span[0], from_span[1]]
        slots = [
            ((rep_index + dr) % 2) * span_count + (span_index + ds) % 2
            for ds in (0, 1)
            for dr in (0, 1)
        ]
        cycle = snake_cycle(tp_count)
        position = [cycle.index(t) for t in range(tp_count)]
        steps = list(range(tp_count // 2 + 1)) + [-k for k in range(1, (tp_count - 1) // 2 + 1)]
        owners = jnp.array(
            [[cycle[(position[t] - k) % tp_count] for k in steps] for t in range(tp_count)],
            jnp.int32,
        )[tp_rank]
        table = jnp.concatenate([jnp.stack(slots).astype(jnp.int32), owners])
    up_full, down_full = (
        lax.all_gather(w_up, "span", axis=1, tiled=True),
        lax.all_gather(w_down, "span", axis=0, tiled=True),
    )
    mod_table = modulation.reshape(modulation.shape[0], -1)
    picker = (jnp.arange(mod_table.shape[0], dtype=jnp.int32)[None, :] == levels[:, None]).astype(
        jnp.bfloat16
    )
    mod_rows = jnp.dot(picker, mod_table, preferred_element_type=jnp.float32).reshape(
        local_count, 6, model_width
    )
    attn_in = (normalize(gathered) * mod_rows[:, 1][:, None] + mod_rows[:, 0][:, None]).astype(
        jnp.bfloat16
    )
    per_device = w_qkv.shape[2]
    projected = jnp.dot(
        attn_in.reshape(token_count, model_width),
        w_qkv.reshape(model_width, -1),
        preferred_element_type=jnp.float32,
    )
    projected = projected.astype(jnp.bfloat16).reshape(local_count, row_count, 3, per_device)
    queries = projected[:, :, 0].reshape(local_count, row_count, -1, HEAD_DIM)
    fresh_kv = projected[:, :, 1:]
    cache_all, fresh_all = (
        lax.all_gather(cache_kv, "span", axis=0, tiled=True),
        lax.all_gather(fresh_kv, "span", axis=0, tiled=True),
    )
    positions = jnp.arange(cache_mask.shape[0], dtype=jnp.int32)
    my_spans = span_index * local_count + jnp.arange(local_count, dtype=jnp.int32)
    mask_rows = jax.vmap(lambda target: select_row(cache_mask, target))(my_spans)
    my_order = jax.vmap(lambda target: select_row(order, target))(my_spans)
    cache_seen = jnp.repeat(
        (mask_rows == 1) | (positions[None, :] == finished[0]), row_count, axis=1
    )
    fresh_seen = jnp.repeat(order[None, :] <= my_order[:, None], row_count, axis=1)
    attended = jax.vmap(
        lambda q_rows, c_seen, f_seen: attend(q_rows, cache_all, fresh_all, c_seen, f_seen)
    )(queries, cache_seen, fresh_seen)
    if gather_weights:
        att_all = lax.all_gather(attended.reshape(token_count, per_device), "tp", axis=1, tiled=True)
        attn_out = grouped_out_proj(table, att_all, weight_sets)
        attn_out = attn_out.reshape(local_count, row_count, model_width)
        residual_full = gathered + mod_rows[:, 2][:, None] * attn_out
        mlp_in = (
            normalize(residual_full) * mod_rows[:, 4][:, None] + mod_rows[:, 3][:, None]
        ).astype(jnp.bfloat16)
    else:
        partial_value = jnp.dot(
            attended.reshape(token_count, -1), w_out, preferred_element_type=jnp.float32
        ).reshape(local_count, row_count, model_width)
        attn_part = lax.psum_scatter(
            partial_value.astype(jnp.bfloat16), "tp", scatter_dimension=2, tiled=True
        ).astype(jnp.float32)
        mod_share = lax.dynamic_slice_in_dim(mod_rows, tp_rank * share_width, share_width, 2)
        residual = hidden_in.astype(jnp.float32) + mod_share[:, 2][:, None] * attn_part
        squares = lax.psum(jnp.sum(residual * residual, axis=2), "tp")
        scaled = residual * lax.rsqrt(squares / model_width + EPSILON)[:, :, None]
        mlp_part = (scaled * mod_share[:, 4][:, None] + mod_share[:, 3][:, None]).astype(
            jnp.bfloat16
        )
        mlp_in = lax.all_gather(mlp_part, "tp", axis=2, tiled=True)
    pre_act = jnp.dot(mlp_in, up_full, preferred_element_type=jnp.float32)
    hidden_units = jax.nn.gelu(pre_act).astype(jnp.bfloat16)
    down_terms = jnp.dot(hidden_units, down_full, preferred_element_type=jnp.float32)
    mlp_out = lax.psum_scatter(
        down_terms.astype(jnp.bfloat16), "tp", scatter_dimension=2, tiled=True
    ).astype(jnp.float32)
    if gather_weights:
        residual = lax.dynamic_slice_in_dim(residual_full, tp_rank * share_width, share_width, 2)
        mod_share = lax.dynamic_slice_in_dim(mod_rows, tp_rank * share_width, share_width, 2)
    result = residual + mod_share[:, 5][:, None] * mlp_out
    return result.astype(jnp.bfloat16)


def solution(mesh):
    placed = (
        P(("rep", "span"), None, "tp"),
        P(("rep", "span")),
        P("rep"),
        P("rep", None),
        P("rep"),
        P(("rep", "span"), None, None, "tp"),
        P(),
        P(None, None, "tp"),
        P("tp", None),
        P(None, ("span", "tp")),
        P(("span", "tp"), None),
    )
    return jax.shard_map(
        local, mesh=mesh, in_specs=placed, out_specs=P(("rep", "span"), None, "tp"), check_vma=False
    )
```

```python
import functools
import math

import jax
import jax.numpy as jnp
from jax import lax
from jax.experimental import pallas as pl
from jax.experimental.pallas import tpu as pltpu
from jax.sharding import PartitionSpec as P

HEAD_DIM = 128


EPSILON = 1e-06
NEGATIVE = -1e30
WEIGHT_GATHER_BYTES = 24 * 2**20


def normalize(values):
    return values * lax.rsqrt(jnp.mean(values * values, axis=-1, keepdims=True) + EPSILON)


def snake_cycle(count):
    return list(range(0, count, 2)) + list(range(count - 1, 0, -2)) if count % 2 == 0 else list(range(count))


def ring_gather(block, axis_name, count):
    cycle = snake_cycle(count)
    ahead = [(cycle[p], cycle[(p + 1) % count]) for p in range(count)]
    behind = [(cycle[p], cycle[(p - 1) % count]) for p in range(count)]
    blocks = [block]
    forward = block
    for _ in range(count // 2):
        forward = lax.ppermute(forward, axis_name, ahead)
        blocks.append(forward)
    backward = block
    for _ in range((count - 1) // 2):
        backward = lax.ppermute(backward, axis_name, behind)
        blocks.append(backward)
    return blocks


def out_proj_kernel(group_count, set_count, tiles_per_set, table_ref, *refs):
    att_refs = refs[:group_count]
    out_ref = refs[-1]
    tile = pl.program_id(0)

    def accumulate(w_refs):
        total = None
        for group in range(group_count):
            term = jnp.dot(att_refs[group][...], w_refs[group][...], preferred_element_type=jnp.float32)
            term = term.astype(jnp.bfloat16).astype(jnp.float32)
            total = term if total is None else total + term
        out_ref[...] = total

    for which in range(set_count):
        w_refs = refs[group_count * (which + 1):group_count * (which + 2)]

        @pl.when(tile // tiles_per_set == which)
        def _():
            accumulate(w_refs)


def grouped_out_proj(table, att_all, weight_sets, tile_width=512):
    set_count = len(weight_sets)
    group_count = len(weight_sets[0])
    head_width, set_width = weight_sets[0][0].shape
    token_count = att_all.shape[0]
    tile_width = min(tile_width, set_width)
    tiles_per_set = set_width // tile_width

    def att_spec(group):
        return pl.BlockSpec((token_count, head_width), lambda n, p: (0, p[set_count + group]))

    def weight_spec(which):
        return pl.BlockSpec(
            (head_width, tile_width),
            lambda n, p: (0, jnp.clip(n - which * tiles_per_set, 0, tiles_per_set - 1)),
        )

    out_spec = pl.BlockSpec(
        (token_count, tile_width),
        lambda n, p: (0, p[n // tiles_per_set] * tiles_per_set + n % tiles_per_set),
    )
    in_specs = [att_spec(g) for g in range(group_count)]
    for which in range(set_count):
        in_specs += [weight_spec(which)] * group_count
    width = set_count * set_width
    flops = 2 * token_count * head_width * group_count * width
    moved = 2 * token_count * head_width * group_count + 2 * group_count * head_width * width
    return pl.pallas_call(
        functools.partial(out_proj_kernel, group_count, set_count, tiles_per_set),
        out_shape=jax.ShapeDtypeStruct((token_count, width), jnp.float32),
        grid_spec=pltpu.PrefetchScalarGridSpec(
            num_scalar_prefetch=1,
            grid=(set_count * tiles_per_set,),
            in_specs=in_specs,
            out_specs=out_spec,
        ),
        cost_estimate=pl.CostEstimate(
            flops=flops, bytes_accessed=moved + token_count * width * 4, transcendentals=0
        ),
    )(table, *([att_all] * group_count), *[b for blocks in weight_sets for b in blocks])


def select_row(source, target):
    matches = jnp.arange(source.shape[0], dtype=jnp.int32) == target
    return jnp.sum(jnp.where(matches.reshape((-1,) + (1,) * (source.ndim - 1)), source, 0), axis=0)


def attend(queries, cache_all, fresh_all, cache_seen, fresh_seen):
    row_count, head_count, head_size = queries.shape
    cache_keys = cache_all[:, :, 0].reshape(-1, head_count, head_size)
    cache_vals = cache_all[:, :, 1].reshape(-1, head_count, head_size)
    fresh_keys = fresh_all[:, :, 0].reshape(-1, head_count, head_size)
    fresh_vals = fresh_all[:, :, 1].reshape(-1, head_count, head_size)
    score_scale = 1.0 / math.sqrt(head_size)
    cache_scores = (
        jnp.einsum("qhd,khd->hqk", queries, cache_keys, preferred_element_type=jnp.float32)
        * score_scale
    )
    fresh_scores = (
        jnp.einsum("qhd,khd->hqk", queries, fresh_keys, preferred_element_type=jnp.float32)
        * score_scale
    )
    cache_scores = jnp.where(cache_seen[None, None, :], cache_scores, NEGATIVE)
    fresh_scores = jnp.where(fresh_seen[None, None, :], fresh_scores, NEGATIVE)
    scores = jnp.concatenate([cache_scores, fresh_scores], axis=2)
    row_max = jnp.max(scores, axis=2, keepdims=True)
    exp_terms = jnp.exp(scores - row_max)
    weights = (exp_terms / jnp.sum(exp_terms, axis=2, keepdims=True)).astype(jnp.bfloat16)
    split_at = cache_keys.shape[0]
    attended = jnp.einsum(
        "hqk,khd->qhd", weights[:, :, :split_at], cache_vals, preferred_element_type=jnp.float32
    )
    attended = attended + jnp.einsum(
        "hqk,khd->qhd", weights[:, :, split_at:], fresh_vals, preferred_element_type=jnp.float32
    )
    return attended.astype(jnp.bfloat16).reshape(row_count, head_count * head_size)


def local(
    hidden_in, levels, order, cache_mask, finished, cache_kv, modulation, w_qkv, w_out, w_up, w_down
):
    span_index = lax.axis_index("span")
    tp_rank = lax.axis_index("tp")
    span_count = lax.psum(1, "span")
    rep_count = lax.psum(1, "rep")
    tp_count = lax.psum(1, "tp")
    model_width = modulation.shape[2]
    share_width = hidden_in.shape[2]
    local_count = hidden_in.shape[0]
    row_count = hidden_in.shape[1]
    token_count = local_count * row_count
    gathered = lax.all_gather(hidden_in, "tp", axis=2, tiled=True).astype(jnp.float32)
    gather_weights = (
        tp_count * w_out.size * w_out.dtype.itemsize <= WEIGHT_GATHER_BYTES and span_count == 2
        and rep_count == 2
    )
    if gather_weights:
        rep_index = lax.axis_index("rep")
        column_part = model_width // (rep_count * span_count)
        slot = rep_index * span_count + span_index
        w_out_part = lax.dynamic_slice_in_dim(w_out, slot * column_part, column_part, 1)
        mine_blocks = ring_gather(w_out_part, "tp", tp_count)
        swap = [(0, 1), (1, 0)]
        rep_blocks = [lax.ppermute(b, "rep", swap) for b in mine_blocks]
        weight_sets = [
            mine_blocks,
            rep_blocks,
            [lax.ppermute(b, "span", swap) for b in mine_blocks],
            [lax.ppermute(b, "span", swap) for b in rep_blocks],
        ]
        slots = [
            ((rep_index + dr) % 2) * span_count + (span_index + ds) % 2
            for ds in (0, 1)
            for dr in (0, 1)
        ]
        cycle = snake_cycle(tp_count)
        position = [cycle.index(t) for t in range(tp_count)]
        steps = list(range(tp_count // 2 + 1)) + [-k for k in range(1, (tp_count - 1) // 2 + 1)]
        owners = jnp.array(
            [[cycle[(position[t] - k) % tp_count] for k in steps] for t in range(tp_count)],
            jnp.int32,
        )[tp_rank]
        table = jnp.concatenate([jnp.stack(slots).astype(jnp.int32), owners])
    up_full, down_full = (
        lax.all_gather(w_up, "span", axis=1, tiled=True),
        lax.all_gather(w_down, "span", axis=0, tiled=True),
    )
    mod_table = modulation.reshape(modulation.shape[0], -1)
    picker = (jnp.arange(mod_table.shape[0], dtype=jnp.int32)[None, :] == levels[:, None]).astype(
        jnp.bfloat16
    )
    mod_rows = jnp.dot(picker, mod_table, preferred_element_type=jnp.float32).reshape(
        local_count, 6, model_width
    )
    attn_in = (normalize(gathered) * mod_rows[:, 1][:, None] + mod_rows[:, 0][:, None]).astype(
        jnp.bfloat16
    )
    per_device = w_qkv.shape[2]
    projected = jnp.dot(
        attn_in.reshape(token_count, model_width),
        w_qkv.reshape(model_width, -1),
        preferred_element_type=jnp.float32,
    )
    projected = projected.astype(jnp.bfloat16).reshape(local_count, row_count, 3, per_device)
    queries = projected[:, :, 0].reshape(local_count, row_count, -1, HEAD_DIM)
    fresh_kv = projected[:, :, 1:]
    cache_all, fresh_all = (
        lax.all_gather(cache_kv, "span", axis=0, tiled=True),
        lax.all_gather(fresh_kv, "span", axis=0, tiled=True),
    )
    positions = jnp.arange(cache_mask.shape[0], dtype=jnp.int32)
    my_spans = span_index * local_count + jnp.arange(local_count, dtype=jnp.int32)
    mask_rows = jax.vmap(lambda target: select_row(cache_mask, target))(my_spans)
    my_order = jax.vmap(lambda target: select_row(order, target))(my_spans)
    cache_seen = jnp.repeat(
        (mask_rows == 1) | (positions[None, :] == finished[0]), row_count, axis=1
    )
    fresh_seen = jnp.repeat(order[None, :] <= my_order[:, None], row_count, axis=1)
    attended = jax.vmap(
        lambda q_rows, c_seen, f_seen: attend(q_rows, cache_all, fresh_all, c_seen, f_seen)
    )(queries, cache_seen, fresh_seen)
    if gather_weights:
        att_all = lax.all_gather(attended.reshape(token_count, per_device), "tp", axis=1, tiled=True)
        attn_out = grouped_out_proj(table, att_all, weight_sets)
        attn_out = attn_out.reshape(local_count, row_count, model_width)
        residual_full = gathered + mod_rows[:, 2][:, None] * attn_out
        mlp_in = (
            normalize(residual_full) * mod_rows[:, 4][:, None] + mod_rows[:, 3][:, None]
        ).astype(jnp.bfloat16)
    else:
        partial_value = jnp.dot(
            attended.reshape(token_count, -1), w_out, preferred_element_type=jnp.float32
        ).reshape(local_count, row_count, model_width)
        attn_part = lax.psum_scatter(
            partial_value.astype(jnp.bfloat16), "tp", scatter_dimension=2, tiled=True
        ).astype(jnp.float32)
        mod_share = lax.dynamic_slice_in_dim(mod_rows, tp_rank * share_width, share_width, 2)
        residual = hidden_in.astype(jnp.float32) + mod_share[:, 2][:, None] * attn_part
        squares = lax.psum(jnp.sum(residual * residual, axis=2), "tp")
        scaled = residual * lax.rsqrt(squares / model_width + EPSILON)[:, :, None]
        mlp_part = (scaled * mod_share[:, 4][:, None] + mod_share[:, 3][:, None]).astype(
            jnp.bfloat16
        )
        mlp_in = lax.all_gather(mlp_part, "tp", axis=2, tiled=True)
    pre_act = jnp.dot(mlp_in, up_full, preferred_element_type=jnp.float32)
    hidden_units = jax.nn.gelu(pre_act).astype(jnp.bfloat16)
    down_terms = jnp.dot(hidden_units, down_full, preferred_element_type=jnp.float32)
    mlp_out = lax.psum_scatter(
        down_terms.astype(jnp.bfloat16), "tp", scatter_dimension=2, tiled=True
    ).astype(jnp.float32)
    if gather_weights:
        residual = lax.dynamic_slice_in_dim(residual_full, tp_rank * share_width, share_width, 2)
        mod_share = lax.dynamic_slice_in_dim(mod_rows, tp_rank * share_width, share_width, 2)
    result = residual + mod_share[:, 5][:, None] * mlp_out
    return result.astype(jnp.bfloat16)


def solution(mesh):
    placed = (
        P(("rep", "span"), None, "tp"),
        P(("rep", "span")),
        P("rep"),
        P("rep", None),
        P("rep"),
        P(("rep", "span"), None, None, "tp"),
        P(),
        P(None, None, "tp"),
        P("tp", None),
        P(None, ("span", "tp")),
        P(("span", "tp"), None),
    )
    return jax.shard_map(
        local, mesh=mesh, in_specs=placed, out_specs=P(("rep", "span"), None, "tp"), check_vma=False
    )
```

```python
import functools
import math

import jax
import jax.numpy as jnp
from jax import lax
from jax.experimental import pallas as pl
from jax.experimental.pallas import tpu as pltpu
from jax.sharding import PartitionSpec as P

HEAD_DIM = 128


EPSILON = 1e-06
NEGATIVE = -1e30
WEIGHT_GATHER_BYTES = 24 * 2**20


def normalize(values):
    return values * lax.rsqrt(jnp.mean(values * values, axis=-1, keepdims=True) + EPSILON)


def snake_cycle(count):
    return list(range(0, count, 2)) + list(range(count - 1, 0, -2)) if count % 2 == 0 else list(range(count))


def ring_gather(block, axis_name, count):
    cycle = snake_cycle(count)
    ahead = [(cycle[p], cycle[(p + 1) % count]) for p in range(count)]
    behind = [(cycle[p], cycle[(p - 1) % count]) for p in range(count)]
    blocks = [block]
    forward = block
    for _ in range(count // 2):
        forward = lax.ppermute(forward, axis_name, ahead)
        blocks.append(forward)
    backward = block
    for _ in range((count - 1) // 2):
        backward = lax.ppermute(backward, axis_name, behind)
        blocks.append(backward)
    return blocks


def ring_reduce_scatter(terms, axis_name, count):
    token_count, width = terms.shape
    block = width // count
    half = block // 2
    cycle = snake_cycle(count)
    position = jnp.array([cycle.index(t) for t in range(count)], jnp.int32)[lax.axis_index(axis_name)]
    owners = jnp.array(cycle, jnp.int32)
    rounded = terms.astype(jnp.bfloat16)

    def own_part(slot, side):
        start = owners[slot % count] * block + side * half
        return lax.dynamic_slice_in_dim(rounded, start, half, 1).astype(jnp.float32)

    ahead = [(cycle[p], cycle[(p + 1) % count]) for p in range(count)]
    behind = [(cycle[p], cycle[(p - 1) % count]) for p in range(count)]
    forward = own_part(position - 1 + count, 0)
    backward = own_part(position + 1, 1)
    for step in range(count - 1):
        forward = lax.ppermute(forward.astype(jnp.bfloat16), axis_name, ahead).astype(jnp.float32)
        forward = forward + own_part(position - 2 - step + 2 * count, 0)
        backward = lax.ppermute(backward.astype(jnp.bfloat16), axis_name, behind).astype(jnp.float32)
        backward = backward + own_part(position + 2 + step, 1)
    return jnp.concatenate([forward, backward], axis=1)


def out_proj_kernel(group_count, tiles_per_half, span_ref, *refs):
    att_refs = refs[:group_count]
    mine_refs = refs[group_count:2 * group_count]
    other_refs = refs[2 * group_count:3 * group_count]
    out_ref = refs[3 * group_count]
    tile = pl.program_id(0)

    def accumulate(w_refs):
        total = None
        for group in range(group_count):
            term = jnp.dot(att_refs[group][...], w_refs[group][...], preferred_element_type=jnp.float32)
            term = term.astype(jnp.bfloat16).astype(jnp.float32)
            total = term if total is None else total + term
        out_ref[...] = total

    @pl.when(tile < tiles_per_half)
    def _():
        accumulate(mine_refs)

    @pl.when(tile >= tiles_per_half)
    def _():
        accumulate(other_refs)


def grouped_out_proj(span_index, att_blocks, mine_blocks, other_blocks, tile_width=512):
    group_count = len(att_blocks)
    token_count, head_width = att_blocks[0].shape
    half_width = mine_blocks[0].shape[1]
    tile_width = min(tile_width, half_width)
    tiles_per_half = half_width // tile_width
    att_spec = pl.BlockSpec((token_count, head_width), lambda n, s: (0, 0))
    mine_spec = pl.BlockSpec(
        (head_width, tile_width), lambda n, s: (0, jnp.minimum(n, tiles_per_half - 1))
    )
    other_spec = pl.BlockSpec(
        (head_width, tile_width), lambda n, s: (0, jnp.maximum(n - tiles_per_half, 0))
    )
    out_spec = pl.BlockSpec(
        (token_count, tile_width),
        lambda n, s: (0, ((n // tiles_per_half + s[0]) % 2) * tiles_per_half + n % tiles_per_half),
    )
    flops = 2 * token_count * head_width * group_count * half_width * 2
    moved = 2 * (group_count * token_count * head_width + 2 * group_count * head_width * half_width)
    return pl.pallas_call(
        functools.partial(out_proj_kernel, group_count, tiles_per_half),
        out_shape=jax.ShapeDtypeStruct((token_count, 2 * half_width), jnp.float32),
        grid_spec=pltpu.PrefetchScalarGridSpec(
            num_scalar_prefetch=1,
            grid=(2 * tiles_per_half,),
            in_specs=[att_spec] * group_count + [mine_spec] * group_count + [other_spec] * group_count,
            out_specs=out_spec,
        ),
        cost_estimate=pl.CostEstimate(
            flops=flops, bytes_accessed=moved + token_count * 2 * half_width * 4, transcendentals=0
        ),
    )(jnp.reshape(span_index, (1,)).astype(jnp.int32), *att_blocks, *mine_blocks, *other_blocks)


def select_row(source, target):
    matches = jnp.arange(source.shape[0], dtype=jnp.int32) == target
    return jnp.sum(jnp.where(matches.reshape((-1,) + (1,) * (source.ndim - 1)), source, 0), axis=0)


def attend(queries, cache_all, fresh_all, cache_seen, fresh_seen):
    row_count, head_count, head_size = queries.shape
    cache_keys = cache_all[:, :, 0].reshape(-1, head_count, head_size)
    cache_vals = cache_all[:, :, 1].reshape(-1, head_count, head_size)
    fresh_keys = fresh_all[:, :, 0].reshape(-1, head_count, head_size)
    fresh_vals = fresh_all[:, :, 1].reshape(-1, head_count, head_size)
    score_scale = 1.0 / math.sqrt(head_size)
    cache_scores = (
        jnp.einsum("qhd,khd->hqk", queries, cache_keys, preferred_element_type=jnp.float32)
        * score_scale
    )
    fresh_scores = (
        jnp.einsum("qhd,khd->hqk", queries, fresh_keys, preferred_element_type=jnp.float32)
        * score_scale
    )
    cache_scores = jnp.where(cache_seen[None, None, :], cache_scores, NEGATIVE)
    fresh_scores = jnp.where(fresh_seen[None, None, :], fresh_scores, NEGATIVE)
    scores = jnp.concatenate([cache_scores, fresh_scores], axis=2)
    row_max = jnp.max(scores, axis=2, keepdims=True)
    exp_terms = jnp.exp(scores - row_max)
    weights = (exp_terms / jnp.sum(exp_terms, axis=2, keepdims=True)).astype(jnp.bfloat16)
    split_at = cache_keys.shape[0]
    attended = jnp.einsum(
        "hqk,khd->qhd", weights[:, :, :split_at], cache_vals, preferred_element_type=jnp.float32
    )
    attended = attended + jnp.einsum(
        "hqk,khd->qhd", weights[:, :, split_at:], fresh_vals, preferred_element_type=jnp.float32
    )
    return attended.astype(jnp.bfloat16).reshape(row_count, head_count * head_size)


def local(
    hidden_in, levels, order, cache_mask, finished, cache_kv, modulation, w_qkv, w_out, w_up, w_down
):
    span_index = lax.axis_index("span")
    tp_rank = lax.axis_index("tp")
    span_count = lax.psum(1, "span")
    tp_count = lax.psum(1, "tp")
    model_width = modulation.shape[2]
    share_width = hidden_in.shape[2]
    local_count = hidden_in.shape[0]
    row_count = hidden_in.shape[1]
    token_count = local_count * row_count
    gathered = lax.all_gather(hidden_in, "tp", axis=2, tiled=True).astype(jnp.float32)
    gather_weights = (
        tp_count * w_out.size * w_out.dtype.itemsize <= WEIGHT_GATHER_BYTES and span_count == 2
    )
    if gather_weights:
        column_part = model_width // span_count
        w_out_part = lax.dynamic_slice_in_dim(w_out, span_index * column_part, column_part, 1)
        mine_blocks = ring_gather(w_out_part, "tp", tp_count)
        other_blocks = [lax.ppermute(b, "span", [(0, 1), (1, 0)]) for b in mine_blocks]
    up_full, down_full = (
        lax.all_gather(w_up, "span", axis=1, tiled=True),
        lax.all_gather(w_down, "span", axis=0, tiled=True),
    )
    mod_table = modulation.reshape(modulation.shape[0], -1)
    picker = (jnp.arange(mod_table.shape[0], dtype=jnp.int32)[None, :] == levels[:, None]).astype(
        jnp.bfloat16
    )
    mod_rows = jnp.dot(picker, mod_table, preferred_element_type=jnp.float32).reshape(
        local_count, 6, model_width
    )
    attn_in = (normalize(gathered) * mod_rows[:, 1][:, None] + mod_rows[:, 0][:, None]).astype(
        jnp.bfloat16
    )
    per_device = w_qkv.shape[2]
    projected = jnp.dot(
        attn_in.reshape(token_count, model_width),
        w_qkv.reshape(model_width, -1),
        preferred_element_type=jnp.float32,
    )
    projected = projected.astype(jnp.bfloat16).reshape(local_count, row_count, 3, per_device)
    queries = projected[:, :, 0].reshape(local_count, row_count, -1, HEAD_DIM)
    fresh_kv = projected[:, :, 1:]
    cache_all, fresh_all = (
        lax.all_gather(cache_kv, "span", axis=0, tiled=True),
        lax.all_gather(fresh_kv, "span", axis=0, tiled=True),
    )
    positions = jnp.arange(cache_mask.shape[0], dtype=jnp.int32)
    my_spans = span_index * local_count + jnp.arange(local_count, dtype=jnp.int32)
    mask_rows = jax.vmap(lambda target: select_row(cache_mask, target))(my_spans)
    my_order = jax.vmap(lambda target: select_row(order, target))(my_spans)
    cache_seen = jnp.repeat(
        (mask_rows == 1) | (positions[None, :] == finished[0]), row_count, axis=1
    )
    fresh_seen = jnp.repeat(order[None, :] <= my_order[:, None], row_count, axis=1)
    attended = jax.vmap(
        lambda q_rows, c_seen, f_seen: attend(q_rows, cache_all, fresh_all, c_seen, f_seen)
    )(queries, cache_seen, fresh_seen)
    if gather_weights:
        att_blocks = ring_gather(attended.reshape(token_count, per_device), "tp", tp_count)
        attn_out = grouped_out_proj(span_index, att_blocks, mine_blocks, other_blocks)
        attn_out = attn_out.reshape(local_count, row_count, model_width)
        residual_full = gathered + mod_rows[:, 2][:, None] * attn_out
        mlp_in = (
            normalize(residual_full) * mod_rows[:, 4][:, None] + mod_rows[:, 3][:, None]
        ).astype(jnp.bfloat16)
    else:
        partial_value = jnp.dot(
            attended.reshape(token_count, -1), w_out, preferred_element_type=jnp.float32
        ).reshape(local_count, row_count, model_width)
        attn_part = lax.psum_scatter(
            partial_value.astype(jnp.bfloat16), "tp", scatter_dimension=2, tiled=True
        ).astype(jnp.float32)
        mod_share = lax.dynamic_slice_in_dim(mod_rows, tp_rank * share_width, share_width, 2)
        residual = hidden_in.astype(jnp.float32) + mod_share[:, 2][:, None] * attn_part
        squares = lax.psum(jnp.sum(residual * residual, axis=2), "tp")
        scaled = residual * lax.rsqrt(squares / model_width + EPSILON)[:, :, None]
        mlp_part = (scaled * mod_share[:, 4][:, None] + mod_share[:, 3][:, None]).astype(
            jnp.bfloat16
        )
        mlp_in = lax.all_gather(mlp_part, "tp", axis=2, tiled=True)
    pre_act = jnp.dot(mlp_in, up_full, preferred_element_type=jnp.float32)
    hidden_units = jax.nn.gelu(pre_act).astype(jnp.bfloat16)
    down_terms = jnp.dot(hidden_units, down_full, preferred_element_type=jnp.float32)
    if gather_weights:
        mlp_out = ring_reduce_scatter(
            down_terms.reshape(token_count, model_width), "tp", tp_count
        ).reshape(local_count, row_count, share_width)
    else:
        mlp_out = lax.psum_scatter(
            down_terms.astype(jnp.bfloat16), "tp", scatter_dimension=2, tiled=True
        ).astype(jnp.float32)
    if gather_weights:
        residual = lax.dynamic_slice_in_dim(residual_full, tp_rank * share_width, share_width, 2)
        mod_share = lax.dynamic_slice_in_dim(mod_rows, tp_rank * share_width, share_width, 2)
    result = residual + mod_share[:, 5][:, None] * mlp_out
    return result.astype(jnp.bfloat16)


def solution(mesh):
    placed = (
        P(("rep", "span"), None, "tp"),
        P(("rep", "span")),
        P("rep"),
        P("rep", None),
        P("rep"),
        P(("rep", "span"), None, None, "tp"),
        P(),
        P(None, None, "tp"),
        P("tp", None),
        P(None, ("span", "tp")),
        P(("span", "tp"), None),
    )
    return jax.shard_map(
        local, mesh=mesh, in_specs=placed, out_specs=P(("rep", "span"), None, "tp"), check_vma=False
    )
```

```python
import functools
import math

import jax
import jax.numpy as jnp
from jax import lax
from jax.experimental import pallas as pl
from jax.experimental.pallas import tpu as pltpu
from jax.sharding import PartitionSpec as P

HEAD_DIM = 128


EPSILON = 1e-06
NEGATIVE = -1e30
WEIGHT_GATHER_BYTES = 24 * 2**20


def normalize(values):
    return values * lax.rsqrt(jnp.mean(values * values, axis=-1, keepdims=True) + EPSILON)


def snake_cycle(count):
    return list(range(0, count, 2)) + list(range(count - 1, 0, -2)) if count % 2 == 0 else list(range(count))


def ring_gather(block, axis_name, count):
    cycle = snake_cycle(count)
    ahead = [(cycle[p], cycle[(p + 1) % count]) for p in range(count)]
    behind = [(cycle[p], cycle[(p - 1) % count]) for p in range(count)]
    blocks = [block]
    forward = block
    for _ in range(count // 2):
        forward = lax.ppermute(forward, axis_name, ahead)
        blocks.append(forward)
    backward = block
    for _ in range((count - 1) // 2):
        backward = lax.ppermute(backward, axis_name, behind)
        blocks.append(backward)
    return blocks


def ring_reduce_scatter(terms, axis_name, count):
    token_count, width = terms.shape
    block = width // count
    half = block // 2
    cycle = snake_cycle(count)
    position = jnp.array([cycle.index(t) for t in range(count)], jnp.int32)[lax.axis_index(axis_name)]
    owners = jnp.array(cycle, jnp.int32)
    rounded = terms.astype(jnp.bfloat16)

    def own_part(slot, side):
        start = owners[slot % count] * block + side * half
        return lax.dynamic_slice_in_dim(rounded, start, half, 1).astype(jnp.float32)

    ahead = [(cycle[p], cycle[(p + 1) % count]) for p in range(count)]
    behind = [(cycle[p], cycle[(p - 1) % count]) for p in range(count)]
    forward = own_part(position - 1 + count, 0)
    backward = own_part(position + 1, 1)
    for step in range(count - 1):
        forward = lax.ppermute(forward.astype(jnp.bfloat16), axis_name, ahead).astype(jnp.float32)
        forward = forward + own_part(position - 2 - step + 2 * count, 0)
        backward = lax.ppermute(backward.astype(jnp.bfloat16), axis_name, behind).astype(jnp.float32)
        backward = backward + own_part(position + 2 + step, 1)
    return jnp.concatenate([forward, backward], axis=1)


def out_proj_kernel(group_count, tiles_per_half, span_ref, *refs):
    att_refs = refs[:group_count]
    mine_refs = refs[group_count:2 * group_count]
    other_refs = refs[2 * group_count:3 * group_count]
    out_ref = refs[3 * group_count]
    tile = pl.program_id(0)

    def accumulate(w_refs):
        total = None
        for group in range(group_count):
            term = jnp.dot(att_refs[group][...], w_refs[group][...], preferred_element_type=jnp.float32)
            term = term.astype(jnp.bfloat16).astype(jnp.float32)
            total = term if total is None else total + term
        out_ref[...] = total

    @pl.when(tile < tiles_per_half)
    def _():
        accumulate(mine_refs)

    @pl.when(tile >= tiles_per_half)
    def _():
        accumulate(other_refs)


def grouped_out_proj(span_index, att_blocks, mine_blocks, other_blocks, tile_width=512):
    group_count = len(att_blocks)
    token_count, head_width = att_blocks[0].shape
    half_width = mine_blocks[0].shape[1]
    tile_width = min(tile_width, half_width)
    tiles_per_half = half_width // tile_width
    att_spec = pl.BlockSpec((token_count, head_width), lambda n, s: (0, 0))
    mine_spec = pl.BlockSpec(
        (head_width, tile_width), lambda n, s: (0, jnp.minimum(n, tiles_per_half - 1))
    )
    other_spec = pl.BlockSpec(
        (head_width, tile_width), lambda n, s: (0, jnp.maximum(n - tiles_per_half, 0))
    )
    out_spec = pl.BlockSpec(
        (token_count, tile_width),
        lambda n, s: (0, ((n // tiles_per_half + s[0]) % 2) * tiles_per_half + n % tiles_per_half),
    )
    flops = 2 * token_count * head_width * group_count * half_width * 2
    moved = 2 * (group_count * token_count * head_width + 2 * group_count * head_width * half_width)
    return pl.pallas_call(
        functools.partial(out_proj_kernel, group_count, tiles_per_half),
        out_shape=jax.ShapeDtypeStruct((token_count, 2 * half_width), jnp.float32),
        grid_spec=pltpu.PrefetchScalarGridSpec(
            num_scalar_prefetch=1,
            grid=(2 * tiles_per_half,),
            in_specs=[att_spec] * group_count + [mine_spec] * group_count + [other_spec] * group_count,
            out_specs=out_spec,
        ),
        cost_estimate=pl.CostEstimate(
            flops=flops, bytes_accessed=moved + token_count * 2 * half_width * 4, transcendentals=0
        ),
    )(jnp.reshape(span_index, (1,)).astype(jnp.int32), *att_blocks, *mine_blocks, *other_blocks)


def select_row(source, target):
    matches = jnp.arange(source.shape[0], dtype=jnp.int32) == target
    return jnp.sum(jnp.where(matches.reshape((-1,) + (1,) * (source.ndim - 1)), source, 0), axis=0)


def attend(queries, cache_all, fresh_all, cache_seen, fresh_seen):
    row_count, head_count, head_size = queries.shape
    cache_keys = cache_all[:, :, 0].reshape(-1, head_count, head_size)
    cache_vals = cache_all[:, :, 1].reshape(-1, head_count, head_size)
    fresh_keys = fresh_all[:, :, 0].reshape(-1, head_count, head_size)
    fresh_vals = fresh_all[:, :, 1].reshape(-1, head_count, head_size)
    score_scale = 1.0 / math.sqrt(head_size)
    cache_scores = (
        jnp.einsum("qhd,khd->hqk", queries, cache_keys, preferred_element_type=jnp.float32)
        * score_scale
    )
    fresh_scores = (
        jnp.einsum("qhd,khd->hqk", queries, fresh_keys, preferred_element_type=jnp.float32)
        * score_scale
    )
    cache_scores = jnp.where(cache_seen[None, None, :], cache_scores, NEGATIVE)
    fresh_scores = jnp.where(fresh_seen[None, None, :], fresh_scores, NEGATIVE)
    scores = jnp.concatenate([cache_scores, fresh_scores], axis=2)
    row_max = jnp.max(scores, axis=2, keepdims=True)
    exp_terms = jnp.exp(scores - row_max)
    weights = (exp_terms / jnp.sum(exp_terms, axis=2, keepdims=True)).astype(jnp.bfloat16)
    split_at = cache_keys.shape[0]
    attended = jnp.einsum(
        "hqk,khd->qhd", weights[:, :, :split_at], cache_vals, preferred_element_type=jnp.float32
    )
    attended = attended + jnp.einsum(
        "hqk,khd->qhd", weights[:, :, split_at:], fresh_vals, preferred_element_type=jnp.float32
    )
    return attended.astype(jnp.bfloat16).reshape(row_count, head_count * head_size)


def local(
    hidden_in, levels, order, cache_mask, finished, cache_kv, modulation, w_qkv, w_out, w_up, w_down
):
    span_index = lax.axis_index("span")
    tp_rank = lax.axis_index("tp")
    span_count = lax.psum(1, "span")
    tp_count = lax.psum(1, "tp")
    model_width = modulation.shape[2]
    share_width = hidden_in.shape[2]
    local_count = hidden_in.shape[0]
    row_count = hidden_in.shape[1]
    token_count = local_count * row_count
    gather_weights = (
        tp_count * w_out.size * w_out.dtype.itemsize <= WEIGHT_GATHER_BYTES and span_count == 2
    )
    if gather_weights:
        cycle = snake_cycle(tp_count)
        position = jnp.array([cycle.index(t) for t in range(tp_count)], jnp.int32)[tp_rank]
        steps = list(range(tp_count // 2 + 1)) + [-k for k in range(1, (tp_count - 1) // 2 + 1)]
        owners = jnp.array(cycle, jnp.int32)
        gathered = jnp.zeros(hidden_in.shape[:2] + (model_width,), hidden_in.dtype)
        for step, piece in zip(steps, ring_gather(hidden_in, "tp", tp_count)):
            owner = owners[(position - step + tp_count) % tp_count]
            gathered = lax.dynamic_update_slice_in_dim(gathered, piece, owner * share_width, 2)
        gathered = gathered.astype(jnp.float32)
    else:
        gathered = lax.all_gather(hidden_in, "tp", axis=2, tiled=True).astype(jnp.float32)
    if gather_weights:
        column_part = model_width // span_count
        w_out_part = lax.dynamic_slice_in_dim(w_out, span_index * column_part, column_part, 1)
        mine_blocks = ring_gather(w_out_part, "tp", tp_count)
        other_blocks = [lax.ppermute(b, "span", [(0, 1), (1, 0)]) for b in mine_blocks]
    up_full, down_full = (
        lax.all_gather(w_up, "span", axis=1, tiled=True),
        lax.all_gather(w_down, "span", axis=0, tiled=True),
    )
    mod_table = modulation.reshape(modulation.shape[0], -1)
    picker = (jnp.arange(mod_table.shape[0], dtype=jnp.int32)[None, :] == levels[:, None]).astype(
        jnp.bfloat16
    )
    mod_rows = jnp.dot(picker, mod_table, preferred_element_type=jnp.float32).reshape(
        local_count, 6, model_width
    )
    attn_in = (normalize(gathered) * mod_rows[:, 1][:, None] + mod_rows[:, 0][:, None]).astype(
        jnp.bfloat16
    )
    per_device = w_qkv.shape[2]
    projected = jnp.dot(
        attn_in.reshape(token_count, model_width),
        w_qkv.reshape(model_width, -1),
        preferred_element_type=jnp.float32,
    )
    projected = projected.astype(jnp.bfloat16).reshape(local_count, row_count, 3, per_device)
    queries = projected[:, :, 0].reshape(local_count, row_count, -1, HEAD_DIM)
    fresh_kv = projected[:, :, 1:]
    cache_all, fresh_all = (
        lax.all_gather(cache_kv, "span", axis=0, tiled=True),
        lax.all_gather(fresh_kv, "span", axis=0, tiled=True),
    )
    positions = jnp.arange(cache_mask.shape[0], dtype=jnp.int32)
    my_spans = span_index * local_count + jnp.arange(local_count, dtype=jnp.int32)
    mask_rows = jax.vmap(lambda target: select_row(cache_mask, target))(my_spans)
    my_order = jax.vmap(lambda target: select_row(order, target))(my_spans)
    cache_seen = jnp.repeat(
        (mask_rows == 1) | (positions[None, :] == finished[0]), row_count, axis=1
    )
    fresh_seen = jnp.repeat(order[None, :] <= my_order[:, None], row_count, axis=1)
    attended = jax.vmap(
        lambda q_rows, c_seen, f_seen: attend(q_rows, cache_all, fresh_all, c_seen, f_seen)
    )(queries, cache_seen, fresh_seen)
    if gather_weights:
        att_blocks = ring_gather(attended.reshape(token_count, per_device), "tp", tp_count)
        attn_out = grouped_out_proj(span_index, att_blocks, mine_blocks, other_blocks)
        attn_out = attn_out.reshape(local_count, row_count, model_width)
        residual_full = gathered + mod_rows[:, 2][:, None] * attn_out
        mlp_in = (
            normalize(residual_full) * mod_rows[:, 4][:, None] + mod_rows[:, 3][:, None]
        ).astype(jnp.bfloat16)
    else:
        partial_value = jnp.dot(
            attended.reshape(token_count, -1), w_out, preferred_element_type=jnp.float32
        ).reshape(local_count, row_count, model_width)
        attn_part = lax.psum_scatter(
            partial_value.astype(jnp.bfloat16), "tp", scatter_dimension=2, tiled=True
        ).astype(jnp.float32)
        mod_share = lax.dynamic_slice_in_dim(mod_rows, tp_rank * share_width, share_width, 2)
        residual = hidden_in.astype(jnp.float32) + mod_share[:, 2][:, None] * attn_part
        squares = lax.psum(jnp.sum(residual * residual, axis=2), "tp")
        scaled = residual * lax.rsqrt(squares / model_width + EPSILON)[:, :, None]
        mlp_part = (scaled * mod_share[:, 4][:, None] + mod_share[:, 3][:, None]).astype(
            jnp.bfloat16
        )
        mlp_in = lax.all_gather(mlp_part, "tp", axis=2, tiled=True)
    pre_act = jnp.dot(mlp_in, up_full, preferred_element_type=jnp.float32)
    hidden_units = jax.nn.gelu(pre_act).astype(jnp.bfloat16)
    down_terms = jnp.dot(hidden_units, down_full, preferred_element_type=jnp.float32)
    if gather_weights:
        mlp_out = ring_reduce_scatter(
            down_terms.reshape(token_count, model_width), "tp", tp_count
        ).reshape(local_count, row_count, share_width)
    else:
        mlp_out = lax.psum_scatter(
            down_terms.astype(jnp.bfloat16), "tp", scatter_dimension=2, tiled=True
        ).astype(jnp.float32)
    if gather_weights:
        residual = lax.dynamic_slice_in_dim(residual_full, tp_rank * share_width, share_width, 2)
        mod_share = lax.dynamic_slice_in_dim(mod_rows, tp_rank * share_width, share_width, 2)
    result = residual + mod_share[:, 5][:, None] * mlp_out
    return result.astype(jnp.bfloat16)


def solution(mesh):
    placed = (
        P(("rep", "span"), None, "tp"),
        P(("rep", "span")),
        P("rep"),
        P("rep", None),
        P("rep"),
        P(("rep", "span"), None, None, "tp"),
        P(),
        P(None, None, "tp"),
        P("tp", None),
        P(None, ("span", "tp")),
        P(("span", "tp"), None),
    )
    return jax.shard_map(
        local, mesh=mesh, in_specs=placed, out_specs=P(("rep", "span"), None, "tp"), check_vma=False
    )
```

```python
import functools
import math

import jax
import jax.numpy as jnp
from jax import lax
from jax.experimental import pallas as pl
from jax.experimental.pallas import tpu as pltpu
from jax.sharding import PartitionSpec as P

HEAD_DIM = 128


EPSILON = 1e-06
NEGATIVE = -1e30
WEIGHT_GATHER_BYTES = 24 * 2**20


def normalize(values):
    return values * lax.rsqrt(jnp.mean(values * values, axis=-1, keepdims=True) + EPSILON)


def snake_cycle(count):
    return list(range(0, count, 2)) + list(range(count - 1, 0, -2)) if count % 2 == 0 else list(range(count))


def ring_gather(block, axis_name, count):
    cycle = snake_cycle(count)
    ahead = [(cycle[p], cycle[(p + 1) % count]) for p in range(count)]
    behind = [(cycle[p], cycle[(p - 1) % count]) for p in range(count)]
    blocks = [block]
    forward = block
    for _ in range(count // 2):
        forward = lax.ppermute(forward, axis_name, ahead)
        blocks.append(forward)
    backward = block
    for _ in range((count - 1) // 2):
        backward = lax.ppermute(backward, axis_name, behind)
        blocks.append(backward)
    return blocks


def ring_reduce_scatter(terms, axis_name, count):
    token_count, width = terms.shape
    block = width // count
    half = block // 2
    cycle = snake_cycle(count)
    position = jnp.array([cycle.index(t) for t in range(count)], jnp.int32)[lax.axis_index(axis_name)]
    owners = jnp.array(cycle, jnp.int32)
    rounded = terms.astype(jnp.bfloat16)

    def own_part(slot, side):
        start = owners[slot % count] * block + side * half
        return lax.dynamic_slice_in_dim(rounded, start, half, 1).astype(jnp.float32)

    ahead = [(cycle[p], cycle[(p + 1) % count]) for p in range(count)]
    behind = [(cycle[p], cycle[(p - 1) % count]) for p in range(count)]
    forward = own_part(position - 1 + count, 0)
    backward = own_part(position + 1, 1)
    for step in range(count - 1):
        forward = lax.ppermute(forward.astype(jnp.bfloat16), axis_name, ahead).astype(jnp.float32)
        forward = forward + own_part(position - 2 - step + 2 * count, 0)
        backward = lax.ppermute(backward.astype(jnp.bfloat16), axis_name, behind).astype(jnp.float32)
        backward = backward + own_part(position + 2 + step, 1)
    return jnp.concatenate([forward, backward], axis=1)


def out_proj_kernel(group_count, set_count, tiles_per_set, place_ref, *refs):
    att_refs = refs[:group_count]
    out_ref = refs[-1]
    tile = pl.program_id(0)

    def accumulate(w_refs):
        total = None
        for group in range(group_count):
            term = jnp.dot(att_refs[group][...], w_refs[group][...], preferred_element_type=jnp.float32)
            term = term.astype(jnp.bfloat16).astype(jnp.float32)
            total = term if total is None else total + term
        out_ref[...] = total

    for which in range(set_count):
        w_refs = refs[group_count * (which + 1):group_count * (which + 2)]

        @pl.when(tile // tiles_per_set == which)
        def _():
            accumulate(w_refs)


def grouped_out_proj(placement, att_blocks, weight_sets, tile_width=512):
    group_count = len(att_blocks)
    set_count = len(weight_sets)
    token_count, head_width = att_blocks[0].shape
    set_width = weight_sets[0][0].shape[1]
    tile_width = min(tile_width, set_width)
    tiles_per_set = set_width // tile_width
    att_spec = pl.BlockSpec((token_count, head_width), lambda n, p: (0, 0))

    def weight_spec(which):
        return pl.BlockSpec(
            (head_width, tile_width),
            lambda n, p: (0, jnp.clip(n - which * tiles_per_set, 0, tiles_per_set - 1)),
        )

    out_spec = pl.BlockSpec(
        (token_count, tile_width),
        lambda n, p: (0, p[n // tiles_per_set] * tiles_per_set + n % tiles_per_set),
    )
    in_specs = [att_spec] * group_count
    for which in range(set_count):
        in_specs += [weight_spec(which)] * group_count
    width = set_count * set_width
    flops = 2 * token_count * head_width * group_count * width
    moved = 2 * group_count * token_count * head_width + 2 * group_count * head_width * width
    return pl.pallas_call(
        functools.partial(out_proj_kernel, group_count, set_count, tiles_per_set),
        out_shape=jax.ShapeDtypeStruct((token_count, width), jnp.float32),
        grid_spec=pltpu.PrefetchScalarGridSpec(
            num_scalar_prefetch=1,
            grid=(set_count * tiles_per_set,),
            in_specs=in_specs,
            out_specs=out_spec,
        ),
        cost_estimate=pl.CostEstimate(
            flops=flops, bytes_accessed=moved + token_count * width * 4, transcendentals=0
        ),
    )(placement, *att_blocks, *[b for blocks in weight_sets for b in blocks])


def select_row(source, target):
    matches = jnp.arange(source.shape[0], dtype=jnp.int32) == target
    return jnp.sum(jnp.where(matches.reshape((-1,) + (1,) * (source.ndim - 1)), source, 0), axis=0)


def attend(queries, cache_all, fresh_all, cache_seen, fresh_seen):
    row_count, head_count, head_size = queries.shape
    cache_keys = cache_all[:, :, 0].reshape(-1, head_count, head_size)
    cache_vals = cache_all[:, :, 1].reshape(-1, head_count, head_size)
    fresh_keys = fresh_all[:, :, 0].reshape(-1, head_count, head_size)
    fresh_vals = fresh_all[:, :, 1].reshape(-1, head_count, head_size)
    score_scale = 1.0 / math.sqrt(head_size)
    cache_scores = (
        jnp.einsum("qhd,khd->hqk", queries, cache_keys, preferred_element_type=jnp.float32)
        * score_scale
    )
    fresh_scores = (
        jnp.einsum("qhd,khd->hqk", queries, fresh_keys, preferred_element_type=jnp.float32)
        * score_scale
    )
    cache_scores = jnp.where(cache_seen[None, None, :], cache_scores, NEGATIVE)
    fresh_scores = jnp.where(fresh_seen[None, None, :], fresh_scores, NEGATIVE)
    scores = jnp.concatenate([cache_scores, fresh_scores], axis=2)
    row_max = jnp.max(scores, axis=2, keepdims=True)
    exp_terms = jnp.exp(scores - row_max)
    weights = (exp_terms / jnp.sum(exp_terms, axis=2, keepdims=True)).astype(jnp.bfloat16)
    split_at = cache_keys.shape[0]
    attended = jnp.einsum(
        "hqk,khd->qhd", weights[:, :, :split_at], cache_vals, preferred_element_type=jnp.float32
    )
    attended = attended + jnp.einsum(
        "hqk,khd->qhd", weights[:, :, split_at:], fresh_vals, preferred_element_type=jnp.float32
    )
    return attended.astype(jnp.bfloat16).reshape(row_count, head_count * head_size)


def local(
    hidden_in, levels, order, cache_mask, finished, cache_kv, modulation, w_qkv, w_out, w_up, w_down
):
    span_index = lax.axis_index("span")
    tp_rank = lax.axis_index("tp")
    span_count = lax.psum(1, "span")
    rep_count = lax.psum(1, "rep")
    tp_count = lax.psum(1, "tp")
    model_width = modulation.shape[2]
    share_width = hidden_in.shape[2]
    local_count = hidden_in.shape[0]
    row_count = hidden_in.shape[1]
    token_count = local_count * row_count
    gather_weights = (
        tp_count * w_out.size * w_out.dtype.itemsize <= WEIGHT_GATHER_BYTES and span_count == 2
        and rep_count == 2
    )
    if gather_weights:
        cycle = snake_cycle(tp_count)
        position = jnp.array([cycle.index(t) for t in range(tp_count)], jnp.int32)[tp_rank]
        steps = list(range(tp_count // 2 + 1)) + [-k for k in range(1, (tp_count - 1) // 2 + 1)]
        owners = jnp.array(cycle, jnp.int32)
        gathered = jnp.zeros(hidden_in.shape[:2] + (model_width,), hidden_in.dtype)
        for step, piece in zip(steps, ring_gather(hidden_in, "tp", tp_count)):
            owner = owners[(position - step + tp_count) % tp_count]
            gathered = lax.dynamic_update_slice_in_dim(gathered, piece, owner * share_width, 2)
        gathered = gathered.astype(jnp.float32)
    else:
        gathered = lax.all_gather(hidden_in, "tp", axis=2, tiled=True).astype(jnp.float32)
    if gather_weights:
        rep_index = lax.axis_index("rep")
        column_part = model_width // (rep_count * span_count)
        slot = rep_index * span_count + span_index
        w_out_part = lax.dynamic_slice_in_dim(w_out, slot * column_part, column_part, 1)
        mine_blocks = ring_gather(w_out_part, "tp", tp_count)
        swap = [(0, 1), (1, 0)]
        rep_blocks = [lax.ppermute(b, "rep", swap) for b in mine_blocks]
        weight_sets = [
            mine_blocks,
            rep_blocks,
            [lax.ppermute(b, "span", swap) for b in mine_blocks],
            [lax.ppermute(b, "span", swap) for b in rep_blocks],
        ]
        placement = jnp.stack(
            [
                ((rep_index + dr) % 2) * span_count + (span_index + ds) % 2
                for ds in (0, 1)
                for dr in (0, 1)
            ]
        ).astype(jnp.int32)
    up_full, down_full = (
        lax.all_gather(w_up, "span", axis=1, tiled=True),
        lax.all_gather(w_down, "span", axis=0, tiled=True),
    )
    mod_table = modulation.reshape(modulation.shape[0], -1)
    picker = (jnp.arange(mod_table.shape[0], dtype=jnp.int32)[None, :] == levels[:, None]).astype(
        jnp.bfloat16
    )
    mod_rows = jnp.dot(picker, mod_table, preferred_element_type=jnp.float32).reshape(
        local_count, 6, model_width
    )
    attn_in = (normalize(gathered) * mod_rows[:, 1][:, None] + mod_rows[:, 0][:, None]).astype(
        jnp.bfloat16
    )
    per_device = w_qkv.shape[2]
    projected = jnp.dot(
        attn_in.reshape(token_count, model_width),
        w_qkv.reshape(model_width, -1),
        preferred_element_type=jnp.float32,
    )
    projected = projected.astype(jnp.bfloat16).reshape(local_count, row_count, 3, per_device)
    queries = projected[:, :, 0].reshape(local_count, row_count, -1, HEAD_DIM)
    fresh_kv = projected[:, :, 1:]
    cache_all, fresh_all = (
        lax.all_gather(cache_kv, "span", axis=0, tiled=True),
        lax.all_gather(fresh_kv, "span", axis=0, tiled=True),
    )
    positions = jnp.arange(cache_mask.shape[0], dtype=jnp.int32)
    my_spans = span_index * local_count + jnp.arange(local_count, dtype=jnp.int32)
    mask_rows = jax.vmap(lambda target: select_row(cache_mask, target))(my_spans)
    my_order = jax.vmap(lambda target: select_row(order, target))(my_spans)
    cache_seen = jnp.repeat(
        (mask_rows == 1) | (positions[None, :] == finished[0]), row_count, axis=1
    )
    fresh_seen = jnp.repeat(order[None, :] <= my_order[:, None], row_count, axis=1)
    attended = jax.vmap(
        lambda q_rows, c_seen, f_seen: attend(q_rows, cache_all, fresh_all, c_seen, f_seen)
    )(queries, cache_seen, fresh_seen)
    if gather_weights:
        att_blocks = ring_gather(attended.reshape(token_count, per_device), "tp", tp_count)
        attn_out = grouped_out_proj(placement, att_blocks, weight_sets)
        attn_out = attn_out.reshape(local_count, row_count, model_width)
        residual_full = gathered + mod_rows[:, 2][:, None] * attn_out
        mlp_in = (
            normalize(residual_full) * mod_rows[:, 4][:, None] + mod_rows[:, 3][:, None]
        ).astype(jnp.bfloat16)
    else:
        partial_value = jnp.dot(
            attended.reshape(token_count, -1), w_out, preferred_element_type=jnp.float32
        ).reshape(local_count, row_count, model_width)
        attn_part = lax.psum_scatter(
            partial_value.astype(jnp.bfloat16), "tp", scatter_dimension=2, tiled=True
        ).astype(jnp.float32)
        mod_share = lax.dynamic_slice_in_dim(mod_rows, tp_rank * share_width, share_width, 2)
        residual = hidden_in.astype(jnp.float32) + mod_share[:, 2][:, None] * attn_part
        squares = lax.psum(jnp.sum(residual * residual, axis=2), "tp")
        scaled = residual * lax.rsqrt(squares / model_width + EPSILON)[:, :, None]
        mlp_part = (scaled * mod_share[:, 4][:, None] + mod_share[:, 3][:, None]).astype(
            jnp.bfloat16
        )
        mlp_in = lax.all_gather(mlp_part, "tp", axis=2, tiled=True)
    pre_act = jnp.dot(mlp_in, up_full, preferred_element_type=jnp.float32)
    hidden_units = jax.nn.gelu(pre_act).astype(jnp.bfloat16)
    down_terms = jnp.dot(hidden_units, down_full, preferred_element_type=jnp.float32)
    if gather_weights:
        mlp_out = ring_reduce_scatter(
            down_terms.reshape(token_count, model_width), "tp", tp_count
        ).reshape(local_count, row_count, share_width)
    else:
        mlp_out = lax.psum_scatter(
            down_terms.astype(jnp.bfloat16), "tp", scatter_dimension=2, tiled=True
        ).astype(jnp.float32)
    if gather_weights:
        residual = lax.dynamic_slice_in_dim(residual_full, tp_rank * share_width, share_width, 2)
        mod_share = lax.dynamic_slice_in_dim(mod_rows, tp_rank * share_width, share_width, 2)
    result = residual + mod_share[:, 5][:, None] * mlp_out
    return result.astype(jnp.bfloat16)


def solution(mesh):
    placed = (
        P(("rep", "span"), None, "tp"),
        P(("rep", "span")),
        P("rep"),
        P("rep", None),
        P("rep"),
        P(("rep", "span"), None, None, "tp"),
        P(),
        P(None, None, "tp"),
        P("tp", None),
        P(None, ("span", "tp")),
        P(("span", "tp"), None),
    )
    return jax.shard_map(
        local, mesh=mesh, in_specs=placed, out_specs=P(("rep", "span"), None, "tp"), check_vma=False
    )
```

```python
import functools
import math

import jax
import jax.numpy as jnp
from jax import lax
from jax.experimental import pallas as pl
from jax.experimental.pallas import tpu as pltpu
from jax.sharding import PartitionSpec as P

HEAD_DIM = 128


EPSILON = 1e-06
NEGATIVE = -1e30
WEIGHT_GATHER_BYTES = 24 * 2**20


def normalize(values):
    return values * lax.rsqrt(jnp.mean(values * values, axis=-1, keepdims=True) + EPSILON)


def snake_cycle(count):
    return list(range(0, count, 2)) + list(range(count - 1, 0, -2)) if count % 2 == 0 else list(range(count))


def ring_gather(block, axis_name, count):
    cycle = snake_cycle(count)
    ahead = [(cycle[p], cycle[(p + 1) % count]) for p in range(count)]
    behind = [(cycle[p], cycle[(p - 1) % count]) for p in range(count)]
    blocks = [block]
    forward = block
    for _ in range(count // 2):
        forward = lax.ppermute(forward, axis_name, ahead)
        blocks.append(forward)
    backward = block
    for _ in range((count - 1) // 2):
        backward = lax.ppermute(backward, axis_name, behind)
        blocks.append(backward)
    return blocks


def ring_reduce_scatter(terms, axis_name, count):
    token_count, width = terms.shape
    block = width // count
    half = block // 2
    cycle = snake_cycle(count)
    position = jnp.array([cycle.index(t) for t in range(count)], jnp.int32)[lax.axis_index(axis_name)]
    owners = jnp.array(cycle, jnp.int32)
    rounded = terms.astype(jnp.bfloat16)

    def own_part(slot, side):
        start = owners[slot % count] * block + side * half
        return lax.dynamic_slice_in_dim(rounded, start, half, 1).astype(jnp.float32)

    ahead = [(cycle[p], cycle[(p + 1) % count]) for p in range(count)]
    behind = [(cycle[p], cycle[(p - 1) % count]) for p in range(count)]
    forward = own_part(position - 1 + count, 0)
    backward = own_part(position + 1, 1)
    for step in range(count - 1):
        forward = lax.ppermute(forward.astype(jnp.bfloat16), axis_name, ahead).astype(jnp.float32)
        forward = forward + own_part(position - 2 - step + 2 * count, 0)
        backward = lax.ppermute(backward.astype(jnp.bfloat16), axis_name, behind).astype(jnp.float32)
        backward = backward + own_part(position + 2 + step, 1)
    return jnp.concatenate([forward, backward], axis=1)


def direct_gather(block, axis_name, count):
    cycle = snake_cycle(count)
    shifts = list(range(1, count // 2 + 1)) + [-k for k in range(1, (count - 1) // 2 + 1)]
    blocks = [block]
    for shift in shifts:
        pairs = [(cycle[(p - shift) % count], cycle[p]) for p in range(count)]
        blocks.append(lax.ppermute(block, axis_name, pairs))
    return blocks


def out_proj_kernel(group_count, tiles_per_half, span_ref, *refs):
    att_refs = refs[:group_count]
    mine_refs = refs[group_count:2 * group_count]
    other_refs = refs[2 * group_count:3 * group_count]
    out_ref = refs[3 * group_count]
    tile = pl.program_id(0)

    def accumulate(w_refs):
        total = None
        for group in range(group_count):
            term = jnp.dot(att_refs[group][...], w_refs[group][...], preferred_element_type=jnp.float32)
            term = term.astype(jnp.bfloat16).astype(jnp.float32)
            total = term if total is None else total + term
        out_ref[...] = total

    @pl.when(tile < tiles_per_half)
    def _():
        accumulate(mine_refs)

    @pl.when(tile >= tiles_per_half)
    def _():
        accumulate(other_refs)


def grouped_out_proj(span_index, att_blocks, mine_blocks, other_blocks, tile_width=512):
    group_count = len(att_blocks)
    token_count, head_width = att_blocks[0].shape
    half_width = mine_blocks[0].shape[1]
    tile_width = min(tile_width, half_width)
    tiles_per_half = half_width // tile_width
    att_spec = pl.BlockSpec((token_count, head_width), lambda n, s: (0, 0))
    mine_spec = pl.BlockSpec(
        (head_width, tile_width), lambda n, s: (0, jnp.minimum(n, tiles_per_half - 1))
    )
    other_spec = pl.BlockSpec(
        (head_width, tile_width), lambda n, s: (0, jnp.maximum(n - tiles_per_half, 0))
    )
    out_spec = pl.BlockSpec(
        (token_count, tile_width),
        lambda n, s: (0, ((n // tiles_per_half + s[0]) % 2) * tiles_per_half + n % tiles_per_half),
    )
    flops = 2 * token_count * head_width * group_count * half_width * 2
    moved = 2 * (group_count * token_count * head_width + 2 * group_count * head_width * half_width)
    return pl.pallas_call(
        functools.partial(out_proj_kernel, group_count, tiles_per_half),
        out_shape=jax.ShapeDtypeStruct((token_count, 2 * half_width), jnp.float32),
        grid_spec=pltpu.PrefetchScalarGridSpec(
            num_scalar_prefetch=1,
            grid=(2 * tiles_per_half,),
            in_specs=[att_spec] * group_count + [mine_spec] * group_count + [other_spec] * group_count,
            out_specs=out_spec,
        ),
        cost_estimate=pl.CostEstimate(
            flops=flops, bytes_accessed=moved + token_count * 2 * half_width * 4, transcendentals=0
        ),
    )(jnp.reshape(span_index, (1,)).astype(jnp.int32), *att_blocks, *mine_blocks, *other_blocks)


def select_row(source, target):
    matches = jnp.arange(source.shape[0], dtype=jnp.int32) == target
    return jnp.sum(jnp.where(matches.reshape((-1,) + (1,) * (source.ndim - 1)), source, 0), axis=0)


def attend(queries, cache_all, fresh_all, cache_seen, fresh_seen):
    row_count, head_count, head_size = queries.shape
    cache_keys = cache_all[:, :, 0].reshape(-1, head_count, head_size)
    cache_vals = cache_all[:, :, 1].reshape(-1, head_count, head_size)
    fresh_keys = fresh_all[:, :, 0].reshape(-1, head_count, head_size)
    fresh_vals = fresh_all[:, :, 1].reshape(-1, head_count, head_size)
    score_scale = 1.0 / math.sqrt(head_size)
    cache_scores = (
        jnp.einsum("qhd,khd->hqk", queries, cache_keys, preferred_element_type=jnp.float32)
        * score_scale
    )
    fresh_scores = (
        jnp.einsum("qhd,khd->hqk", queries, fresh_keys, preferred_element_type=jnp.float32)
        * score_scale
    )
    cache_scores = jnp.where(cache_seen[None, None, :], cache_scores, NEGATIVE)
    fresh_scores = jnp.where(fresh_seen[None, None, :], fresh_scores, NEGATIVE)
    scores = jnp.concatenate([cache_scores, fresh_scores], axis=2)
    row_max = jnp.max(scores, axis=2, keepdims=True)
    exp_terms = jnp.exp(scores - row_max)
    weights = (exp_terms / jnp.sum(exp_terms, axis=2, keepdims=True)).astype(jnp.bfloat16)
    split_at = cache_keys.shape[0]
    attended = jnp.einsum(
        "hqk,khd->qhd", weights[:, :, :split_at], cache_vals, preferred_element_type=jnp.float32
    )
    attended = attended + jnp.einsum(
        "hqk,khd->qhd", weights[:, :, split_at:], fresh_vals, preferred_element_type=jnp.float32
    )
    return attended.astype(jnp.bfloat16).reshape(row_count, head_count * head_size)


def local(
    hidden_in, levels, order, cache_mask, finished, cache_kv, modulation, w_qkv, w_out, w_up, w_down
):
    span_index = lax.axis_index("span")
    tp_rank = lax.axis_index("tp")
    span_count = lax.psum(1, "span")
    tp_count = lax.psum(1, "tp")
    model_width = modulation.shape[2]
    share_width = hidden_in.shape[2]
    local_count = hidden_in.shape[0]
    row_count = hidden_in.shape[1]
    token_count = local_count * row_count
    gather_weights = (
        tp_count * w_out.size * w_out.dtype.itemsize <= WEIGHT_GATHER_BYTES and span_count == 2
    )
    if gather_weights:
        cycle = snake_cycle(tp_count)
        position = jnp.array([cycle.index(t) for t in range(tp_count)], jnp.int32)[tp_rank]
        steps = list(range(tp_count // 2 + 1)) + [-k for k in range(1, (tp_count - 1) // 2 + 1)]
        owners = jnp.array(cycle, jnp.int32)
        gathered = jnp.zeros(hidden_in.shape[:2] + (model_width,), hidden_in.dtype)
        for step, piece in zip(steps, ring_gather(hidden_in, "tp", tp_count)):
            owner = owners[(position - step + tp_count) % tp_count]
            gathered = lax.dynamic_update_slice_in_dim(gathered, piece, owner * share_width, 2)
        gathered = gathered.astype(jnp.float32)
    else:
        gathered = lax.all_gather(hidden_in, "tp", axis=2, tiled=True).astype(jnp.float32)
    if gather_weights:
        column_part = model_width // span_count
        w_out_part = lax.dynamic_slice_in_dim(w_out, span_index * column_part, column_part, 1)
        mine_blocks = ring_gather(w_out_part, "tp", tp_count)
        other_blocks = [lax.ppermute(b, "span", [(0, 1), (1, 0)]) for b in mine_blocks]
    up_full, down_full = (
        lax.all_gather(w_up, "span", axis=1, tiled=True),
        lax.all_gather(w_down, "span", axis=0, tiled=True),
    )
    mod_table = modulation.reshape(modulation.shape[0], -1)
    picker = (jnp.arange(mod_table.shape[0], dtype=jnp.int32)[None, :] == levels[:, None]).astype(
        jnp.bfloat16
    )
    mod_rows = jnp.dot(picker, mod_table, preferred_element_type=jnp.float32).reshape(
        local_count, 6, model_width
    )
    attn_in = (normalize(gathered) * mod_rows[:, 1][:, None] + mod_rows[:, 0][:, None]).astype(
        jnp.bfloat16
    )
    per_device = w_qkv.shape[2]
    projected = jnp.dot(
        attn_in.reshape(token_count, model_width),
        w_qkv.reshape(model_width, -1),
        preferred_element_type=jnp.float32,
    )
    projected = projected.astype(jnp.bfloat16).reshape(local_count, row_count, 3, per_device)
    queries = projected[:, :, 0].reshape(local_count, row_count, -1, HEAD_DIM)
    fresh_kv = projected[:, :, 1:]
    cache_all, fresh_all = (
        lax.all_gather(cache_kv, "span", axis=0, tiled=True),
        lax.all_gather(fresh_kv, "span", axis=0, tiled=True),
    )
    positions = jnp.arange(cache_mask.shape[0], dtype=jnp.int32)
    my_spans = span_index * local_count + jnp.arange(local_count, dtype=jnp.int32)
    mask_rows = jax.vmap(lambda target: select_row(cache_mask, target))(my_spans)
    my_order = jax.vmap(lambda target: select_row(order, target))(my_spans)
    cache_seen = jnp.repeat(
        (mask_rows == 1) | (positions[None, :] == finished[0]), row_count, axis=1
    )
    fresh_seen = jnp.repeat(order[None, :] <= my_order[:, None], row_count, axis=1)
    attended = jax.vmap(
        lambda q_rows, c_seen, f_seen: attend(q_rows, cache_all, fresh_all, c_seen, f_seen)
    )(queries, cache_seen, fresh_seen)
    if gather_weights:
        att_blocks = direct_gather(attended.reshape(token_count, per_device), "tp", tp_count)
        attn_out = grouped_out_proj(span_index, att_blocks, mine_blocks, other_blocks)
        attn_out = attn_out.reshape(local_count, row_count, model_width)
        residual_full = gathered + mod_rows[:, 2][:, None] * attn_out
        mlp_in = (
            normalize(residual_full) * mod_rows[:, 4][:, None] + mod_rows[:, 3][:, None]
        ).astype(jnp.bfloat16)
    else:
        partial_value = jnp.dot(
            attended.reshape(token_count, -1), w_out, preferred_element_type=jnp.float32
        ).reshape(local_count, row_count, model_width)
        attn_part = lax.psum_scatter(
            partial_value.astype(jnp.bfloat16), "tp", scatter_dimension=2, tiled=True
        ).astype(jnp.float32)
        mod_share = lax.dynamic_slice_in_dim(mod_rows, tp_rank * share_width, share_width, 2)
        residual = hidden_in.astype(jnp.float32) + mod_share[:, 2][:, None] * attn_part
        squares = lax.psum(jnp.sum(residual * residual, axis=2), "tp")
        scaled = residual * lax.rsqrt(squares / model_width + EPSILON)[:, :, None]
        mlp_part = (scaled * mod_share[:, 4][:, None] + mod_share[:, 3][:, None]).astype(
            jnp.bfloat16
        )
        mlp_in = lax.all_gather(mlp_part, "tp", axis=2, tiled=True)
    pre_act = jnp.dot(mlp_in, up_full, preferred_element_type=jnp.float32)
    hidden_units = jax.nn.gelu(pre_act).astype(jnp.bfloat16)
    down_terms = jnp.dot(hidden_units, down_full, preferred_element_type=jnp.float32)
    if gather_weights:
        mlp_out = ring_reduce_scatter(
            down_terms.reshape(token_count, model_width), "tp", tp_count
        ).reshape(local_count, row_count, share_width)
    else:
        mlp_out = lax.psum_scatter(
            down_terms.astype(jnp.bfloat16), "tp", scatter_dimension=2, tiled=True
        ).astype(jnp.float32)
    if gather_weights:
        residual = lax.dynamic_slice_in_dim(residual_full, tp_rank * share_width, share_width, 2)
        mod_share = lax.dynamic_slice_in_dim(mod_rows, tp_rank * share_width, share_width, 2)
    result = residual + mod_share[:, 5][:, None] * mlp_out
    return result.astype(jnp.bfloat16)


def solution(mesh):
    placed = (
        P(("rep", "span"), None, "tp"),
        P(("rep", "span")),
        P("rep"),
        P("rep", None),
        P("rep"),
        P(("rep", "span"), None, None, "tp"),
        P(),
        P(None, None, "tp"),
        P("tp", None),
        P(None, ("span", "tp")),
        P(("span", "tp"), None),
    )
    return jax.shard_map(
        local, mesh=mesh, in_specs=placed, out_specs=P(("rep", "span"), None, "tp"), check_vma=False
    )
```

```python
import functools
import math

import jax
import jax.numpy as jnp
from jax import lax
from jax.experimental import pallas as pl
from jax.experimental.pallas import tpu as pltpu
from jax.sharding import PartitionSpec as P

HEAD_DIM = 128


EPSILON = 1e-06
NEGATIVE = -1e30
WEIGHT_GATHER_BYTES = 24 * 2**20


def normalize(values):
    return values * lax.rsqrt(jnp.mean(values * values, axis=-1, keepdims=True) + EPSILON)


def snake_cycle(count):
    return list(range(0, count, 2)) + list(range(count - 1, 0, -2)) if count % 2 == 0 else list(range(count))


def ring_gather(block, axis_name, count):
    cycle = snake_cycle(count)
    ahead = [(cycle[p], cycle[(p + 1) % count]) for p in range(count)]
    behind = [(cycle[p], cycle[(p - 1) % count]) for p in range(count)]
    blocks = [block]
    forward = block
    for _ in range(count // 2):
        forward = lax.ppermute(forward, axis_name, ahead)
        blocks.append(forward)
    backward = block
    for _ in range((count - 1) // 2):
        backward = lax.ppermute(backward, axis_name, behind)
        blocks.append(backward)
    return blocks


def ring_reduce_scatter(terms, axis_name, count):
    token_count, width = terms.shape
    block = width // count
    half = block // 2
    cycle = snake_cycle(count)
    position = jnp.array([cycle.index(t) for t in range(count)], jnp.int32)[lax.axis_index(axis_name)]
    owners = jnp.array(cycle, jnp.int32)
    rounded = terms.astype(jnp.bfloat16)

    def own_part(slot, side):
        start = owners[slot % count] * block + side * half
        return lax.dynamic_slice_in_dim(rounded, start, half, 1).astype(jnp.float32)

    ahead = [(cycle[p], cycle[(p + 1) % count]) for p in range(count)]
    behind = [(cycle[p], cycle[(p - 1) % count]) for p in range(count)]
    forward = own_part(position - 1 + count, 0)
    backward = own_part(position + 1, 1)
    for step in range(count - 1):
        forward = lax.ppermute(forward.astype(jnp.bfloat16), axis_name, ahead).astype(jnp.float32)
        forward = forward + own_part(position - 2 - step + 2 * count, 0)
        backward = lax.ppermute(backward.astype(jnp.bfloat16), axis_name, behind).astype(jnp.float32)
        backward = backward + own_part(position + 2 + step, 1)
    return jnp.concatenate([forward, backward], axis=1)


def out_proj_kernel(group_count, tiles_per_half, row_count, span_ref, *refs):
    att_refs = refs[:group_count]
    mine_refs = refs[group_count:2 * group_count]
    other_refs = refs[2 * group_count:3 * group_count]
    hidden_ref, scale_ref, out_ref, squares_ref = refs[3 * group_count:]
    tile = pl.program_id(0)

    def accumulate(w_refs):
        total = None
        for group in range(group_count):
            term = jnp.dot(att_refs[group][...], w_refs[group][...], preferred_element_type=jnp.float32)
            term = term.astype(jnp.bfloat16).astype(jnp.float32)
            total = term if total is None else total + term
        for span in range(scale_ref.shape[0]):
            rows = slice(span * row_count, (span + 1) * row_count)
            out_ref[rows, :] = (
                hidden_ref[rows, :].astype(jnp.float32) + scale_ref[span:span + 1, :] * total[rows, :]
            )
        result = out_ref[...]
        squares_ref[...] = jnp.broadcast_to(
            jnp.sum(result * result, axis=1, keepdims=True), squares_ref.shape
        )

    @pl.when(tile < tiles_per_half)
    def _():
        accumulate(mine_refs)

    @pl.when(tile >= tiles_per_half)
    def _():
        accumulate(other_refs)


def grouped_out_proj(
    span_index, att_blocks, mine_blocks, other_blocks, hidden, scale, tile_width=512
):
    group_count = len(att_blocks)
    token_count, head_width = att_blocks[0].shape
    half_width = mine_blocks[0].shape[1]
    span_rows = scale.shape[0]
    tile_width = min(tile_width, half_width)
    tiles_per_half = half_width // tile_width
    att_spec = pl.BlockSpec((token_count, head_width), lambda n, s: (0, 0))
    mine_spec = pl.BlockSpec(
        (head_width, tile_width), lambda n, s: (0, jnp.minimum(n, tiles_per_half - 1))
    )
    other_spec = pl.BlockSpec(
        (head_width, tile_width), lambda n, s: (0, jnp.maximum(n - tiles_per_half, 0))
    )

    def column(n, s):
        return ((n // tiles_per_half + s[0]) % 2) * tiles_per_half + n % tiles_per_half

    out_spec = pl.BlockSpec((token_count, tile_width), lambda n, s: (0, column(n, s)))
    hidden_spec = pl.BlockSpec((token_count, tile_width), lambda n, s: (0, column(n, s)))
    scale_spec = pl.BlockSpec((span_rows, tile_width), lambda n, s: (0, column(n, s)))
    squares_spec = pl.BlockSpec((token_count, 128), lambda n, s: (0, n))
    tile_count = 2 * tiles_per_half
    flops = 2 * token_count * head_width * group_count * half_width * 2
    moved = 2 * (group_count * token_count * head_width + 2 * group_count * head_width * half_width)
    moved += token_count * 2 * half_width * (4 + 2)
    residual, squares = pl.pallas_call(
        functools.partial(out_proj_kernel, group_count, tiles_per_half, token_count // span_rows),
        out_shape=(
            jax.ShapeDtypeStruct((token_count, 2 * half_width), jnp.float32),
            jax.ShapeDtypeStruct((token_count, tile_count * 128), jnp.float32),
        ),
        grid_spec=pltpu.PrefetchScalarGridSpec(
            num_scalar_prefetch=1,
            grid=(tile_count,),
            in_specs=[att_spec] * group_count + [mine_spec] * group_count + [other_spec] * group_count
            + [hidden_spec, scale_spec],
            out_specs=[out_spec, squares_spec],
        ),
        cost_estimate=pl.CostEstimate(flops=flops, bytes_accessed=moved, transcendentals=0),
    )(
        jnp.reshape(span_index, (1,)).astype(jnp.int32),
        *att_blocks,
        *mine_blocks,
        *other_blocks,
        hidden,
        scale,
    )
    return residual, squares.reshape(token_count, tile_count, 128)[:, :, 0].sum(axis=1)


def select_row(source, target):
    matches = jnp.arange(source.shape[0], dtype=jnp.int32) == target
    return jnp.sum(jnp.where(matches.reshape((-1,) + (1,) * (source.ndim - 1)), source, 0), axis=0)


def attend(queries, cache_all, fresh_all, cache_seen, fresh_seen):
    row_count, head_count, head_size = queries.shape
    cache_keys = cache_all[:, :, 0].reshape(-1, head_count, head_size)
    cache_vals = cache_all[:, :, 1].reshape(-1, head_count, head_size)
    fresh_keys = fresh_all[:, :, 0].reshape(-1, head_count, head_size)
    fresh_vals = fresh_all[:, :, 1].reshape(-1, head_count, head_size)
    score_scale = 1.0 / math.sqrt(head_size)
    cache_scores = (
        jnp.einsum("qhd,khd->hqk", queries, cache_keys, preferred_element_type=jnp.float32)
        * score_scale
    )
    fresh_scores = (
        jnp.einsum("qhd,khd->hqk", queries, fresh_keys, preferred_element_type=jnp.float32)
        * score_scale
    )
    cache_scores = jnp.where(cache_seen[None, None, :], cache_scores, NEGATIVE)
    fresh_scores = jnp.where(fresh_seen[None, None, :], fresh_scores, NEGATIVE)
    scores = jnp.concatenate([cache_scores, fresh_scores], axis=2)
    row_max = jnp.max(scores, axis=2, keepdims=True)
    exp_terms = jnp.exp(scores - row_max)
    weights = (exp_terms / jnp.sum(exp_terms, axis=2, keepdims=True)).astype(jnp.bfloat16)
    split_at = cache_keys.shape[0]
    attended = jnp.einsum(
        "hqk,khd->qhd", weights[:, :, :split_at], cache_vals, preferred_element_type=jnp.float32
    )
    attended = attended + jnp.einsum(
        "hqk,khd->qhd", weights[:, :, split_at:], fresh_vals, preferred_element_type=jnp.float32
    )
    return attended.astype(jnp.bfloat16).reshape(row_count, head_count * head_size)


def local(
    hidden_in, levels, order, cache_mask, finished, cache_kv, modulation, w_qkv, w_out, w_up, w_down
):
    span_index = lax.axis_index("span")
    tp_rank = lax.axis_index("tp")
    span_count = lax.psum(1, "span")
    tp_count = lax.psum(1, "tp")
    model_width = modulation.shape[2]
    share_width = hidden_in.shape[2]
    local_count = hidden_in.shape[0]
    row_count = hidden_in.shape[1]
    token_count = local_count * row_count
    gather_weights = (
        tp_count * w_out.size * w_out.dtype.itemsize <= WEIGHT_GATHER_BYTES and span_count == 2
    )
    if gather_weights:
        cycle = snake_cycle(tp_count)
        position = jnp.array([cycle.index(t) for t in range(tp_count)], jnp.int32)[tp_rank]
        steps = list(range(tp_count // 2 + 1)) + [-k for k in range(1, (tp_count - 1) // 2 + 1)]
        owners = jnp.array(cycle, jnp.int32)
        gathered = jnp.zeros(hidden_in.shape[:2] + (model_width,), hidden_in.dtype)
        for step, piece in zip(steps, ring_gather(hidden_in, "tp", tp_count)):
            owner = owners[(position - step + tp_count) % tp_count]
            gathered = lax.dynamic_update_slice_in_dim(gathered, piece, owner * share_width, 2)
        gathered_narrow = gathered
        gathered = gathered.astype(jnp.float32)
    else:
        gathered = lax.all_gather(hidden_in, "tp", axis=2, tiled=True).astype(jnp.float32)
    if gather_weights:
        column_part = model_width // span_count
        w_out_part = lax.dynamic_slice_in_dim(w_out, span_index * column_part, column_part, 1)
        mine_blocks = ring_gather(w_out_part, "tp", tp_count)
        other_blocks = [lax.ppermute(b, "span", [(0, 1), (1, 0)]) for b in mine_blocks]
    up_full, down_full = (
        lax.all_gather(w_up, "span", axis=1, tiled=True),
        lax.all_gather(w_down, "span", axis=0, tiled=True),
    )
    mod_table = modulation.reshape(modulation.shape[0], -1)
    picker = (jnp.arange(mod_table.shape[0], dtype=jnp.int32)[None, :] == levels[:, None]).astype(
        jnp.bfloat16
    )
    mod_rows = jnp.dot(picker, mod_table, preferred_element_type=jnp.float32).reshape(
        local_count, 6, model_width
    )
    attn_in = (normalize(gathered) * mod_rows[:, 1][:, None] + mod_rows[:, 0][:, None]).astype(
        jnp.bfloat16
    )
    per_device = w_qkv.shape[2]
    projected = jnp.dot(
        attn_in.reshape(token_count, model_width),
        w_qkv.reshape(model_width, -1),
        preferred_element_type=jnp.float32,
    )
    projected = projected.astype(jnp.bfloat16).reshape(local_count, row_count, 3, per_device)
    queries = projected[:, :, 0].reshape(local_count, row_count, -1, HEAD_DIM)
    fresh_kv = projected[:, :, 1:]
    cache_all, fresh_all = (
        lax.all_gather(cache_kv, "span", axis=0, tiled=True),
        lax.all_gather(fresh_kv, "span", axis=0, tiled=True),
    )
    positions = jnp.arange(cache_mask.shape[0], dtype=jnp.int32)
    my_spans = span_index * local_count + jnp.arange(local_count, dtype=jnp.int32)
    mask_rows = jax.vmap(lambda target: select_row(cache_mask, target))(my_spans)
    my_order = jax.vmap(lambda target: select_row(order, target))(my_spans)
    cache_seen = jnp.repeat(
        (mask_rows == 1) | (positions[None, :] == finished[0]), row_count, axis=1
    )
    fresh_seen = jnp.repeat(order[None, :] <= my_order[:, None], row_count, axis=1)
    attended = jax.vmap(
        lambda q_rows, c_seen, f_seen: attend(q_rows, cache_all, fresh_all, c_seen, f_seen)
    )(queries, cache_seen, fresh_seen)
    if gather_weights:
        att_blocks = ring_gather(attended.reshape(token_count, per_device), "tp", tp_count)
        residual_rows, square_sums = grouped_out_proj(
            span_index,
            att_blocks,
            mine_blocks,
            other_blocks,
            gathered_narrow.reshape(token_count, model_width),
            mod_rows[:, 2],
        )
        residual_full = residual_rows.reshape(local_count, row_count, model_width)
        inverse = lax.rsqrt(square_sums.reshape(local_count, row_count, 1) / model_width + EPSILON)
        mlp_in = (
            residual_full * inverse * mod_rows[:, 4][:, None] + mod_rows[:, 3][:, None]
        ).astype(jnp.bfloat16)
    else:
        partial_value = jnp.dot(
            attended.reshape(token_count, -1), w_out, preferred_element_type=jnp.float32
        ).reshape(local_count, row_count, model_width)
        attn_part = lax.psum_scatter(
            partial_value.astype(jnp.bfloat16), "tp", scatter_dimension=2, tiled=True
        ).astype(jnp.float32)
        mod_share = lax.dynamic_slice_in_dim(mod_rows, tp_rank * share_width, share_width, 2)
        residual = hidden_in.astype(jnp.float32) + mod_share[:, 2][:, None] * attn_part
        squares = lax.psum(jnp.sum(residual * residual, axis=2), "tp")
        scaled = residual * lax.rsqrt(squares / model_width + EPSILON)[:, :, None]
        mlp_part = (scaled * mod_share[:, 4][:, None] + mod_share[:, 3][:, None]).astype(
            jnp.bfloat16
        )
        mlp_in = lax.all_gather(mlp_part, "tp", axis=2, tiled=True)
    pre_act = jnp.dot(mlp_in, up_full, preferred_element_type=jnp.float32)
    hidden_units = jax.nn.gelu(pre_act).astype(jnp.bfloat16)
    down_terms = jnp.dot(hidden_units, down_full, preferred_element_type=jnp.float32)
    if gather_weights:
        mlp_out = ring_reduce_scatter(
            down_terms.reshape(token_count, model_width), "tp", tp_count
        ).reshape(local_count, row_count, share_width)
    else:
        mlp_out = lax.psum_scatter(
            down_terms.astype(jnp.bfloat16), "tp", scatter_dimension=2, tiled=True
        ).astype(jnp.float32)
    if gather_weights:
        residual = lax.dynamic_slice_in_dim(residual_full, tp_rank * share_width, share_width, 2)
        mod_share = lax.dynamic_slice_in_dim(mod_rows, tp_rank * share_width, share_width, 2)
    result = residual + mod_share[:, 5][:, None] * mlp_out
    return result.astype(jnp.bfloat16)


def solution(mesh):
    placed = (
        P(("rep", "span"), None, "tp"),
        P(("rep", "span")),
        P("rep"),
        P("rep", None),
        P("rep"),
        P(("rep", "span"), None, None, "tp"),
        P(),
        P(None, None, "tp"),
        P("tp", None),
        P(None, ("span", "tp")),
        P(("span", "tp"), None),
    )
    return jax.shard_map(
        local, mesh=mesh, in_specs=placed, out_specs=P(("rep", "span"), None, "tp"), check_vma=False
    )
```

```python
import functools
import math

import jax
import jax.numpy as jnp
from jax import lax
from jax.experimental import pallas as pl
from jax.experimental.pallas import tpu as pltpu
from jax.sharding import PartitionSpec as P

HEAD_DIM = 128


EPSILON = 1e-06
NEGATIVE = -1e30
WEIGHT_GATHER_BYTES = 24 * 2**20


def normalize(values):
    return values * lax.rsqrt(jnp.mean(values * values, axis=-1, keepdims=True) + EPSILON)


def snake_cycle(count):
    return list(range(0, count, 2)) + list(range(count - 1, 0, -2)) if count % 2 == 0 else list(range(count))


def ring_gather(block, axis_name, count, reverse=False):
    cycle = snake_cycle(count)[::-1] if reverse else snake_cycle(count)
    ahead = [(cycle[p], cycle[(p + 1) % count]) for p in range(count)]
    behind = [(cycle[p], cycle[(p - 1) % count]) for p in range(count)]
    blocks = [block]
    forward = block
    for _ in range(count // 2):
        forward = lax.ppermute(forward, axis_name, ahead)
        blocks.append(forward)
    backward = block
    for _ in range((count - 1) // 2):
        backward = lax.ppermute(backward, axis_name, behind)
        blocks.append(backward)
    return blocks


def ring_reduce_scatter(terms, axis_name, count):
    token_count, width = terms.shape
    block = width // count
    half = block // 2
    cycle = snake_cycle(count)
    position = jnp.array([cycle.index(t) for t in range(count)], jnp.int32)[lax.axis_index(axis_name)]
    owners = jnp.array(cycle, jnp.int32)
    rounded = terms.astype(jnp.bfloat16)

    def own_part(slot, side):
        start = owners[slot % count] * block + side * half
        return lax.dynamic_slice_in_dim(rounded, start, half, 1).astype(jnp.float32)

    ahead = [(cycle[p], cycle[(p + 1) % count]) for p in range(count)]
    behind = [(cycle[p], cycle[(p - 1) % count]) for p in range(count)]
    forward = own_part(position - 1 + count, 0)
    backward = own_part(position + 1, 1)
    for step in range(count - 1):
        forward = lax.ppermute(forward.astype(jnp.bfloat16), axis_name, ahead).astype(jnp.float32)
        forward = forward + own_part(position - 2 - step + 2 * count, 0)
        backward = lax.ppermute(backward.astype(jnp.bfloat16), axis_name, behind).astype(jnp.float32)
        backward = backward + own_part(position + 2 + step, 1)
    return jnp.concatenate([forward, backward], axis=1)


def out_proj_kernel(group_count, tiles_per_half, row_count, span_ref, *refs):
    att_refs = refs[:group_count]
    mine_refs = refs[group_count:2 * group_count]
    other_refs = refs[2 * group_count:3 * group_count]
    hidden_ref, scale_ref, out_ref, squares_ref = refs[3 * group_count:]
    tile = pl.program_id(0)

    def accumulate(w_refs):
        total = None
        for group in range(group_count):
            term = jnp.dot(att_refs[group][...], w_refs[group][...], preferred_element_type=jnp.float32)
            term = term.astype(jnp.bfloat16).astype(jnp.float32)
            total = term if total is None else total + term
        for span in range(scale_ref.shape[0]):
            rows = slice(span * row_count, (span + 1) * row_count)
            out_ref[rows, :] = (
                hidden_ref[rows, :].astype(jnp.float32) + scale_ref[span:span + 1, :] * total[rows, :]
            )
        result = out_ref[...]
        squares_ref[...] = jnp.broadcast_to(
            jnp.sum(result * result, axis=1, keepdims=True), squares_ref.shape
        )

    @pl.when(tile < tiles_per_half)
    def _():
        accumulate(mine_refs)

    @pl.when(tile >= tiles_per_half)
    def _():
        accumulate(other_refs)


def grouped_out_proj(
    span_index, att_blocks, mine_blocks, other_blocks, hidden, scale, tile_width=512
):
    group_count = len(att_blocks)
    token_count, head_width = att_blocks[0].shape
    half_width = mine_blocks[0].shape[1]
    span_rows = scale.shape[0]
    tile_width = min(tile_width, half_width)
    tiles_per_half = half_width // tile_width
    att_spec = pl.BlockSpec((token_count, head_width), lambda n, s: (0, 0))
    mine_spec = pl.BlockSpec(
        (head_width, tile_width), lambda n, s: (0, jnp.minimum(n, tiles_per_half - 1))
    )
    other_spec = pl.BlockSpec(
        (head_width, tile_width), lambda n, s: (0, jnp.maximum(n - tiles_per_half, 0))
    )

    def column(n, s):
        return ((n // tiles_per_half + s[0]) % 2) * tiles_per_half + n % tiles_per_half

    out_spec = pl.BlockSpec((token_count, tile_width), lambda n, s: (0, column(n, s)))
    hidden_spec = pl.BlockSpec((token_count, tile_width), lambda n, s: (0, column(n, s)))
    scale_spec = pl.BlockSpec((span_rows, tile_width), lambda n, s: (0, column(n, s)))
    squares_spec = pl.BlockSpec((token_count, 128), lambda n, s: (0, n))
    tile_count = 2 * tiles_per_half
    flops = 2 * token_count * head_width * group_count * half_width * 2
    moved = 2 * (group_count * token_count * head_width + 2 * group_count * head_width * half_width)
    moved += token_count * 2 * half_width * (4 + 2)
    residual, squares = pl.pallas_call(
        functools.partial(out_proj_kernel, group_count, tiles_per_half, token_count // span_rows),
        out_shape=(
            jax.ShapeDtypeStruct((token_count, 2 * half_width), jnp.float32),
            jax.ShapeDtypeStruct((token_count, tile_count * 128), jnp.float32),
        ),
        grid_spec=pltpu.PrefetchScalarGridSpec(
            num_scalar_prefetch=1,
            grid=(tile_count,),
            in_specs=[att_spec] * group_count + [mine_spec] * group_count + [other_spec] * group_count
            + [hidden_spec, scale_spec],
            out_specs=[out_spec, squares_spec],
        ),
        cost_estimate=pl.CostEstimate(flops=flops, bytes_accessed=moved, transcendentals=0),
    )(
        jnp.reshape(span_index, (1,)).astype(jnp.int32),
        *att_blocks,
        *mine_blocks,
        *other_blocks,
        hidden,
        scale,
    )
    return residual, squares.reshape(token_count, tile_count, 128)[:, :, 0].sum(axis=1)


def select_row(source, target):
    matches = jnp.arange(source.shape[0], dtype=jnp.int32) == target
    return jnp.sum(jnp.where(matches.reshape((-1,) + (1,) * (source.ndim - 1)), source, 0), axis=0)


def attend(queries, cache_all, fresh_all, cache_seen, fresh_seen):
    row_count, head_count, head_size = queries.shape
    cache_keys = cache_all[:, :, 0].reshape(-1, head_count, head_size)
    cache_vals = cache_all[:, :, 1].reshape(-1, head_count, head_size)
    fresh_keys = fresh_all[:, :, 0].reshape(-1, head_count, head_size)
    fresh_vals = fresh_all[:, :, 1].reshape(-1, head_count, head_size)
    score_scale = 1.0 / math.sqrt(head_size)
    cache_scores = (
        jnp.einsum("qhd,khd->hqk", queries, cache_keys, preferred_element_type=jnp.float32)
        * score_scale
    )
    fresh_scores = (
        jnp.einsum("qhd,khd->hqk", queries, fresh_keys, preferred_element_type=jnp.float32)
        * score_scale
    )
    cache_scores = jnp.where(cache_seen[None, None, :], cache_scores, NEGATIVE)
    fresh_scores = jnp.where(fresh_seen[None, None, :], fresh_scores, NEGATIVE)
    scores = jnp.concatenate([cache_scores, fresh_scores], axis=2)
    row_max = jnp.max(scores, axis=2, keepdims=True)
    exp_terms = jnp.exp(scores - row_max)
    weights = (exp_terms / jnp.sum(exp_terms, axis=2, keepdims=True)).astype(jnp.bfloat16)
    split_at = cache_keys.shape[0]
    attended = jnp.einsum(
        "hqk,khd->qhd", weights[:, :, :split_at], cache_vals, preferred_element_type=jnp.float32
    )
    attended = attended + jnp.einsum(
        "hqk,khd->qhd", weights[:, :, split_at:], fresh_vals, preferred_element_type=jnp.float32
    )
    return attended.astype(jnp.bfloat16).reshape(row_count, head_count * head_size)


def local(
    hidden_in, levels, order, cache_mask, finished, cache_kv, modulation, w_qkv, w_out, w_up, w_down
):
    span_index = lax.axis_index("span")
    tp_rank = lax.axis_index("tp")
    span_count = lax.psum(1, "span")
    tp_count = lax.psum(1, "tp")
    model_width = modulation.shape[2]
    share_width = hidden_in.shape[2]
    local_count = hidden_in.shape[0]
    row_count = hidden_in.shape[1]
    token_count = local_count * row_count
    gather_weights = (
        tp_count * w_out.size * w_out.dtype.itemsize <= WEIGHT_GATHER_BYTES and span_count == 2
    )
    if gather_weights:
        cycle = snake_cycle(tp_count)
        position = jnp.array([cycle.index(t) for t in range(tp_count)], jnp.int32)[tp_rank]
        steps = list(range(tp_count // 2 + 1)) + [-k for k in range(1, (tp_count - 1) // 2 + 1)]
        owners = jnp.array(cycle, jnp.int32)
        gathered = jnp.zeros(hidden_in.shape[:2] + (model_width,), hidden_in.dtype)
        for step, piece in zip(steps, ring_gather(hidden_in, "tp", tp_count)):
            owner = owners[(position - step + tp_count) % tp_count]
            gathered = lax.dynamic_update_slice_in_dim(gathered, piece, owner * share_width, 2)
        gathered_narrow = gathered
        gathered = gathered.astype(jnp.float32)
    else:
        gathered = lax.all_gather(hidden_in, "tp", axis=2, tiled=True).astype(jnp.float32)
    if gather_weights:
        column_part = model_width // span_count
        w_out_part = lax.dynamic_slice_in_dim(w_out, span_index * column_part, column_part, 1)
        mine_blocks = ring_gather(w_out_part, "tp", tp_count, reverse=True)
        other_blocks = [lax.ppermute(b, "span", [(0, 1), (1, 0)]) for b in mine_blocks]
    up_full, down_full = (
        lax.all_gather(w_up, "span", axis=1, tiled=True),
        lax.all_gather(w_down, "span", axis=0, tiled=True),
    )
    mod_table = modulation.reshape(modulation.shape[0], -1)
    picker = (jnp.arange(mod_table.shape[0], dtype=jnp.int32)[None, :] == levels[:, None]).astype(
        jnp.bfloat16
    )
    mod_rows = jnp.dot(picker, mod_table, preferred_element_type=jnp.float32).reshape(
        local_count, 6, model_width
    )
    attn_in = (normalize(gathered) * mod_rows[:, 1][:, None] + mod_rows[:, 0][:, None]).astype(
        jnp.bfloat16
    )
    per_device = w_qkv.shape[2]
    projected = jnp.dot(
        attn_in.reshape(token_count, model_width),
        w_qkv.reshape(model_width, -1),
        preferred_element_type=jnp.float32,
    )
    projected = projected.astype(jnp.bfloat16).reshape(local_count, row_count, 3, per_device)
    queries = projected[:, :, 0].reshape(local_count, row_count, -1, HEAD_DIM)
    fresh_kv = projected[:, :, 1:]
    cache_all, fresh_all = (
        lax.all_gather(cache_kv, "span", axis=0, tiled=True),
        lax.all_gather(fresh_kv, "span", axis=0, tiled=True),
    )
    positions = jnp.arange(cache_mask.shape[0], dtype=jnp.int32)
    my_spans = span_index * local_count + jnp.arange(local_count, dtype=jnp.int32)
    mask_rows = jax.vmap(lambda target: select_row(cache_mask, target))(my_spans)
    my_order = jax.vmap(lambda target: select_row(order, target))(my_spans)
    cache_seen = jnp.repeat(
        (mask_rows == 1) | (positions[None, :] == finished[0]), row_count, axis=1
    )
    fresh_seen = jnp.repeat(order[None, :] <= my_order[:, None], row_count, axis=1)
    attended = jax.vmap(
        lambda q_rows, c_seen, f_seen: attend(q_rows, cache_all, fresh_all, c_seen, f_seen)
    )(queries, cache_seen, fresh_seen)
    if gather_weights:
        att_blocks = ring_gather(
            attended.reshape(token_count, per_device), "tp", tp_count, reverse=True
        )
        residual_rows, square_sums = grouped_out_proj(
            span_index,
            att_blocks,
            mine_blocks,
            other_blocks,
            gathered_narrow.reshape(token_count, model_width),
            mod_rows[:, 2],
        )
        residual_full = residual_rows.reshape(local_count, row_count, model_width)
        inverse = lax.rsqrt(square_sums.reshape(local_count, row_count, 1) / model_width + EPSILON)
        mlp_in = (
            residual_full * inverse * mod_rows[:, 4][:, None] + mod_rows[:, 3][:, None]
        ).astype(jnp.bfloat16)
    else:
        partial_value = jnp.dot(
            attended.reshape(token_count, -1), w_out, preferred_element_type=jnp.float32
        ).reshape(local_count, row_count, model_width)
        attn_part = lax.psum_scatter(
            partial_value.astype(jnp.bfloat16), "tp", scatter_dimension=2, tiled=True
        ).astype(jnp.float32)
        mod_share = lax.dynamic_slice_in_dim(mod_rows, tp_rank * share_width, share_width, 2)
        residual = hidden_in.astype(jnp.float32) + mod_share[:, 2][:, None] * attn_part
        squares = lax.psum(jnp.sum(residual * residual, axis=2), "tp")
        scaled = residual * lax.rsqrt(squares / model_width + EPSILON)[:, :, None]
        mlp_part = (scaled * mod_share[:, 4][:, None] + mod_share[:, 3][:, None]).astype(
            jnp.bfloat16
        )
        mlp_in = lax.all_gather(mlp_part, "tp", axis=2, tiled=True)
    pre_act = jnp.dot(mlp_in, up_full, preferred_element_type=jnp.float32)
    hidden_units = jax.nn.gelu(pre_act).astype(jnp.bfloat16)
    down_terms = jnp.dot(hidden_units, down_full, preferred_element_type=jnp.float32)
    if gather_weights:
        mlp_out = ring_reduce_scatter(
            down_terms.reshape(token_count, model_width), "tp", tp_count
        ).reshape(local_count, row_count, share_width)
    else:
        mlp_out = lax.psum_scatter(
            down_terms.astype(jnp.bfloat16), "tp", scatter_dimension=2, tiled=True
        ).astype(jnp.float32)
    if gather_weights:
        residual = lax.dynamic_slice_in_dim(residual_full, tp_rank * share_width, share_width, 2)
        mod_share = lax.dynamic_slice_in_dim(mod_rows, tp_rank * share_width, share_width, 2)
    result = residual + mod_share[:, 5][:, None] * mlp_out
    return result.astype(jnp.bfloat16)


def solution(mesh):
    placed = (
        P(("rep", "span"), None, "tp"),
        P(("rep", "span")),
        P("rep"),
        P("rep", None),
        P("rep"),
        P(("rep", "span"), None, None, "tp"),
        P(),
        P(None, None, "tp"),
        P("tp", None),
        P(None, ("span", "tp")),
        P(("span", "tp"), None),
    )
    return jax.shard_map(
        local, mesh=mesh, in_specs=placed, out_specs=P(("rep", "span"), None, "tp"), check_vma=False
    )
```

```python
import functools
import math

import jax
import jax.numpy as jnp
from jax import lax
from jax.experimental import pallas as pl
from jax.experimental.pallas import tpu as pltpu
from jax.sharding import PartitionSpec as P

HEAD_DIM = 128


EPSILON = 1e-06
NEGATIVE = -1e30
WEIGHT_GATHER_BYTES = 24 * 2**20


def normalize(values):
    return values * lax.rsqrt(jnp.mean(values * values, axis=-1, keepdims=True) + EPSILON)


def snake_cycle(count):
    return list(range(0, count, 2)) + list(range(count - 1, 0, -2)) if count % 2 == 0 else list(range(count))


def ring_gather(block, axis_name, count):
    cycle = snake_cycle(count)
    ahead = [(cycle[p], cycle[(p + 1) % count]) for p in range(count)]
    behind = [(cycle[p], cycle[(p - 1) % count]) for p in range(count)]
    blocks = [block]
    forward = block
    for _ in range(count // 2):
        forward = lax.ppermute(forward, axis_name, ahead)
        blocks.append(forward)
    backward = block
    for _ in range((count - 1) // 2):
        backward = lax.ppermute(backward, axis_name, behind)
        blocks.append(backward)
    return blocks


def ring_reduce_scatter(terms, axis_name, count):
    token_count, width = terms.shape
    block = width // count
    half = block // 2
    cycle = snake_cycle(count)
    position = jnp.array([cycle.index(t) for t in range(count)], jnp.int32)[lax.axis_index(axis_name)]
    owners = jnp.array(cycle, jnp.int32)
    rounded = terms.astype(jnp.bfloat16)

    def own_part(slot, side):
        start = owners[slot % count] * block + side * half
        return lax.dynamic_slice_in_dim(rounded, start, half, 1).astype(jnp.float32)

    ahead = [(cycle[p], cycle[(p + 1) % count]) for p in range(count)]
    behind = [(cycle[p], cycle[(p - 1) % count]) for p in range(count)]
    forward = own_part(position - 1 + count, 0)
    backward = own_part(position + 1, 1)
    for step in range(count - 1):
        forward = lax.ppermute(forward.astype(jnp.bfloat16), axis_name, ahead).astype(jnp.float32)
        forward = forward + own_part(position - 2 - step + 2 * count, 0)
        backward = lax.ppermute(backward.astype(jnp.bfloat16), axis_name, behind).astype(jnp.float32)
        backward = backward + own_part(position + 2 + step, 1)
    return jnp.concatenate([forward, backward], axis=1)


def out_proj_kernel(group_count, tiles_per_half, row_count, span_ref, *refs):
    att_refs = refs[:group_count]
    mine_refs = refs[group_count:2 * group_count]
    other_refs = refs[2 * group_count:3 * group_count]
    hidden_ref, scale_ref, out_ref, squares_ref = refs[3 * group_count:]
    tile = pl.program_id(0)

    def accumulate(w_refs):
        total = None
        for group in range(group_count):
            term = jnp.dot(att_refs[group][...], w_refs[group][...], preferred_element_type=jnp.float32)
            term = term.astype(jnp.bfloat16).astype(jnp.float32)
            total = term if total is None else total + term
        for span in range(scale_ref.shape[0]):
            rows = slice(span * row_count, (span + 1) * row_count)
            out_ref[rows, :] = (
                hidden_ref[rows, :].astype(jnp.float32) + scale_ref[span:span + 1, :] * total[rows, :]
            )
        result = out_ref[...]
        squares_ref[...] = jnp.broadcast_to(
            jnp.sum(result * result, axis=1, keepdims=True), squares_ref.shape
        )

    @pl.when(tile < tiles_per_half)
    def _():
        accumulate(mine_refs)

    @pl.when(tile >= tiles_per_half)
    def _():
        accumulate(other_refs)


def grouped_out_proj(
    span_index, att_blocks, mine_blocks, other_blocks, hidden, scale, tile_width=512
):
    group_count = len(att_blocks)
    token_count, head_width = att_blocks[0].shape
    half_width = mine_blocks[0].shape[1]
    span_rows = scale.shape[0]
    tile_width = min(tile_width, half_width)
    tiles_per_half = half_width // tile_width
    att_spec = pl.BlockSpec((token_count, head_width), lambda n, s: (0, 0))
    mine_spec = pl.BlockSpec(
        (head_width, tile_width), lambda n, s: (0, jnp.minimum(n, tiles_per_half - 1))
    )
    other_spec = pl.BlockSpec(
        (head_width, tile_width), lambda n, s: (0, jnp.maximum(n - tiles_per_half, 0))
    )

    def column(n, s):
        return ((n // tiles_per_half + s[0]) % 2) * tiles_per_half + n % tiles_per_half

    out_spec = pl.BlockSpec((token_count, tile_width), lambda n, s: (0, column(n, s)))
    hidden_spec = pl.BlockSpec((token_count, tile_width), lambda n, s: (0, column(n, s)))
    scale_spec = pl.BlockSpec((span_rows, tile_width), lambda n, s: (0, column(n, s)))
    squares_spec = pl.BlockSpec((token_count, 128), lambda n, s: (0, n))
    tile_count = 2 * tiles_per_half
    flops = 2 * token_count * head_width * group_count * half_width * 2
    moved = 2 * (group_count * token_count * head_width + 2 * group_count * head_width * half_width)
    moved += token_count * 2 * half_width * (4 + 2)
    residual, squares = pl.pallas_call(
        functools.partial(out_proj_kernel, group_count, tiles_per_half, token_count // span_rows),
        out_shape=(
            jax.ShapeDtypeStruct((token_count, 2 * half_width), jnp.float32),
            jax.ShapeDtypeStruct((token_count, tile_count * 128), jnp.float32),
        ),
        grid_spec=pltpu.PrefetchScalarGridSpec(
            num_scalar_prefetch=1,
            grid=(tile_count,),
            in_specs=[att_spec] * group_count + [mine_spec] * group_count + [other_spec] * group_count
            + [hidden_spec, scale_spec],
            out_specs=[out_spec, squares_spec],
        ),
        cost_estimate=pl.CostEstimate(flops=flops, bytes_accessed=moved, transcendentals=0),
    )(
        jnp.reshape(span_index, (1,)).astype(jnp.int32),
        *att_blocks,
        *mine_blocks,
        *other_blocks,
        hidden,
        scale,
    )
    return residual, squares.reshape(token_count, tile_count, 128)[:, :, 0].sum(axis=1)


def select_row(source, target):
    matches = jnp.arange(source.shape[0], dtype=jnp.int32) == target
    return jnp.sum(jnp.where(matches.reshape((-1,) + (1,) * (source.ndim - 1)), source, 0), axis=0)


def attend(queries, cache_all, fresh_all, cache_seen, fresh_seen):
    row_count, head_count, head_size = queries.shape
    cache_keys = cache_all[:, :, 0].reshape(-1, head_count, head_size)
    cache_vals = cache_all[:, :, 1].reshape(-1, head_count, head_size)
    fresh_keys = fresh_all[:, :, 0].reshape(-1, head_count, head_size)
    fresh_vals = fresh_all[:, :, 1].reshape(-1, head_count, head_size)
    score_scale = 1.0 / math.sqrt(head_size)
    cache_scores = (
        jnp.einsum("qhd,khd->hqk", queries, cache_keys, preferred_element_type=jnp.float32)
        * score_scale
    )
    fresh_scores = (
        jnp.einsum("qhd,khd->hqk", queries, fresh_keys, preferred_element_type=jnp.float32)
        * score_scale
    )
    cache_scores = jnp.where(cache_seen[None, None, :], cache_scores, NEGATIVE)
    fresh_scores = jnp.where(fresh_seen[None, None, :], fresh_scores, NEGATIVE)
    scores = jnp.concatenate([cache_scores, fresh_scores], axis=2)
    row_max = jnp.max(scores, axis=2, keepdims=True)
    exp_terms = jnp.exp(scores - row_max)
    weights = (exp_terms / jnp.sum(exp_terms, axis=2, keepdims=True)).astype(jnp.bfloat16)
    split_at = cache_keys.shape[0]
    attended = jnp.einsum(
        "hqk,khd->qhd", weights[:, :, :split_at], cache_vals, preferred_element_type=jnp.float32
    )
    attended = attended + jnp.einsum(
        "hqk,khd->qhd", weights[:, :, split_at:], fresh_vals, preferred_element_type=jnp.float32
    )
    return attended.astype(jnp.bfloat16).reshape(row_count, head_count * head_size)


def local(
    hidden_in, levels, order, cache_mask, finished, cache_kv, modulation, w_qkv, w_out, w_up, w_down
):
    span_index = lax.axis_index("span")
    tp_rank = lax.axis_index("tp")
    span_count = lax.psum(1, "span")
    tp_count = lax.psum(1, "tp")
    model_width = modulation.shape[2]
    share_width = hidden_in.shape[2]
    local_count = hidden_in.shape[0]
    row_count = hidden_in.shape[1]
    token_count = local_count * row_count
    gather_weights = (
        tp_count * w_out.size * w_out.dtype.itemsize <= WEIGHT_GATHER_BYTES and span_count == 2
    )
    if gather_weights:
        cycle = snake_cycle(tp_count)
        position = jnp.array([cycle.index(t) for t in range(tp_count)], jnp.int32)[tp_rank]
        steps = list(range(tp_count // 2 + 1)) + [-k for k in range(1, (tp_count - 1) // 2 + 1)]
        owners = jnp.array(cycle, jnp.int32)
        gathered = jnp.zeros(hidden_in.shape[:2] + (model_width,), hidden_in.dtype)
        for step, piece in zip(steps, ring_gather(hidden_in, "tp", tp_count)):
            owner = owners[(position - step + tp_count) % tp_count]
            gathered = lax.dynamic_update_slice_in_dim(gathered, piece, owner * share_width, 2)
        gathered_narrow = gathered
    else:
        gathered = lax.all_gather(hidden_in, "tp", axis=2, tiled=True).astype(jnp.float32)
    if gather_weights:
        column_part = model_width // span_count
        w_out_part = lax.dynamic_slice_in_dim(w_out, span_index * column_part, column_part, 1)
        gathered_narrow, w_out_part = lax.optimization_barrier((gathered_narrow, w_out_part))
        mine_blocks = ring_gather(w_out_part, "tp", tp_count)
        other_blocks = [lax.ppermute(b, "span", [(0, 1), (1, 0)]) for b in mine_blocks]
    if gather_weights:
        gathered = gathered_narrow.astype(jnp.float32)
    up_full, down_full = (
        lax.all_gather(w_up, "span", axis=1, tiled=True),
        lax.all_gather(w_down, "span", axis=0, tiled=True),
    )
    mod_table = modulation.reshape(modulation.shape[0], -1)
    picker = (jnp.arange(mod_table.shape[0], dtype=jnp.int32)[None, :] == levels[:, None]).astype(
        jnp.bfloat16
    )
    mod_rows = jnp.dot(picker, mod_table, preferred_element_type=jnp.float32).reshape(
        local_count, 6, model_width
    )
    attn_in = (normalize(gathered) * mod_rows[:, 1][:, None] + mod_rows[:, 0][:, None]).astype(
        jnp.bfloat16
    )
    per_device = w_qkv.shape[2]
    projected = jnp.dot(
        attn_in.reshape(token_count, model_width),
        w_qkv.reshape(model_width, -1),
        preferred_element_type=jnp.float32,
    )
    projected = projected.astype(jnp.bfloat16).reshape(local_count, row_count, 3, per_device)
    queries = projected[:, :, 0].reshape(local_count, row_count, -1, HEAD_DIM)
    fresh_kv = projected[:, :, 1:]
    cache_all, fresh_all = (
        lax.all_gather(cache_kv, "span", axis=0, tiled=True),
        lax.all_gather(fresh_kv, "span", axis=0, tiled=True),
    )
    positions = jnp.arange(cache_mask.shape[0], dtype=jnp.int32)
    my_spans = span_index * local_count + jnp.arange(local_count, dtype=jnp.int32)
    mask_rows = jax.vmap(lambda target: select_row(cache_mask, target))(my_spans)
    my_order = jax.vmap(lambda target: select_row(order, target))(my_spans)
    cache_seen = jnp.repeat(
        (mask_rows == 1) | (positions[None, :] == finished[0]), row_count, axis=1
    )
    fresh_seen = jnp.repeat(order[None, :] <= my_order[:, None], row_count, axis=1)
    attended = jax.vmap(
        lambda q_rows, c_seen, f_seen: attend(q_rows, cache_all, fresh_all, c_seen, f_seen)
    )(queries, cache_seen, fresh_seen)
    if gather_weights:
        att_blocks = ring_gather(attended.reshape(token_count, per_device), "tp", tp_count)
        residual_rows, square_sums = grouped_out_proj(
            span_index,
            att_blocks,
            mine_blocks,
            other_blocks,
            gathered_narrow.reshape(token_count, model_width),
            mod_rows[:, 2],
        )
        residual_full = residual_rows.reshape(local_count, row_count, model_width)
        inverse = lax.rsqrt(square_sums.reshape(local_count, row_count, 1) / model_width + EPSILON)
        mlp_in = (
            residual_full * inverse * mod_rows[:, 4][:, None] + mod_rows[:, 3][:, None]
        ).astype(jnp.bfloat16)
    else:
        partial_value = jnp.dot(
            attended.reshape(token_count, -1), w_out, preferred_element_type=jnp.float32
        ).reshape(local_count, row_count, model_width)
        attn_part = lax.psum_scatter(
            partial_value.astype(jnp.bfloat16), "tp", scatter_dimension=2, tiled=True
        ).astype(jnp.float32)
        mod_share = lax.dynamic_slice_in_dim(mod_rows, tp_rank * share_width, share_width, 2)
        residual = hidden_in.astype(jnp.float32) + mod_share[:, 2][:, None] * attn_part
        squares = lax.psum(jnp.sum(residual * residual, axis=2), "tp")
        scaled = residual * lax.rsqrt(squares / model_width + EPSILON)[:, :, None]
        mlp_part = (scaled * mod_share[:, 4][:, None] + mod_share[:, 3][:, None]).astype(
            jnp.bfloat16
        )
        mlp_in = lax.all_gather(mlp_part, "tp", axis=2, tiled=True)
    pre_act = jnp.dot(mlp_in, up_full, preferred_element_type=jnp.float32)
    hidden_units = jax.nn.gelu(pre_act).astype(jnp.bfloat16)
    down_terms = jnp.dot(hidden_units, down_full, preferred_element_type=jnp.float32)
    if gather_weights:
        mlp_out = ring_reduce_scatter(
            down_terms.reshape(token_count, model_width), "tp", tp_count
        ).reshape(local_count, row_count, share_width)
    else:
        mlp_out = lax.psum_scatter(
            down_terms.astype(jnp.bfloat16), "tp", scatter_dimension=2, tiled=True
        ).astype(jnp.float32)
    if gather_weights:
        residual = lax.dynamic_slice_in_dim(residual_full, tp_rank * share_width, share_width, 2)
        mod_share = lax.dynamic_slice_in_dim(mod_rows, tp_rank * share_width, share_width, 2)
    result = residual + mod_share[:, 5][:, None] * mlp_out
    return result.astype(jnp.bfloat16)


def solution(mesh):
    placed = (
        P(("rep", "span"), None, "tp"),
        P(("rep", "span")),
        P("rep"),
        P("rep", None),
        P("rep"),
        P(("rep", "span"), None, None, "tp"),
        P(),
        P(None, None, "tp"),
        P("tp", None),
        P(None, ("span", "tp")),
        P(("span", "tp"), None),
    )
    return jax.shard_map(
        local, mesh=mesh, in_specs=placed, out_specs=P(("rep", "span"), None, "tp"), check_vma=False
    )
```

```python
import functools
import math

import jax
import jax.numpy as jnp
from jax import lax
from jax.experimental import pallas as pl
from jax.experimental.pallas import tpu as pltpu
from jax.sharding import PartitionSpec as P

HEAD_DIM = 128


EPSILON = 1e-06
NEGATIVE = -1e30
WEIGHT_GATHER_BYTES = 24 * 2**20


def normalize(values):
    return values * lax.rsqrt(jnp.mean(values * values, axis=-1, keepdims=True) + EPSILON)


def snake_cycle(count):
    return list(range(0, count, 2)) + list(range(count - 1, 0, -2)) if count % 2 == 0 else list(range(count))


def ring_gather(block, axis_name, count):
    cycle = snake_cycle(count)
    ahead = [(cycle[p], cycle[(p + 1) % count]) for p in range(count)]
    behind = [(cycle[p], cycle[(p - 1) % count]) for p in range(count)]
    blocks = [block]
    forward = block
    for _ in range(count // 2):
        forward = lax.ppermute(forward, axis_name, ahead)
        blocks.append(forward)
    backward = block
    for _ in range((count - 1) // 2):
        backward = lax.ppermute(backward, axis_name, behind)
        blocks.append(backward)
    return blocks


def ring_reduce_scatter(terms, axis_name, count):
    token_count, width = terms.shape
    block = width // count
    half = block // 2
    cycle = snake_cycle(count)
    position = jnp.array([cycle.index(t) for t in range(count)], jnp.int32)[lax.axis_index(axis_name)]
    owners = jnp.array(cycle, jnp.int32)
    rounded = terms.astype(jnp.bfloat16)

    def own_part(slot, side):
        start = owners[slot % count] * block + side * half
        return lax.dynamic_slice_in_dim(rounded, start, half, 1).astype(jnp.float32)

    ahead = [(cycle[p], cycle[(p + 1) % count]) for p in range(count)]
    behind = [(cycle[p], cycle[(p - 1) % count]) for p in range(count)]
    forward = own_part(position - 1 + count, 0)
    backward = own_part(position + 1, 1)
    for step in range(count - 1):
        forward = lax.ppermute(forward.astype(jnp.bfloat16), axis_name, ahead).astype(jnp.float32)
        forward = forward + own_part(position - 2 - step + 2 * count, 0)
        backward = lax.ppermute(backward.astype(jnp.bfloat16), axis_name, behind).astype(jnp.float32)
        backward = backward + own_part(position + 2 + step, 1)
    return jnp.concatenate([forward, backward], axis=1)


def out_proj_kernel(group_count, tiles_per_half, row_count, span_ref, *refs):
    att_refs = refs[:group_count]
    mine_refs = refs[group_count:2 * group_count]
    other_refs = refs[2 * group_count:3 * group_count]
    hidden_ref, scale_ref, out_ref, squares_ref = refs[3 * group_count:]
    tile = pl.program_id(0)

    def accumulate(w_refs):
        total = None
        for group in range(group_count):
            term = jnp.dot(att_refs[group][...], w_refs[group][...], preferred_element_type=jnp.float32)
            term = term.astype(jnp.bfloat16).astype(jnp.float32)
            total = term if total is None else total + term
        for span in range(scale_ref.shape[0]):
            rows = slice(span * row_count, (span + 1) * row_count)
            out_ref[rows, :] = (
                hidden_ref[rows, :].astype(jnp.float32) + scale_ref[span:span + 1, :] * total[rows, :]
            )
        result = out_ref[...]
        squares_ref[...] = jnp.broadcast_to(
            jnp.sum(result * result, axis=1, keepdims=True), squares_ref.shape
        )

    @pl.when(tile < tiles_per_half)
    def _():
        accumulate(mine_refs)

    @pl.when(tile >= tiles_per_half)
    def _():
        accumulate(other_refs)


def grouped_out_proj(
    span_index, att_blocks, mine_blocks, other_blocks, hidden, scale, tile_width=512
):
    group_count = len(att_blocks)
    token_count, head_width = att_blocks[0].shape
    half_width = mine_blocks[0].shape[1]
    span_rows = scale.shape[0]
    tile_width = min(tile_width, half_width)
    tiles_per_half = half_width // tile_width
    att_spec = pl.BlockSpec((token_count, head_width), lambda n, s: (0, 0))
    mine_spec = pl.BlockSpec(
        (head_width, tile_width), lambda n, s: (0, jnp.minimum(n, tiles_per_half - 1))
    )
    other_spec = pl.BlockSpec(
        (head_width, tile_width), lambda n, s: (0, jnp.maximum(n - tiles_per_half, 0))
    )

    def column(n, s):
        return ((n // tiles_per_half + s[0]) % 2) * tiles_per_half + n % tiles_per_half

    out_spec = pl.BlockSpec((token_count, tile_width), lambda n, s: (0, column(n, s)))
    hidden_spec = pl.BlockSpec((token_count, tile_width), lambda n, s: (0, column(n, s)))
    scale_spec = pl.BlockSpec((span_rows, tile_width), lambda n, s: (0, column(n, s)))
    squares_spec = pl.BlockSpec((token_count, 128), lambda n, s: (0, n))
    tile_count = 2 * tiles_per_half
    flops = 2 * token_count * head_width * group_count * half_width * 2
    moved = 2 * (group_count * token_count * head_width + 2 * group_count * head_width * half_width)
    moved += token_count * 2 * half_width * (4 + 2)
    residual, squares = pl.pallas_call(
        functools.partial(out_proj_kernel, group_count, tiles_per_half, token_count // span_rows),
        out_shape=(
            jax.ShapeDtypeStruct((token_count, 2 * half_width), jnp.float32),
            jax.ShapeDtypeStruct((token_count, tile_count * 128), jnp.float32),
        ),
        grid_spec=pltpu.PrefetchScalarGridSpec(
            num_scalar_prefetch=1,
            grid=(tile_count,),
            in_specs=[att_spec] * group_count + [mine_spec] * group_count + [other_spec] * group_count
            + [hidden_spec, scale_spec],
            out_specs=[out_spec, squares_spec],
        ),
        cost_estimate=pl.CostEstimate(flops=flops, bytes_accessed=moved, transcendentals=0),
    )(
        jnp.reshape(span_index, (1,)).astype(jnp.int32),
        *att_blocks,
        *mine_blocks,
        *other_blocks,
        hidden,
        scale,
    )
    return residual, squares.reshape(token_count, tile_count, 128)[:, :, 0].sum(axis=1)


def select_row(source, target):
    matches = jnp.arange(source.shape[0], dtype=jnp.int32) == target
    return jnp.sum(jnp.where(matches.reshape((-1,) + (1,) * (source.ndim - 1)), source, 0), axis=0)


def attend(queries, cache_all, fresh_all, cache_seen, fresh_seen):
    row_count, head_count, head_size = queries.shape
    cache_keys = cache_all[:, :, 0].reshape(-1, head_count, head_size)
    cache_vals = cache_all[:, :, 1].reshape(-1, head_count, head_size)
    fresh_keys = fresh_all[:, :, 0].reshape(-1, head_count, head_size)
    fresh_vals = fresh_all[:, :, 1].reshape(-1, head_count, head_size)
    score_scale = 1.0 / math.sqrt(head_size)
    cache_scores = (
        jnp.einsum("qhd,khd->hqk", queries, cache_keys, preferred_element_type=jnp.float32)
        * score_scale
    )
    fresh_scores = (
        jnp.einsum("qhd,khd->hqk", queries, fresh_keys, preferred_element_type=jnp.float32)
        * score_scale
    )
    cache_scores = jnp.where(cache_seen[None, None, :], cache_scores, NEGATIVE)
    fresh_scores = jnp.where(fresh_seen[None, None, :], fresh_scores, NEGATIVE)
    scores = jnp.concatenate([cache_scores, fresh_scores], axis=2)
    row_max = jnp.max(scores, axis=2, keepdims=True)
    exp_terms = jnp.exp(scores - row_max)
    weights = (exp_terms / jnp.sum(exp_terms, axis=2, keepdims=True)).astype(jnp.bfloat16)
    split_at = cache_keys.shape[0]
    attended = jnp.einsum(
        "hqk,khd->qhd", weights[:, :, :split_at], cache_vals, preferred_element_type=jnp.float32
    )
    attended = attended + jnp.einsum(
        "hqk,khd->qhd", weights[:, :, split_at:], fresh_vals, preferred_element_type=jnp.float32
    )
    return attended.astype(jnp.bfloat16).reshape(row_count, head_count * head_size)


def local(
    hidden_in, levels, order, cache_mask, finished, cache_kv, modulation, w_qkv, w_out, w_up, w_down
):
    span_index = lax.axis_index("span")
    tp_rank = lax.axis_index("tp")
    span_count = lax.psum(1, "span")
    tp_count = lax.psum(1, "tp")
    model_width = modulation.shape[2]
    share_width = hidden_in.shape[2]
    local_count = hidden_in.shape[0]
    row_count = hidden_in.shape[1]
    token_count = local_count * row_count
    gather_weights = (
        tp_count * w_out.size * w_out.dtype.itemsize <= WEIGHT_GATHER_BYTES and span_count == 2
    )
    if gather_weights:
        cycle = snake_cycle(tp_count)
        position = jnp.array([cycle.index(t) for t in range(tp_count)], jnp.int32)[tp_rank]
        steps = list(range(tp_count // 2 + 1)) + [-k for k in range(1, (tp_count - 1) // 2 + 1)]
        owners = jnp.array(cycle, jnp.int32)
        gathered = jnp.zeros(hidden_in.shape[:2] + (model_width,), hidden_in.dtype)
        for step, piece in zip(steps, ring_gather(hidden_in, "tp", tp_count)):
            owner = owners[(position - step + tp_count) % tp_count]
            gathered = lax.dynamic_update_slice_in_dim(gathered, piece, owner * share_width, 2)
        gathered_narrow = gathered
        gathered = gathered.astype(jnp.float32)
    else:
        gathered = lax.all_gather(hidden_in, "tp", axis=2, tiled=True).astype(jnp.float32)
    if gather_weights:
        column_part = model_width // span_count
        w_out_part = lax.dynamic_slice_in_dim(w_out, span_index * column_part, column_part, 1)
        mine_blocks = ring_gather(w_out_part, "tp", tp_count)
        other_blocks = [lax.ppermute(b, "span", [(0, 1), (1, 0)]) for b in mine_blocks]
    up_full, down_full = (
        lax.all_gather(w_up, "span", axis=1, tiled=True),
        lax.all_gather(w_down, "span", axis=0, tiled=True),
    )
    mod_table = modulation.reshape(modulation.shape[0], -1)
    picker = (jnp.arange(mod_table.shape[0], dtype=jnp.int32)[None, :] == levels[:, None]).astype(
        jnp.bfloat16
    )
    mod_rows = jnp.dot(picker, mod_table, preferred_element_type=jnp.float32).reshape(
        local_count, 6, model_width
    )
    attn_in = (normalize(gathered) * mod_rows[:, 1][:, None] + mod_rows[:, 0][:, None]).astype(
        jnp.bfloat16
    )
    per_device = w_qkv.shape[2]
    projected = jnp.dot(
        attn_in.reshape(token_count, model_width),
        w_qkv.reshape(model_width, -1),
        preferred_element_type=jnp.float32,
    )
    projected = projected.astype(jnp.bfloat16).reshape(local_count, row_count, 3, per_device)
    queries = projected[:, :, 0].reshape(local_count, row_count, -1, HEAD_DIM)
    fresh_kv = projected[:, :, 1:]
    cache_all, fresh_all = (
        lax.all_gather(cache_kv, "span", axis=0, tiled=True),
        lax.all_gather(fresh_kv, "span", axis=0, tiled=True),
    )
    positions = jnp.arange(cache_mask.shape[0], dtype=jnp.int32)
    my_spans = span_index * local_count + jnp.arange(local_count, dtype=jnp.int32)
    mask_rows = jax.vmap(lambda target: select_row(cache_mask, target))(my_spans)
    my_order = jax.vmap(lambda target: select_row(order, target))(my_spans)
    cache_seen = jnp.repeat(
        (mask_rows == 1) | (positions[None, :] == finished[0]), row_count, axis=1
    )
    fresh_seen = jnp.repeat(order[None, :] <= my_order[:, None], row_count, axis=1)
    attended = jax.vmap(
        lambda q_rows, c_seen, f_seen: attend(q_rows, cache_all, fresh_all, c_seen, f_seen)
    )(queries, cache_seen, fresh_seen)
    if gather_weights:
        att_blocks = ring_gather(attended.reshape(token_count, per_device), "tp", tp_count)
        halves = 2 if local_count % 2 == 0 else 1
        per_half = local_count // halves
        half_tokens = per_half * row_count
        hidden_rows = gathered_narrow.reshape(token_count, model_width)
        outputs = []
        for half in range(halves):
            rows = slice(half * half_tokens, (half + 1) * half_tokens)
            mod_half = mod_rows[half * per_half:(half + 1) * per_half]
            residual_rows, square_sums = grouped_out_proj(
                span_index,
                [b[rows] for b in att_blocks],
                mine_blocks,
                other_blocks,
                hidden_rows[rows],
                mod_half[:, 2],
            )
            residual_full = residual_rows.reshape(per_half, row_count, model_width)
            inverse = lax.rsqrt(square_sums.reshape(per_half, row_count, 1) / model_width + EPSILON)
            mlp_in = (
                residual_full * inverse * mod_half[:, 4][:, None] + mod_half[:, 3][:, None]
            ).astype(jnp.bfloat16)
            pre_act = jnp.dot(mlp_in, up_full, preferred_element_type=jnp.float32)
            hidden_units = jax.nn.gelu(pre_act).astype(jnp.bfloat16)
            down_terms = jnp.dot(hidden_units, down_full, preferred_element_type=jnp.float32)
            mlp_out = ring_reduce_scatter(
                down_terms.reshape(half_tokens, model_width), "tp", tp_count
            ).reshape(per_half, row_count, share_width)
            residual = lax.dynamic_slice_in_dim(residual_full, tp_rank * share_width, share_width, 2)
            mod_share = lax.dynamic_slice_in_dim(mod_half, tp_rank * share_width, share_width, 2)
            outputs.append((residual + mod_share[:, 5][:, None] * mlp_out).astype(jnp.bfloat16))
        return jnp.concatenate(outputs, axis=0)
    else:
        partial_value = jnp.dot(
            attended.reshape(token_count, -1), w_out, preferred_element_type=jnp.float32
        ).reshape(local_count, row_count, model_width)
        attn_part = lax.psum_scatter(
            partial_value.astype(jnp.bfloat16), "tp", scatter_dimension=2, tiled=True
        ).astype(jnp.float32)
        mod_share = lax.dynamic_slice_in_dim(mod_rows, tp_rank * share_width, share_width, 2)
        residual = hidden_in.astype(jnp.float32) + mod_share[:, 2][:, None] * attn_part
        squares = lax.psum(jnp.sum(residual * residual, axis=2), "tp")
        scaled = residual * lax.rsqrt(squares / model_width + EPSILON)[:, :, None]
        mlp_part = (scaled * mod_share[:, 4][:, None] + mod_share[:, 3][:, None]).astype(
            jnp.bfloat16
        )
        mlp_in = lax.all_gather(mlp_part, "tp", axis=2, tiled=True)
    pre_act = jnp.dot(mlp_in, up_full, preferred_element_type=jnp.float32)
    hidden_units = jax.nn.gelu(pre_act).astype(jnp.bfloat16)
    down_terms = jnp.dot(hidden_units, down_full, preferred_element_type=jnp.float32)
    mlp_out = lax.psum_scatter(
        down_terms.astype(jnp.bfloat16), "tp", scatter_dimension=2, tiled=True
    ).astype(jnp.float32)
    result = residual + mod_share[:, 5][:, None] * mlp_out
    return result.astype(jnp.bfloat16)


def solution(mesh):
    placed = (
        P(("rep", "span"), None, "tp"),
        P(("rep", "span")),
        P("rep"),
        P("rep", None),
        P("rep"),
        P(("rep", "span"), None, None, "tp"),
        P(),
        P(None, None, "tp"),
        P("tp", None),
        P(None, ("span", "tp")),
        P(("span", "tp"), None),
    )
    return jax.shard_map(
        local, mesh=mesh, in_specs=placed, out_specs=P(("rep", "span"), None, "tp"), check_vma=False
    )
```

```python
import functools
import math

import jax
import jax.numpy as jnp
from jax import lax
from jax.experimental import pallas as pl
from jax.experimental.pallas import tpu as pltpu
from jax.sharding import PartitionSpec as P

HEAD_DIM = 128


EPSILON = 1e-06
NEGATIVE = -1e30
WEIGHT_GATHER_BYTES = 24 * 2**20


def normalize(values):
    return values * lax.rsqrt(jnp.mean(values * values, axis=-1, keepdims=True) + EPSILON)


def snake_cycle(count):
    return list(range(0, count, 2)) + list(range(count - 1, 0, -2)) if count % 2 == 0 else list(range(count))


def ring_gather(block, axis_name, count):
    cycle = snake_cycle(count)
    ahead = [(cycle[p], cycle[(p + 1) % count]) for p in range(count)]
    behind = [(cycle[p], cycle[(p - 1) % count]) for p in range(count)]
    blocks = [block]
    forward = block
    for _ in range(count // 2):
        forward = lax.ppermute(forward, axis_name, ahead)
        blocks.append(forward)
    backward = block
    for _ in range((count - 1) // 2):
        backward = lax.ppermute(backward, axis_name, behind)
        blocks.append(backward)
    return blocks


def ring_reduce_scatter(terms, axis_name, count):
    token_count, width = terms.shape
    block = width // count
    half = block // 2
    cycle = snake_cycle(count)
    position = jnp.array([cycle.index(t) for t in range(count)], jnp.int32)[lax.axis_index(axis_name)]
    owners = jnp.array(cycle, jnp.int32)
    rounded = terms.astype(jnp.bfloat16)

    def own_part(slot, side):
        start = owners[slot % count] * block + side * half
        return lax.dynamic_slice_in_dim(rounded, start, half, 1).astype(jnp.float32)

    ahead = [(cycle[p], cycle[(p + 1) % count]) for p in range(count)]
    behind = [(cycle[p], cycle[(p - 1) % count]) for p in range(count)]
    forward = own_part(position - 1 + count, 0)
    backward = own_part(position + 1, 1)
    for step in range(count - 1):
        forward = lax.ppermute(forward.astype(jnp.bfloat16), axis_name, ahead).astype(jnp.float32)
        forward = forward + own_part(position - 2 - step + 2 * count, 0)
        backward = lax.ppermute(backward.astype(jnp.bfloat16), axis_name, behind).astype(jnp.float32)
        backward = backward + own_part(position + 2 + step, 1)
    return jnp.concatenate([forward, backward], axis=1)


def out_proj_kernel(group_count, tiles_per_half, row_count, span_ref, *refs):
    att_refs = refs[:group_count]
    mine_refs = refs[group_count:2 * group_count]
    other_refs = refs[2 * group_count:3 * group_count]
    hidden_ref, scale_ref, out_ref, squares_ref = refs[3 * group_count:]
    tile = pl.program_id(0)

    def accumulate(w_refs):
        total = None
        for group in range(group_count):
            term = jnp.dot(att_refs[group][...], w_refs[group][...], preferred_element_type=jnp.float32)
            term = term.astype(jnp.bfloat16).astype(jnp.float32)
            total = term if total is None else total + term
        for span in range(scale_ref.shape[0]):
            rows = slice(span * row_count, (span + 1) * row_count)
            out_ref[rows, :] = (
                hidden_ref[rows, :].astype(jnp.float32) + scale_ref[span:span + 1, :] * total[rows, :]
            )
        result = out_ref[...]
        partial = jnp.broadcast_to(jnp.sum(result * result, axis=1, keepdims=True), squares_ref.shape)

        @pl.when(tile == 0)
        def _():
            squares_ref[...] = partial

        @pl.when(tile > 0)
        def _():
            squares_ref[...] += partial

    @pl.when(tile < tiles_per_half)
    def _():
        accumulate(mine_refs)

    @pl.when(tile >= tiles_per_half)
    def _():
        accumulate(other_refs)


def grouped_out_proj(
    span_index, att_blocks, mine_blocks, other_blocks, hidden, scale, tile_width=512
):
    group_count = len(att_blocks)
    token_count, head_width = att_blocks[0].shape
    half_width = mine_blocks[0].shape[1]
    span_rows = scale.shape[0]
    tile_width = min(tile_width, half_width)
    tiles_per_half = half_width // tile_width
    att_spec = pl.BlockSpec((token_count, head_width), lambda n, s: (0, 0))
    mine_spec = pl.BlockSpec(
        (head_width, tile_width), lambda n, s: (0, jnp.minimum(n, tiles_per_half - 1))
    )
    other_spec = pl.BlockSpec(
        (head_width, tile_width), lambda n, s: (0, jnp.maximum(n - tiles_per_half, 0))
    )

    def column(n, s):
        return ((n // tiles_per_half + s[0]) % 2) * tiles_per_half + n % tiles_per_half

    out_spec = pl.BlockSpec((token_count, tile_width), lambda n, s: (0, column(n, s)))
    hidden_spec = pl.BlockSpec((token_count, tile_width), lambda n, s: (0, column(n, s)))
    scale_spec = pl.BlockSpec((span_rows, tile_width), lambda n, s: (0, column(n, s)))
    squares_spec = pl.BlockSpec((token_count, 128), lambda n, s: (0, 0))
    tile_count = 2 * tiles_per_half
    flops = 2 * token_count * head_width * group_count * half_width * 2
    moved = 2 * (group_count * token_count * head_width + 2 * group_count * head_width * half_width)
    moved += token_count * 2 * half_width * (4 + 2)
    residual, squares = pl.pallas_call(
        functools.partial(out_proj_kernel, group_count, tiles_per_half, token_count // span_rows),
        out_shape=(
            jax.ShapeDtypeStruct((token_count, 2 * half_width), jnp.float32),
            jax.ShapeDtypeStruct((token_count, 128), jnp.float32),
        ),
        grid_spec=pltpu.PrefetchScalarGridSpec(
            num_scalar_prefetch=1,
            grid=(tile_count,),
            in_specs=[att_spec] * group_count + [mine_spec] * group_count + [other_spec] * group_count
            + [hidden_spec, scale_spec],
            out_specs=[out_spec, squares_spec],
        ),
        cost_estimate=pl.CostEstimate(flops=flops, bytes_accessed=moved, transcendentals=0),
    )(
        jnp.reshape(span_index, (1,)).astype(jnp.int32),
        *att_blocks,
        *mine_blocks,
        *other_blocks,
        hidden,
        scale,
    )
    return residual, squares[:, 0]


def select_row(source, target):
    matches = jnp.arange(source.shape[0], dtype=jnp.int32) == target
    return jnp.sum(jnp.where(matches.reshape((-1,) + (1,) * (source.ndim - 1)), source, 0), axis=0)


def attend(queries, cache_all, fresh_all, cache_seen, fresh_seen):
    row_count, head_count, head_size = queries.shape
    cache_keys = cache_all[:, :, 0].reshape(-1, head_count, head_size)
    cache_vals = cache_all[:, :, 1].reshape(-1, head_count, head_size)
    fresh_keys = fresh_all[:, :, 0].reshape(-1, head_count, head_size)
    fresh_vals = fresh_all[:, :, 1].reshape(-1, head_count, head_size)
    score_scale = 1.0 / math.sqrt(head_size)
    cache_scores = (
        jnp.einsum("qhd,khd->hqk", queries, cache_keys, preferred_element_type=jnp.float32)
        * score_scale
    )
    fresh_scores = (
        jnp.einsum("qhd,khd->hqk", queries, fresh_keys, preferred_element_type=jnp.float32)
        * score_scale
    )
    cache_scores = jnp.where(cache_seen[None, None, :], cache_scores, NEGATIVE)
    fresh_scores = jnp.where(fresh_seen[None, None, :], fresh_scores, NEGATIVE)
    scores = jnp.concatenate([cache_scores, fresh_scores], axis=2)
    row_max = jnp.max(scores, axis=2, keepdims=True)
    exp_terms = jnp.exp(scores - row_max)
    weights = (exp_terms / jnp.sum(exp_terms, axis=2, keepdims=True)).astype(jnp.bfloat16)
    split_at = cache_keys.shape[0]
    attended = jnp.einsum(
        "hqk,khd->qhd", weights[:, :, :split_at], cache_vals, preferred_element_type=jnp.float32
    )
    attended = attended + jnp.einsum(
        "hqk,khd->qhd", weights[:, :, split_at:], fresh_vals, preferred_element_type=jnp.float32
    )
    return attended.astype(jnp.bfloat16).reshape(row_count, head_count * head_size)


def local(
    hidden_in, levels, order, cache_mask, finished, cache_kv, modulation, w_qkv, w_out, w_up, w_down
):
    span_index = lax.axis_index("span")
    tp_rank = lax.axis_index("tp")
    span_count = lax.psum(1, "span")
    tp_count = lax.psum(1, "tp")
    model_width = modulation.shape[2]
    share_width = hidden_in.shape[2]
    local_count = hidden_in.shape[0]
    row_count = hidden_in.shape[1]
    token_count = local_count * row_count
    gather_weights = (
        tp_count * w_out.size * w_out.dtype.itemsize <= WEIGHT_GATHER_BYTES and span_count == 2
    )
    if gather_weights:
        cycle = snake_cycle(tp_count)
        position = jnp.array([cycle.index(t) for t in range(tp_count)], jnp.int32)[tp_rank]
        steps = list(range(tp_count // 2 + 1)) + [-k for k in range(1, (tp_count - 1) // 2 + 1)]
        owners = jnp.array(cycle, jnp.int32)
        gathered = jnp.zeros(hidden_in.shape[:2] + (model_width,), hidden_in.dtype)
        for step, piece in zip(steps, ring_gather(hidden_in, "tp", tp_count)):
            owner = owners[(position - step + tp_count) % tp_count]
            gathered = lax.dynamic_update_slice_in_dim(gathered, piece, owner * share_width, 2)
        gathered_narrow = gathered
        gathered = gathered.astype(jnp.float32)
    else:
        gathered = lax.all_gather(hidden_in, "tp", axis=2, tiled=True).astype(jnp.float32)
    if gather_weights:
        column_part = model_width // span_count
        w_out_part = lax.dynamic_slice_in_dim(w_out, span_index * column_part, column_part, 1)
        mine_blocks = ring_gather(w_out_part, "tp", tp_count)
        other_blocks = [lax.ppermute(b, "span", [(0, 1), (1, 0)]) for b in mine_blocks]
    up_full, down_full = (
        lax.all_gather(w_up, "span", axis=1, tiled=True),
        lax.all_gather(w_down, "span", axis=0, tiled=True),
    )
    mod_table = modulation.reshape(modulation.shape[0], -1)
    picker = (jnp.arange(mod_table.shape[0], dtype=jnp.int32)[None, :] == levels[:, None]).astype(
        jnp.bfloat16
    )
    mod_rows = jnp.dot(picker, mod_table, preferred_element_type=jnp.float32).reshape(
        local_count, 6, model_width
    )
    attn_in = (normalize(gathered) * mod_rows[:, 1][:, None] + mod_rows[:, 0][:, None]).astype(
        jnp.bfloat16
    )
    per_device = w_qkv.shape[2]
    projected = jnp.dot(
        attn_in.reshape(token_count, model_width),
        w_qkv.reshape(model_width, -1),
        preferred_element_type=jnp.float32,
    )
    projected = projected.astype(jnp.bfloat16).reshape(local_count, row_count, 3, per_device)
    queries = projected[:, :, 0].reshape(local_count, row_count, -1, HEAD_DIM)
    fresh_kv = projected[:, :, 1:]
    cache_all, fresh_all = (
        lax.all_gather(cache_kv, "span", axis=0, tiled=True),
        lax.all_gather(fresh_kv, "span", axis=0, tiled=True),
    )
    positions = jnp.arange(cache_mask.shape[0], dtype=jnp.int32)
    my_spans = span_index * local_count + jnp.arange(local_count, dtype=jnp.int32)
    mask_rows = jax.vmap(lambda target: select_row(cache_mask, target))(my_spans)
    my_order = jax.vmap(lambda target: select_row(order, target))(my_spans)
    cache_seen = jnp.repeat(
        (mask_rows == 1) | (positions[None, :] == finished[0]), row_count, axis=1
    )
    fresh_seen = jnp.repeat(order[None, :] <= my_order[:, None], row_count, axis=1)
    attended = jax.vmap(
        lambda q_rows, c_seen, f_seen: attend(q_rows, cache_all, fresh_all, c_seen, f_seen)
    )(queries, cache_seen, fresh_seen)
    if gather_weights:
        att_blocks = ring_gather(attended.reshape(token_count, per_device), "tp", tp_count)
        residual_rows, square_sums = grouped_out_proj(
            span_index,
            att_blocks,
            mine_blocks,
            other_blocks,
            gathered_narrow.reshape(token_count, model_width),
            mod_rows[:, 2],
        )
        residual_full = residual_rows.reshape(local_count, row_count, model_width)
        inverse = lax.rsqrt(square_sums.reshape(local_count, row_count, 1) / model_width + EPSILON)
        mlp_in = (
            residual_full * inverse * mod_rows[:, 4][:, None] + mod_rows[:, 3][:, None]
        ).astype(jnp.bfloat16)
    else:
        partial_value = jnp.dot(
            attended.reshape(token_count, -1), w_out, preferred_element_type=jnp.float32
        ).reshape(local_count, row_count, model_width)
        attn_part = lax.psum_scatter(
            partial_value.astype(jnp.bfloat16), "tp", scatter_dimension=2, tiled=True
        ).astype(jnp.float32)
        mod_share = lax.dynamic_slice_in_dim(mod_rows, tp_rank * share_width, share_width, 2)
        residual = hidden_in.astype(jnp.float32) + mod_share[:, 2][:, None] * attn_part
        squares = lax.psum(jnp.sum(residual * residual, axis=2), "tp")
        scaled = residual * lax.rsqrt(squares / model_width + EPSILON)[:, :, None]
        mlp_part = (scaled * mod_share[:, 4][:, None] + mod_share[:, 3][:, None]).astype(
            jnp.bfloat16
        )
        mlp_in = lax.all_gather(mlp_part, "tp", axis=2, tiled=True)
    pre_act = jnp.dot(mlp_in, up_full, preferred_element_type=jnp.float32)
    hidden_units = jax.nn.gelu(pre_act).astype(jnp.bfloat16)
    down_terms = jnp.dot(hidden_units, down_full, preferred_element_type=jnp.float32)
    if gather_weights:
        mlp_out = ring_reduce_scatter(
            down_terms.reshape(token_count, model_width), "tp", tp_count
        ).reshape(local_count, row_count, share_width)
    else:
        mlp_out = lax.psum_scatter(
            down_terms.astype(jnp.bfloat16), "tp", scatter_dimension=2, tiled=True
        ).astype(jnp.float32)
    if gather_weights:
        residual = lax.dynamic_slice_in_dim(residual_full, tp_rank * share_width, share_width, 2)
        mod_share = lax.dynamic_slice_in_dim(mod_rows, tp_rank * share_width, share_width, 2)
    result = residual + mod_share[:, 5][:, None] * mlp_out
    return result.astype(jnp.bfloat16)


def solution(mesh):
    placed = (
        P(("rep", "span"), None, "tp"),
        P(("rep", "span")),
        P("rep"),
        P("rep", None),
        P("rep"),
        P(("rep", "span"), None, None, "tp"),
        P(),
        P(None, None, "tp"),
        P("tp", None),
        P(None, ("span", "tp")),
        P(("span", "tp"), None),
    )
    return jax.shard_map(
        local, mesh=mesh, in_specs=placed, out_specs=P(("rep", "span"), None, "tp"), check_vma=False
    )
```

```python
import functools
import math

import jax
import jax.numpy as jnp
from jax import lax
from jax.experimental import pallas as pl
from jax.experimental.pallas import tpu as pltpu
from jax.sharding import PartitionSpec as P

HEAD_DIM = 128


EPSILON = 1e-06
NEGATIVE = -1e30
WEIGHT_GATHER_BYTES = 24 * 2**20


def normalize(values):
    return values * lax.rsqrt(jnp.mean(values * values, axis=-1, keepdims=True) + EPSILON)


def snake_cycle(count):
    return list(range(0, count, 2)) + list(range(count - 1, 0, -2)) if count % 2 == 0 else list(range(count))


def ring_gather(block, axis_name, count):
    cycle = snake_cycle(count)
    ahead = [(cycle[p], cycle[(p + 1) % count]) for p in range(count)]
    behind = [(cycle[p], cycle[(p - 1) % count]) for p in range(count)]
    blocks = [block]
    forward = block
    for _ in range(count // 2):
        forward = lax.ppermute(forward, axis_name, ahead)
        blocks.append(forward)
    backward = block
    for _ in range((count - 1) // 2):
        backward = lax.ppermute(backward, axis_name, behind)
        blocks.append(backward)
    return blocks


def ring_reduce_scatter(terms, axis_name, count):
    token_count, width = terms.shape
    block = width // count
    half = block // 2
    cycle = snake_cycle(count)
    position = jnp.array([cycle.index(t) for t in range(count)], jnp.int32)[lax.axis_index(axis_name)]
    owners = jnp.array(cycle, jnp.int32)
    rounded = terms.astype(jnp.bfloat16)

    def own_part(slot, side):
        start = owners[slot % count] * block + side * half
        return lax.dynamic_slice_in_dim(rounded, start, half, 1).astype(jnp.float32)

    ahead = [(cycle[p], cycle[(p + 1) % count]) for p in range(count)]
    behind = [(cycle[p], cycle[(p - 1) % count]) for p in range(count)]
    forward = own_part(position - 1 + count, 0)
    backward = own_part(position + 1, 1)
    for step in range(count - 1):
        forward = lax.ppermute(forward.astype(jnp.bfloat16), axis_name, ahead).astype(jnp.float32)
        forward = forward + own_part(position - 2 - step + 2 * count, 0)
        backward = lax.ppermute(backward.astype(jnp.bfloat16), axis_name, behind).astype(jnp.float32)
        backward = backward + own_part(position + 2 + step, 1)
    return jnp.concatenate([forward, backward], axis=1)


def out_proj_kernel(group_count, tiles_per_half, row_count, span_ref, *refs):
    att_refs = refs[:group_count]
    mine_refs = refs[group_count:2 * group_count]
    other_refs = refs[2 * group_count:3 * group_count]
    hidden_ref, scale_ref, out_ref, squares_ref = refs[3 * group_count:]
    tile = pl.program_id(0)

    def accumulate(w_refs):
        total = None
        for group in range(group_count):
            term = jnp.dot(att_refs[group][...], w_refs[group][...], preferred_element_type=jnp.float32)
            term = term.astype(jnp.bfloat16).astype(jnp.float32)
            total = term if total is None else total + term
        for span in range(scale_ref.shape[0]):
            rows = slice(span * row_count, (span + 1) * row_count)
            out_ref[rows, :] = (
                hidden_ref[rows, :].astype(jnp.float32) + scale_ref[span:span + 1, :] * total[rows, :]
            )
        result = out_ref[...]
        partial = jnp.broadcast_to(jnp.sum(result * result, axis=1, keepdims=True), squares_ref.shape)

        @pl.when(tile == 0)
        def _():
            squares_ref[...] = partial

        @pl.when(tile > 0)
        def _():
            squares_ref[...] += partial

    @pl.when(tile < tiles_per_half)
    def _():
        accumulate(mine_refs)

    @pl.when(tile >= tiles_per_half)
    def _():
        accumulate(other_refs)


def grouped_out_proj(
    span_index, att_blocks, mine_blocks, other_blocks, hidden, scale, tile_width=1024
):
    group_count = len(att_blocks)
    token_count, head_width = att_blocks[0].shape
    half_width = mine_blocks[0].shape[1]
    span_rows = scale.shape[0]
    tile_width = min(tile_width, half_width)
    tiles_per_half = half_width // tile_width
    att_spec = pl.BlockSpec((token_count, head_width), lambda n, s: (0, 0))
    mine_spec = pl.BlockSpec(
        (head_width, tile_width), lambda n, s: (0, jnp.minimum(n, tiles_per_half - 1))
    )
    other_spec = pl.BlockSpec(
        (head_width, tile_width), lambda n, s: (0, jnp.maximum(n - tiles_per_half, 0))
    )

    def column(n, s):
        return ((n // tiles_per_half + s[0]) % 2) * tiles_per_half + n % tiles_per_half

    out_spec = pl.BlockSpec((token_count, tile_width), lambda n, s: (0, column(n, s)))
    hidden_spec = pl.BlockSpec((token_count, tile_width), lambda n, s: (0, column(n, s)))
    scale_spec = pl.BlockSpec((span_rows, tile_width), lambda n, s: (0, column(n, s)))
    squares_spec = pl.BlockSpec((token_count, 128), lambda n, s: (0, 0))
    tile_count = 2 * tiles_per_half
    flops = 2 * token_count * head_width * group_count * half_width * 2
    moved = 2 * (group_count * token_count * head_width + 2 * group_count * head_width * half_width)
    moved += token_count * 2 * half_width * (4 + 2)
    residual, squares = pl.pallas_call(
        functools.partial(out_proj_kernel, group_count, tiles_per_half, token_count // span_rows),
        out_shape=(
            jax.ShapeDtypeStruct((token_count, 2 * half_width), jnp.float32),
            jax.ShapeDtypeStruct((token_count, 128), jnp.float32),
        ),
        grid_spec=pltpu.PrefetchScalarGridSpec(
            num_scalar_prefetch=1,
            grid=(tile_count,),
            in_specs=[att_spec] * group_count + [mine_spec] * group_count + [other_spec] * group_count
            + [hidden_spec, scale_spec],
            out_specs=[out_spec, squares_spec],
        ),
        cost_estimate=pl.CostEstimate(flops=flops, bytes_accessed=moved, transcendentals=0),
    )(
        jnp.reshape(span_index, (1,)).astype(jnp.int32),
        *att_blocks,
        *mine_blocks,
        *other_blocks,
        hidden,
        scale,
    )
    return residual, squares[:, 0]


def select_row(source, target):
    matches = jnp.arange(source.shape[0], dtype=jnp.int32) == target
    return jnp.sum(jnp.where(matches.reshape((-1,) + (1,) * (source.ndim - 1)), source, 0), axis=0)


def attend(queries, cache_all, fresh_all, cache_seen, fresh_seen):
    row_count, head_count, head_size = queries.shape
    cache_keys = cache_all[:, :, 0].reshape(-1, head_count, head_size)
    cache_vals = cache_all[:, :, 1].reshape(-1, head_count, head_size)
    fresh_keys = fresh_all[:, :, 0].reshape(-1, head_count, head_size)
    fresh_vals = fresh_all[:, :, 1].reshape(-1, head_count, head_size)
    score_scale = 1.0 / math.sqrt(head_size)
    cache_scores = (
        jnp.einsum("qhd,khd->hqk", queries, cache_keys, preferred_element_type=jnp.float32)
        * score_scale
    )
    fresh_scores = (
        jnp.einsum("qhd,khd->hqk", queries, fresh_keys, preferred_element_type=jnp.float32)
        * score_scale
    )
    cache_scores = jnp.where(cache_seen[None, None, :], cache_scores, NEGATIVE)
    fresh_scores = jnp.where(fresh_seen[None, None, :], fresh_scores, NEGATIVE)
    scores = jnp.concatenate([cache_scores, fresh_scores], axis=2)
    row_max = jnp.max(scores, axis=2, keepdims=True)
    exp_terms = jnp.exp(scores - row_max)
    weights = (exp_terms / jnp.sum(exp_terms, axis=2, keepdims=True)).astype(jnp.bfloat16)
    split_at = cache_keys.shape[0]
    attended = jnp.einsum(
        "hqk,khd->qhd", weights[:, :, :split_at], cache_vals, preferred_element_type=jnp.float32
    )
    attended = attended + jnp.einsum(
        "hqk,khd->qhd", weights[:, :, split_at:], fresh_vals, preferred_element_type=jnp.float32
    )
    return attended.astype(jnp.bfloat16).reshape(row_count, head_count * head_size)


def local(
    hidden_in, levels, order, cache_mask, finished, cache_kv, modulation, w_qkv, w_out, w_up, w_down
):
    span_index = lax.axis_index("span")
    tp_rank = lax.axis_index("tp")
    span_count = lax.psum(1, "span")
    tp_count = lax.psum(1, "tp")
    model_width = modulation.shape[2]
    share_width = hidden_in.shape[2]
    local_count = hidden_in.shape[0]
    row_count = hidden_in.shape[1]
    token_count = local_count * row_count
    gather_weights = (
        tp_count * w_out.size * w_out.dtype.itemsize <= WEIGHT_GATHER_BYTES and span_count == 2
    )
    if gather_weights:
        cycle = snake_cycle(tp_count)
        position = jnp.array([cycle.index(t) for t in range(tp_count)], jnp.int32)[tp_rank]
        steps = list(range(tp_count // 2 + 1)) + [-k for k in range(1, (tp_count - 1) // 2 + 1)]
        owners = jnp.array(cycle, jnp.int32)
        gathered = jnp.zeros(hidden_in.shape[:2] + (model_width,), hidden_in.dtype)
        for step, piece in zip(steps, ring_gather(hidden_in, "tp", tp_count)):
            owner = owners[(position - step + tp_count) % tp_count]
            gathered = lax.dynamic_update_slice_in_dim(gathered, piece, owner * share_width, 2)
        gathered_narrow = gathered
        gathered = gathered.astype(jnp.float32)
    else:
        gathered = lax.all_gather(hidden_in, "tp", axis=2, tiled=True).astype(jnp.float32)
    if gather_weights:
        column_part = model_width // span_count
        w_out_part = lax.dynamic_slice_in_dim(w_out, span_index * column_part, column_part, 1)
        mine_blocks = ring_gather(w_out_part, "tp", tp_count)
        other_blocks = [lax.ppermute(b, "span", [(0, 1), (1, 0)]) for b in mine_blocks]
    up_full, down_full = (
        lax.all_gather(w_up, "span", axis=1, tiled=True),
        lax.all_gather(w_down, "span", axis=0, tiled=True),
    )
    mod_table = modulation.reshape(modulation.shape[0], -1)
    picker = (jnp.arange(mod_table.shape[0], dtype=jnp.int32)[None, :] == levels[:, None]).astype(
        jnp.bfloat16
    )
    mod_rows = jnp.dot(picker, mod_table, preferred_element_type=jnp.float32).reshape(
        local_count, 6, model_width
    )
    attn_in = (normalize(gathered) * mod_rows[:, 1][:, None] + mod_rows[:, 0][:, None]).astype(
        jnp.bfloat16
    )
    per_device = w_qkv.shape[2]
    projected = jnp.dot(
        attn_in.reshape(token_count, model_width),
        w_qkv.reshape(model_width, -1),
        preferred_element_type=jnp.float32,
    )
    projected = projected.astype(jnp.bfloat16).reshape(local_count, row_count, 3, per_device)
    queries = projected[:, :, 0].reshape(local_count, row_count, -1, HEAD_DIM)
    fresh_kv = projected[:, :, 1:]
    cache_all, fresh_all = (
        lax.all_gather(cache_kv, "span", axis=0, tiled=True),
        lax.all_gather(fresh_kv, "span", axis=0, tiled=True),
    )
    positions = jnp.arange(cache_mask.shape[0], dtype=jnp.int32)
    my_spans = span_index * local_count + jnp.arange(local_count, dtype=jnp.int32)
    mask_rows = jax.vmap(lambda target: select_row(cache_mask, target))(my_spans)
    my_order = jax.vmap(lambda target: select_row(order, target))(my_spans)
    cache_seen = jnp.repeat(
        (mask_rows == 1) | (positions[None, :] == finished[0]), row_count, axis=1
    )
    fresh_seen = jnp.repeat(order[None, :] <= my_order[:, None], row_count, axis=1)
    attended = jax.vmap(
        lambda q_rows, c_seen, f_seen: attend(q_rows, cache_all, fresh_all, c_seen, f_seen)
    )(queries, cache_seen, fresh_seen)
    if gather_weights:
        att_blocks = ring_gather(attended.reshape(token_count, per_device), "tp", tp_count)
        residual_rows, square_sums = grouped_out_proj(
            span_index,
            att_blocks,
            mine_blocks,
            other_blocks,
            gathered_narrow.reshape(token_count, model_width),
            mod_rows[:, 2],
        )
        residual_full = residual_rows.reshape(local_count, row_count, model_width)
        inverse = lax.rsqrt(square_sums.reshape(local_count, row_count, 1) / model_width + EPSILON)
        mlp_in = (
            residual_full * inverse * mod_rows[:, 4][:, None] + mod_rows[:, 3][:, None]
        ).astype(jnp.bfloat16)
    else:
        partial_value = jnp.dot(
            attended.reshape(token_count, -1), w_out, preferred_element_type=jnp.float32
        ).reshape(local_count, row_count, model_width)
        attn_part = lax.psum_scatter(
            partial_value.astype(jnp.bfloat16), "tp", scatter_dimension=2, tiled=True
        ).astype(jnp.float32)
        mod_share = lax.dynamic_slice_in_dim(mod_rows, tp_rank * share_width, share_width, 2)
        residual = hidden_in.astype(jnp.float32) + mod_share[:, 2][:, None] * attn_part
        squares = lax.psum(jnp.sum(residual * residual, axis=2), "tp")
        scaled = residual * lax.rsqrt(squares / model_width + EPSILON)[:, :, None]
        mlp_part = (scaled * mod_share[:, 4][:, None] + mod_share[:, 3][:, None]).astype(
            jnp.bfloat16
        )
        mlp_in = lax.all_gather(mlp_part, "tp", axis=2, tiled=True)
    pre_act = jnp.dot(mlp_in, up_full, preferred_element_type=jnp.float32)
    hidden_units = jax.nn.gelu(pre_act).astype(jnp.bfloat16)
    down_terms = jnp.dot(hidden_units, down_full, preferred_element_type=jnp.float32)
    if gather_weights:
        mlp_out = ring_reduce_scatter(
            down_terms.reshape(token_count, model_width), "tp", tp_count
        ).reshape(local_count, row_count, share_width)
    else:
        mlp_out = lax.psum_scatter(
            down_terms.astype(jnp.bfloat16), "tp", scatter_dimension=2, tiled=True
        ).astype(jnp.float32)
    if gather_weights:
        residual = lax.dynamic_slice_in_dim(residual_full, tp_rank * share_width, share_width, 2)
        mod_share = lax.dynamic_slice_in_dim(mod_rows, tp_rank * share_width, share_width, 2)
    result = residual + mod_share[:, 5][:, None] * mlp_out
    return result.astype(jnp.bfloat16)


def solution(mesh):
    placed = (
        P(("rep", "span"), None, "tp"),
        P(("rep", "span")),
        P("rep"),
        P("rep", None),
        P("rep"),
        P(("rep", "span"), None, None, "tp"),
        P(),
        P(None, None, "tp"),
        P("tp", None),
        P(None, ("span", "tp")),
        P(("span", "tp"), None),
    )
    return jax.shard_map(
        local, mesh=mesh, in_specs=placed, out_specs=P(("rep", "span"), None, "tp"), check_vma=False
    )
```

```python
import functools
import math

import jax
import jax.numpy as jnp
from jax import lax
from jax.experimental import pallas as pl
from jax.experimental.pallas import tpu as pltpu
from jax.sharding import PartitionSpec as P

HEAD_DIM = 128


EPSILON = 1e-06
NEGATIVE = -1e30
WEIGHT_GATHER_BYTES = 24 * 2**20


def normalize(values):
    return values * lax.rsqrt(jnp.mean(values * values, axis=-1, keepdims=True) + EPSILON)


def snake_cycle(count):
    return list(range(0, count, 2)) + list(range(count - 1, 0, -2)) if count % 2 == 0 else list(range(count))


def ring_gather(block, axis_name, count):
    cycle = snake_cycle(count)
    ahead = [(cycle[p], cycle[(p + 1) % count]) for p in range(count)]
    behind = [(cycle[p], cycle[(p - 1) % count]) for p in range(count)]
    blocks = [block]
    forward = block
    for _ in range(count // 2):
        forward = lax.ppermute(forward, axis_name, ahead)
        blocks.append(forward)
    backward = block
    for _ in range((count - 1) // 2):
        backward = lax.ppermute(backward, axis_name, behind)
        blocks.append(backward)
    return blocks


def ring_reduce_scatter(terms, axis_name, count):
    token_count, width = terms.shape
    block = width // count
    half = block // 2
    cycle = snake_cycle(count)
    position = jnp.array([cycle.index(t) for t in range(count)], jnp.int32)[lax.axis_index(axis_name)]
    owners = jnp.array(cycle, jnp.int32)
    rounded = terms.astype(jnp.bfloat16)

    def own_part(slot, side):
        start = owners[slot % count] * block + side * half
        return lax.dynamic_slice_in_dim(rounded, start, half, 1).astype(jnp.float32)

    ahead = [(cycle[p], cycle[(p + 1) % count]) for p in range(count)]
    behind = [(cycle[p], cycle[(p - 1) % count]) for p in range(count)]
    forward = own_part(position - 1 + count, 0)
    backward = own_part(position + 1, 1)
    for step in range(count - 1):
        forward = lax.ppermute(forward.astype(jnp.bfloat16), axis_name, ahead).astype(jnp.float32)
        forward = forward + own_part(position - 2 - step + 2 * count, 0)
        backward = lax.ppermute(backward.astype(jnp.bfloat16), axis_name, behind).astype(jnp.float32)
        backward = backward + own_part(position + 2 + step, 1)
    return jnp.concatenate([forward, backward], axis=1)


def out_proj_kernel(group_count, tiles_per_half, row_count, span_ref, *refs):
    att_refs = refs[:group_count]
    mine_refs = refs[group_count:2 * group_count]
    other_refs = refs[2 * group_count:3 * group_count]
    hidden_ref, scale_ref, out_ref, squares_ref = refs[3 * group_count:]
    tile = pl.program_id(0)

    def accumulate(w_refs):
        total = None
        for group in range(group_count):
            term = jnp.dot(att_refs[group][...], w_refs[group][...], preferred_element_type=jnp.float32)
            term = term.astype(jnp.bfloat16).astype(jnp.float32)
            total = term if total is None else total + term
        for span in range(scale_ref.shape[0]):
            rows = slice(span * row_count, (span + 1) * row_count)
            out_ref[rows, :] = (
                hidden_ref[rows, :].astype(jnp.float32) + scale_ref[span:span + 1, :] * total[rows, :]
            )
        result = out_ref[...]
        partial = jnp.broadcast_to(jnp.sum(result * result, axis=1, keepdims=True), squares_ref.shape)

        @pl.when(tile == 0)
        def _():
            squares_ref[...] = partial

        @pl.when(tile > 0)
        def _():
            squares_ref[...] += partial

    @pl.when(tile < tiles_per_half)
    def _():
        accumulate(mine_refs)

    @pl.when(tile >= tiles_per_half)
    def _():
        accumulate(other_refs)


def grouped_out_proj(
    span_index, att_blocks, mine_blocks, other_blocks, hidden, scale, tile_width=512
):
    group_count = len(att_blocks)
    token_count, head_width = att_blocks[0].shape
    half_width = mine_blocks[0].shape[1]
    span_rows = scale.shape[0]
    tile_width = min(tile_width, half_width)
    tiles_per_half = half_width // tile_width
    att_spec = pl.BlockSpec((token_count, head_width), lambda n, s: (0, 0))
    mine_spec = pl.BlockSpec(
        (head_width, tile_width), lambda n, s: (0, jnp.minimum(n, tiles_per_half - 1))
    )
    other_spec = pl.BlockSpec(
        (head_width, tile_width), lambda n, s: (0, jnp.maximum(n - tiles_per_half, 0))
    )

    def column(n, s):
        return ((n // tiles_per_half + s[0]) % 2) * tiles_per_half + n % tiles_per_half

    out_spec = pl.BlockSpec((token_count, tile_width), lambda n, s: (0, column(n, s)))
    hidden_spec = pl.BlockSpec((token_count, tile_width), lambda n, s: (0, column(n, s)))
    scale_spec = pl.BlockSpec((span_rows, tile_width), lambda n, s: (0, column(n, s)))
    squares_spec = pl.BlockSpec((token_count, 128), lambda n, s: (0, 0))
    tile_count = 2 * tiles_per_half
    flops = 2 * token_count * head_width * group_count * half_width * 2
    moved = 2 * (group_count * token_count * head_width + 2 * group_count * head_width * half_width)
    moved += token_count * 2 * half_width * (4 + 2)
    residual, squares = pl.pallas_call(
        functools.partial(out_proj_kernel, group_count, tiles_per_half, token_count // span_rows),
        out_shape=(
            jax.ShapeDtypeStruct((token_count, 2 * half_width), jnp.float32),
            jax.ShapeDtypeStruct((token_count, 128), jnp.float32),
        ),
        grid_spec=pltpu.PrefetchScalarGridSpec(
            num_scalar_prefetch=1,
            grid=(tile_count,),
            in_specs=[att_spec] * group_count + [mine_spec] * group_count + [other_spec] * group_count
            + [hidden_spec, scale_spec],
            out_specs=[out_spec, squares_spec],
        ),
        cost_estimate=pl.CostEstimate(flops=flops, bytes_accessed=moved, transcendentals=0),
    )(
        jnp.reshape(span_index, (1,)).astype(jnp.int32),
        *att_blocks,
        *mine_blocks,
        *other_blocks,
        hidden,
        scale,
    )
    return residual, squares[:, 0]


def select_row(source, target):
    matches = jnp.arange(source.shape[0], dtype=jnp.int32) == target
    return jnp.sum(jnp.where(matches.reshape((-1,) + (1,) * (source.ndim - 1)), source, 0), axis=0)


def attend(queries, cache_all, fresh_all, cache_seen, fresh_seen):
    row_count, head_count, head_size = queries.shape
    cache_keys = cache_all[:, :, 0].reshape(-1, head_count, head_size)
    cache_vals = cache_all[:, :, 1].reshape(-1, head_count, head_size)
    fresh_keys = fresh_all[:, :, 0].reshape(-1, head_count, head_size)
    fresh_vals = fresh_all[:, :, 1].reshape(-1, head_count, head_size)
    score_scale = 1.0 / math.sqrt(head_size)
    cache_scores = (
        jnp.einsum("qhd,khd->hqk", queries, cache_keys, preferred_element_type=jnp.float32)
        * score_scale
    )
    fresh_scores = (
        jnp.einsum("qhd,khd->hqk", queries, fresh_keys, preferred_element_type=jnp.float32)
        * score_scale
    )
    cache_scores = jnp.where(cache_seen[None, None, :], cache_scores, NEGATIVE)
    fresh_scores = jnp.where(fresh_seen[None, None, :], fresh_scores, NEGATIVE)
    scores = jnp.concatenate([cache_scores, fresh_scores], axis=2)
    row_max = jnp.max(scores, axis=2, keepdims=True)
    exp_terms = jnp.exp(scores - row_max)
    weights = (exp_terms / jnp.sum(exp_terms, axis=2, keepdims=True)).astype(jnp.bfloat16)
    split_at = cache_keys.shape[0]
    attended = jnp.einsum(
        "hqk,khd->qhd", weights[:, :, :split_at], cache_vals, preferred_element_type=jnp.float32
    )
    attended = attended + jnp.einsum(
        "hqk,khd->qhd", weights[:, :, split_at:], fresh_vals, preferred_element_type=jnp.float32
    )
    return attended.astype(jnp.bfloat16).reshape(row_count, head_count * head_size)


def local(
    hidden_in, levels, order, cache_mask, finished, cache_kv, modulation, w_qkv, w_out, w_up, w_down
):
    span_index = lax.axis_index("span")
    tp_rank = lax.axis_index("tp")
    span_count = lax.psum(1, "span")
    tp_count = lax.psum(1, "tp")
    model_width = modulation.shape[2]
    share_width = hidden_in.shape[2]
    local_count = hidden_in.shape[0]
    row_count = hidden_in.shape[1]
    token_count = local_count * row_count
    gather_weights = (
        tp_count * w_out.size * w_out.dtype.itemsize <= WEIGHT_GATHER_BYTES and span_count == 2
    )
    if gather_weights:
        cycle = snake_cycle(tp_count)
        position = jnp.array([cycle.index(t) for t in range(tp_count)], jnp.int32)[tp_rank]
        steps = list(range(tp_count // 2 + 1)) + [-k for k in range(1, (tp_count - 1) // 2 + 1)]
        owners = jnp.array(cycle, jnp.int32)
        gathered = jnp.zeros(hidden_in.shape[:2] + (model_width,), hidden_in.dtype)
        for step, piece in zip(steps, ring_gather(hidden_in, "tp", tp_count)):
            owner = owners[(position - step + tp_count) % tp_count]
            gathered = lax.dynamic_update_slice_in_dim(gathered, piece, owner * share_width, 2)
        gathered_narrow = gathered
        gathered = gathered.astype(jnp.float32)
    else:
        gathered = lax.all_gather(hidden_in, "tp", axis=2, tiled=True).astype(jnp.float32)
    if gather_weights:
        column_part = model_width // span_count
        w_out_part = lax.dynamic_slice_in_dim(w_out, span_index * column_part, column_part, 1)
        mine_blocks = ring_gather(w_out_part, "tp", tp_count)
        other_blocks = [lax.ppermute(b, "span", [(0, 1), (1, 0)]) for b in mine_blocks]
    up_full, down_full = (
        lax.all_gather(w_up, "span", axis=1, tiled=True),
        lax.all_gather(w_down, "span", axis=0, tiled=True),
    )
    mod_table = modulation.reshape(modulation.shape[0], -1)
    picker = (jnp.arange(mod_table.shape[0], dtype=jnp.int32)[None, :] == levels[:, None]).astype(
        jnp.bfloat16
    )
    mod_rows = jnp.dot(picker, mod_table, preferred_element_type=jnp.float32).reshape(
        local_count, 6, model_width
    )
    attn_in = (normalize(gathered) * mod_rows[:, 1][:, None] + mod_rows[:, 0][:, None]).astype(
        jnp.bfloat16
    )
    per_device = w_qkv.shape[2]
    projected = jnp.dot(
        attn_in.reshape(token_count, model_width),
        w_qkv.reshape(model_width, -1),
        preferred_element_type=jnp.float32,
    )
    projected = projected.astype(jnp.bfloat16).reshape(local_count, row_count, 3, per_device)
    queries = projected[:, :, 0].reshape(local_count, row_count, -1, HEAD_DIM)
    fresh_kv = projected[:, :, 1:]
    cache_all, fresh_all = (
        lax.all_gather(cache_kv, "span", axis=0, tiled=True),
        lax.all_gather(fresh_kv, "span", axis=0, tiled=True),
    )
    positions = jnp.arange(cache_mask.shape[0], dtype=jnp.int32)
    my_spans = span_index * local_count + jnp.arange(local_count, dtype=jnp.int32)
    mask_rows = jax.vmap(lambda target: select_row(cache_mask, target))(my_spans)
    my_order = jax.vmap(lambda target: select_row(order, target))(my_spans)
    cache_seen = jnp.repeat(
        (mask_rows == 1) | (positions[None, :] == finished[0]), row_count, axis=1
    )
    fresh_seen = jnp.repeat(order[None, :] <= my_order[:, None], row_count, axis=1)
    attended = jax.vmap(
        lambda q_rows, c_seen, f_seen: attend(q_rows, cache_all, fresh_all, c_seen, f_seen)
    )(queries, cache_seen, fresh_seen)
    if gather_weights:
        att_blocks = ring_gather(attended.reshape(token_count, per_device), "tp", tp_count)
        residual_rows, square_sums = grouped_out_proj(
            span_index,
            att_blocks,
            mine_blocks,
            other_blocks,
            gathered_narrow.reshape(token_count, model_width),
            mod_rows[:, 2],
        )
        residual_full = residual_rows.reshape(local_count, row_count, model_width)
        inverse = lax.rsqrt(square_sums.reshape(local_count, row_count, 1) / model_width + EPSILON)
        mlp_in = (
            residual_full * inverse * mod_rows[:, 4][:, None] + mod_rows[:, 3][:, None]
        ).astype(jnp.bfloat16)
    else:
        partial_value = jnp.dot(
            attended.reshape(token_count, -1), w_out, preferred_element_type=jnp.float32
        ).reshape(local_count, row_count, model_width)
        attn_part = lax.psum_scatter(
            partial_value.astype(jnp.bfloat16), "tp", scatter_dimension=2, tiled=True
        ).astype(jnp.float32)
        mod_share = lax.dynamic_slice_in_dim(mod_rows, tp_rank * share_width, share_width, 2)
        residual = hidden_in.astype(jnp.float32) + mod_share[:, 2][:, None] * attn_part
        squares = lax.psum(jnp.sum(residual * residual, axis=2), "tp")
        scaled = residual * lax.rsqrt(squares / model_width + EPSILON)[:, :, None]
        mlp_part = (scaled * mod_share[:, 4][:, None] + mod_share[:, 3][:, None]).astype(
            jnp.bfloat16
        )
        mlp_in = lax.all_gather(mlp_part, "tp", axis=2, tiled=True)
    pre_act = jnp.dot(mlp_in, up_full, preferred_element_type=jnp.float32)
    hidden_units = jax.nn.gelu(pre_act).astype(jnp.bfloat16)
    down_terms = jnp.dot(hidden_units, down_full, preferred_element_type=jnp.float32)
    if gather_weights:
        split = share_width // 2
        blocks = down_terms.reshape(token_count, tp_count, share_width)
        ring_part = ring_reduce_scatter(
            blocks[:, :, :split].reshape(token_count, tp_count * split), "tp", tp_count
        )
        offload_part = lax.psum_scatter(
            blocks[:, :, split:].astype(jnp.bfloat16), "tp", scatter_dimension=1, tiled=True
        ).reshape(token_count, share_width - split)
        mlp_out = jnp.concatenate(
            [ring_part, offload_part.astype(jnp.float32)], axis=1
        ).reshape(local_count, row_count, share_width)
    else:
        mlp_out = lax.psum_scatter(
            down_terms.astype(jnp.bfloat16), "tp", scatter_dimension=2, tiled=True
        ).astype(jnp.float32)
    if gather_weights:
        residual = lax.dynamic_slice_in_dim(residual_full, tp_rank * share_width, share_width, 2)
        mod_share = lax.dynamic_slice_in_dim(mod_rows, tp_rank * share_width, share_width, 2)
    result = residual + mod_share[:, 5][:, None] * mlp_out
    return result.astype(jnp.bfloat16)


def solution(mesh):
    placed = (
        P(("rep", "span"), None, "tp"),
        P(("rep", "span")),
        P("rep"),
        P("rep", None),
        P("rep"),
        P(("rep", "span"), None, None, "tp"),
        P(),
        P(None, None, "tp"),
        P("tp", None),
        P(None, ("span", "tp")),
        P(("span", "tp"), None),
    )
    return jax.shard_map(
        local, mesh=mesh, in_specs=placed, out_specs=P(("rep", "span"), None, "tp"), check_vma=False
    )
```

```python
import functools
import math

import jax
import jax.numpy as jnp
from jax import lax
from jax.experimental import pallas as pl
from jax.experimental.pallas import tpu as pltpu
from jax.sharding import PartitionSpec as P

HEAD_DIM = 128


EPSILON = 1e-06
NEGATIVE = -1e30
WEIGHT_GATHER_BYTES = 24 * 2**20


def normalize(values):
    return values * lax.rsqrt(jnp.mean(values * values, axis=-1, keepdims=True) + EPSILON)


def snake_cycle(count):
    return list(range(0, count, 2)) + list(range(count - 1, 0, -2)) if count % 2 == 0 else list(range(count))


def ring_gather(block, axis_name, count):
    cycle = snake_cycle(count)
    ahead = [(cycle[p], cycle[(p + 1) % count]) for p in range(count)]
    behind = [(cycle[p], cycle[(p - 1) % count]) for p in range(count)]
    blocks = [block]
    forward = block
    for _ in range(count // 2):
        forward = lax.ppermute(forward, axis_name, ahead)
        blocks.append(forward)
    backward = block
    for _ in range((count - 1) // 2):
        backward = lax.ppermute(backward, axis_name, behind)
        blocks.append(backward)
    return blocks


def ring_reduce_scatter(terms, axis_name, count):
    token_count, width = terms.shape
    block = width // count
    half = block // 2
    cycle = snake_cycle(count)
    position = jnp.array([cycle.index(t) for t in range(count)], jnp.int32)[lax.axis_index(axis_name)]
    owners = jnp.array(cycle, jnp.int32)
    rounded = terms.astype(jnp.bfloat16)

    def own_part(slot, side):
        start = owners[slot % count] * block + side * half
        return lax.dynamic_slice_in_dim(rounded, start, half, 1).astype(jnp.float32)

    ahead = [(cycle[p], cycle[(p + 1) % count]) for p in range(count)]
    behind = [(cycle[p], cycle[(p - 1) % count]) for p in range(count)]
    forward = own_part(position - 1 + count, 0)
    backward = own_part(position + 1, 1)
    for step in range(count - 1):
        forward = lax.ppermute(forward.astype(jnp.bfloat16), axis_name, ahead).astype(jnp.float32)
        forward = forward + own_part(position - 2 - step + 2 * count, 0)
        backward = lax.ppermute(backward.astype(jnp.bfloat16), axis_name, behind).astype(jnp.float32)
        backward = backward + own_part(position + 2 + step, 1)
    return jnp.concatenate([forward, backward], axis=1)


def out_proj_kernel(group_count, tiles_per_half, row_count, span_ref, *refs):
    att_refs = refs[:group_count]
    mine_refs = refs[group_count:2 * group_count]
    other_refs = refs[2 * group_count:3 * group_count]
    hidden_ref, scale_ref, out_ref, squares_ref = refs[3 * group_count:]
    tile = pl.program_id(0)

    def accumulate(w_refs):
        total = None
        for group in range(group_count):
            term = jnp.dot(att_refs[group][...], w_refs[group][...], preferred_element_type=jnp.float32)
            term = term.astype(jnp.bfloat16).astype(jnp.float32)
            total = term if total is None else total + term
        for span in range(scale_ref.shape[0]):
            rows = slice(span * row_count, (span + 1) * row_count)
            out_ref[rows, :] = (
                hidden_ref[rows, :].astype(jnp.float32) + scale_ref[span:span + 1, :] * total[rows, :]
            )
        result = out_ref[...]
        partial = jnp.broadcast_to(jnp.sum(result * result, axis=1, keepdims=True), squares_ref.shape)

        @pl.when(tile == 0)
        def _():
            squares_ref[...] = partial

        @pl.when(tile > 0)
        def _():
            squares_ref[...] += partial

    @pl.when(tile < tiles_per_half)
    def _():
        accumulate(mine_refs)

    @pl.when(tile >= tiles_per_half)
    def _():
        accumulate(other_refs)


def grouped_out_proj(
    span_index, att_blocks, mine_blocks, other_halves, hidden, scale, tile_width=1024
):
    group_count = len(att_blocks)
    token_count, head_width = att_blocks[0].shape
    half_width = mine_blocks[0].shape[1]
    span_rows = scale.shape[0]
    tile_width = min(tile_width, half_width)
    tiles_per_half = half_width // tile_width
    att_spec = pl.BlockSpec((token_count, head_width), lambda n, s: (0, 0))
    mine_spec = pl.BlockSpec(
        (head_width, tile_width), lambda n, s: (0, jnp.minimum(n, tiles_per_half - 1))
    )
    def other_spec(group):
        return pl.BlockSpec(
            (None, None, head_width, tile_width),
            lambda n, s: (1 - s[0], group, 0, jnp.maximum(n - tiles_per_half, 0)),
        )


    def column(n, s):
        return ((n // tiles_per_half + s[0]) % 2) * tiles_per_half + n % tiles_per_half

    out_spec = pl.BlockSpec((token_count, tile_width), lambda n, s: (0, column(n, s)))
    hidden_spec = pl.BlockSpec((token_count, tile_width), lambda n, s: (0, column(n, s)))
    scale_spec = pl.BlockSpec((span_rows, tile_width), lambda n, s: (0, column(n, s)))
    squares_spec = pl.BlockSpec((token_count, 128), lambda n, s: (0, 0))
    tile_count = 2 * tiles_per_half
    flops = 2 * token_count * head_width * group_count * half_width * 2
    moved = 2 * (group_count * token_count * head_width + 2 * group_count * head_width * half_width)
    moved += token_count * 2 * half_width * (4 + 2)
    residual, squares = pl.pallas_call(
        functools.partial(out_proj_kernel, group_count, tiles_per_half, token_count // span_rows),
        out_shape=(
            jax.ShapeDtypeStruct((token_count, 2 * half_width), jnp.float32),
            jax.ShapeDtypeStruct((token_count, 128), jnp.float32),
        ),
        grid_spec=pltpu.PrefetchScalarGridSpec(
            num_scalar_prefetch=1,
            grid=(tile_count,),
            in_specs=[att_spec] * group_count + [mine_spec] * group_count
            + [other_spec(g) for g in range(group_count)]
            + [hidden_spec, scale_spec],
            out_specs=[out_spec, squares_spec],
        ),
        cost_estimate=pl.CostEstimate(flops=flops, bytes_accessed=moved, transcendentals=0),
    )(
        jnp.reshape(span_index, (1,)).astype(jnp.int32),
        *att_blocks,
        *mine_blocks,
        *([other_halves] * group_count),
        hidden,
        scale,
    )
    return residual, squares[:, 0]


def select_row(source, target):
    matches = jnp.arange(source.shape[0], dtype=jnp.int32) == target
    return jnp.sum(jnp.where(matches.reshape((-1,) + (1,) * (source.ndim - 1)), source, 0), axis=0)


def attend(queries, cache_all, fresh_all, cache_seen, fresh_seen):
    row_count, head_count, head_size = queries.shape
    cache_keys = cache_all[:, :, 0].reshape(-1, head_count, head_size)
    cache_vals = cache_all[:, :, 1].reshape(-1, head_count, head_size)
    fresh_keys = fresh_all[:, :, 0].reshape(-1, head_count, head_size)
    fresh_vals = fresh_all[:, :, 1].reshape(-1, head_count, head_size)
    score_scale = 1.0 / math.sqrt(head_size)
    cache_scores = (
        jnp.einsum("qhd,khd->hqk", queries, cache_keys, preferred_element_type=jnp.float32)
        * score_scale
    )
    fresh_scores = (
        jnp.einsum("qhd,khd->hqk", queries, fresh_keys, preferred_element_type=jnp.float32)
        * score_scale
    )
    cache_scores = jnp.where(cache_seen[None, None, :], cache_scores, NEGATIVE)
    fresh_scores = jnp.where(fresh_seen[None, None, :], fresh_scores, NEGATIVE)
    scores = jnp.concatenate([cache_scores, fresh_scores], axis=2)
    row_max = jnp.max(scores, axis=2, keepdims=True)
    exp_terms = jnp.exp(scores - row_max)
    weights = (exp_terms / jnp.sum(exp_terms, axis=2, keepdims=True)).astype(jnp.bfloat16)
    split_at = cache_keys.shape[0]
    attended = jnp.einsum(
        "hqk,khd->qhd", weights[:, :, :split_at], cache_vals, preferred_element_type=jnp.float32
    )
    attended = attended + jnp.einsum(
        "hqk,khd->qhd", weights[:, :, split_at:], fresh_vals, preferred_element_type=jnp.float32
    )
    return attended.astype(jnp.bfloat16).reshape(row_count, head_count * head_size)


def local(
    hidden_in, levels, order, cache_mask, finished, cache_kv, modulation, w_qkv, w_out, w_up, w_down
):
    span_index = lax.axis_index("span")
    tp_rank = lax.axis_index("tp")
    span_count = lax.psum(1, "span")
    tp_count = lax.psum(1, "tp")
    model_width = modulation.shape[2]
    share_width = hidden_in.shape[2]
    local_count = hidden_in.shape[0]
    row_count = hidden_in.shape[1]
    token_count = local_count * row_count
    gather_weights = (
        tp_count * w_out.size * w_out.dtype.itemsize <= WEIGHT_GATHER_BYTES and span_count == 2
    )
    if gather_weights:
        cycle = snake_cycle(tp_count)
        position = jnp.array([cycle.index(t) for t in range(tp_count)], jnp.int32)[tp_rank]
        steps = list(range(tp_count // 2 + 1)) + [-k for k in range(1, (tp_count - 1) // 2 + 1)]
        owners = jnp.array(cycle, jnp.int32)
        gathered = jnp.zeros(hidden_in.shape[:2] + (model_width,), hidden_in.dtype)
        for step, piece in zip(steps, ring_gather(hidden_in, "tp", tp_count)):
            owner = owners[(position - step + tp_count) % tp_count]
            gathered = lax.dynamic_update_slice_in_dim(gathered, piece, owner * share_width, 2)
        gathered_narrow = gathered
        gathered = gathered.astype(jnp.float32)
    else:
        gathered = lax.all_gather(hidden_in, "tp", axis=2, tiled=True).astype(jnp.float32)
    if gather_weights:
        column_part = model_width // span_count
        w_out_part = lax.dynamic_slice_in_dim(w_out, span_index * column_part, column_part, 1)
        mine_blocks = ring_gather(w_out_part, "tp", tp_count)
        both_halves = lax.all_gather(jnp.stack(mine_blocks), "span", axis=0)
    up_full, down_full = (
        lax.all_gather(w_up, "span", axis=1, tiled=True),
        lax.all_gather(w_down, "span", axis=0, tiled=True),
    )
    mod_table = modulation.reshape(modulation.shape[0], -1)
    picker = (jnp.arange(mod_table.shape[0], dtype=jnp.int32)[None, :] == levels[:, None]).astype(
        jnp.bfloat16
    )
    mod_rows = jnp.dot(picker, mod_table, preferred_element_type=jnp.float32).reshape(
        local_count, 6, model_width
    )
    attn_in = (normalize(gathered) * mod_rows[:, 1][:, None] + mod_rows[:, 0][:, None]).astype(
        jnp.bfloat16
    )
    per_device = w_qkv.shape[2]
    projected = jnp.dot(
        attn_in.reshape(token_count, model_width),
        w_qkv.reshape(model_width, -1),
        preferred_element_type=jnp.float32,
    )
    projected = projected.astype(jnp.bfloat16).reshape(local_count, row_count, 3, per_device)
    queries = projected[:, :, 0].reshape(local_count, row_count, -1, HEAD_DIM)
    fresh_kv = projected[:, :, 1:]
    cache_all, fresh_all = (
        lax.all_gather(cache_kv, "span", axis=0, tiled=True),
        lax.all_gather(fresh_kv, "span", axis=0, tiled=True),
    )
    positions = jnp.arange(cache_mask.shape[0], dtype=jnp.int32)
    my_spans = span_index * local_count + jnp.arange(local_count, dtype=jnp.int32)
    mask_rows = jax.vmap(lambda target: select_row(cache_mask, target))(my_spans)
    my_order = jax.vmap(lambda target: select_row(order, target))(my_spans)
    cache_seen = jnp.repeat(
        (mask_rows == 1) | (positions[None, :] == finished[0]), row_count, axis=1
    )
    fresh_seen = jnp.repeat(order[None, :] <= my_order[:, None], row_count, axis=1)
    attended = jax.vmap(
        lambda q_rows, c_seen, f_seen: attend(q_rows, cache_all, fresh_all, c_seen, f_seen)
    )(queries, cache_seen, fresh_seen)
    if gather_weights:
        att_blocks = ring_gather(attended.reshape(token_count, per_device), "tp", tp_count)
        residual_rows, square_sums = grouped_out_proj(
            span_index,
            att_blocks,
            mine_blocks,
            both_halves,
            gathered_narrow.reshape(token_count, model_width),
            mod_rows[:, 2],
        )
        residual_full = residual_rows.reshape(local_count, row_count, model_width)
        inverse = lax.rsqrt(square_sums.reshape(local_count, row_count, 1) / model_width + EPSILON)
        mlp_in = (
            residual_full * inverse * mod_rows[:, 4][:, None] + mod_rows[:, 3][:, None]
        ).astype(jnp.bfloat16)
    else:
        partial_value = jnp.dot(
            attended.reshape(token_count, -1), w_out, preferred_element_type=jnp.float32
        ).reshape(local_count, row_count, model_width)
        attn_part = lax.psum_scatter(
            partial_value.astype(jnp.bfloat16), "tp", scatter_dimension=2, tiled=True
        ).astype(jnp.float32)
        mod_share = lax.dynamic_slice_in_dim(mod_rows, tp_rank * share_width, share_width, 2)
        residual = hidden_in.astype(jnp.float32) + mod_share[:, 2][:, None] * attn_part
        squares = lax.psum(jnp.sum(residual * residual, axis=2), "tp")
        scaled = residual * lax.rsqrt(squares / model_width + EPSILON)[:, :, None]
        mlp_part = (scaled * mod_share[:, 4][:, None] + mod_share[:, 3][:, None]).astype(
            jnp.bfloat16
        )
        mlp_in = lax.all_gather(mlp_part, "tp", axis=2, tiled=True)
    pre_act = jnp.dot(mlp_in, up_full, preferred_element_type=jnp.float32)
    hidden_units = jax.nn.gelu(pre_act).astype(jnp.bfloat16)
    down_terms = jnp.dot(hidden_units, down_full, preferred_element_type=jnp.float32)
    if gather_weights:
        mlp_out = ring_reduce_scatter(
            down_terms.reshape(token_count, model_width), "tp", tp_count
        ).reshape(local_count, row_count, share_width)
    else:
        mlp_out = lax.psum_scatter(
            down_terms.astype(jnp.bfloat16), "tp", scatter_dimension=2, tiled=True
        ).astype(jnp.float32)
    if gather_weights:
        residual = lax.dynamic_slice_in_dim(residual_full, tp_rank * share_width, share_width, 2)
        mod_share = lax.dynamic_slice_in_dim(mod_rows, tp_rank * share_width, share_width, 2)
    result = residual + mod_share[:, 5][:, None] * mlp_out
    return result.astype(jnp.bfloat16)


def solution(mesh):
    placed = (
        P(("rep", "span"), None, "tp"),
        P(("rep", "span")),
        P("rep"),
        P("rep", None),
        P("rep"),
        P(("rep", "span"), None, None, "tp"),
        P(),
        P(None, None, "tp"),
        P("tp", None),
        P(None, ("span", "tp")),
        P(("span", "tp"), None),
    )
    return jax.shard_map(
        local, mesh=mesh, in_specs=placed, out_specs=P(("rep", "span"), None, "tp"), check_vma=False
    )
```

```python
import functools
import math

import jax
import jax.numpy as jnp
from jax import lax
from jax.experimental import pallas as pl
from jax.experimental.pallas import tpu as pltpu
from jax.sharding import PartitionSpec as P

HEAD_DIM = 128


EPSILON = 1e-06
NEGATIVE = -1e30
WEIGHT_GATHER_BYTES = 24 * 2**20


def normalize(values):
    return values * lax.rsqrt(jnp.mean(values * values, axis=-1, keepdims=True) + EPSILON)


def snake_cycle(count):
    return list(range(0, count, 2)) + list(range(count - 1, 0, -2)) if count % 2 == 0 else list(range(count))


def ring_gather(block, axis_name, count):
    cycle = snake_cycle(count)
    ahead = [(cycle[p], cycle[(p + 1) % count]) for p in range(count)]
    behind = [(cycle[p], cycle[(p - 1) % count]) for p in range(count)]
    blocks = [block]
    forward = block
    for _ in range(count // 2):
        forward = lax.ppermute(forward, axis_name, ahead)
        blocks.append(forward)
    backward = block
    for _ in range((count - 1) // 2):
        backward = lax.ppermute(backward, axis_name, behind)
        blocks.append(backward)
    return blocks


def ring_reduce_scatter(terms, axis_name, count):
    token_count, width = terms.shape
    block = width // count
    half = block // 2
    cycle = snake_cycle(count)
    position = jnp.array([cycle.index(t) for t in range(count)], jnp.int32)[lax.axis_index(axis_name)]
    owners = jnp.array(cycle, jnp.int32)
    rounded = terms.astype(jnp.bfloat16)

    def own_part(slot, side):
        start = owners[slot % count] * block + side * half
        return lax.dynamic_slice_in_dim(rounded, start, half, 1).astype(jnp.float32)

    ahead = [(cycle[p], cycle[(p + 1) % count]) for p in range(count)]
    behind = [(cycle[p], cycle[(p - 1) % count]) for p in range(count)]
    forward = own_part(position - 1 + count, 0)
    backward = own_part(position + 1, 1)
    for step in range(count - 1):
        forward = lax.ppermute(forward.astype(jnp.bfloat16), axis_name, ahead).astype(jnp.float32)
        forward = forward + own_part(position - 2 - step + 2 * count, 0)
        backward = lax.ppermute(backward.astype(jnp.bfloat16), axis_name, behind).astype(jnp.float32)
        backward = backward + own_part(position + 2 + step, 1)
    return jnp.concatenate([forward, backward], axis=1)


def out_proj_kernel(group_count, tiles_per_half, row_count, span_ref, *refs):
    att_refs = refs[:group_count]
    mine_refs = refs[group_count:2 * group_count]
    other_refs = refs[2 * group_count:3 * group_count]
    hidden_ref, scale_ref, out_ref, squares_ref = refs[3 * group_count:]
    tile = pl.program_id(0)

    def accumulate(w_refs):
        total = None
        for group in range(group_count):
            term = jnp.dot(att_refs[group][...], w_refs[group][...], preferred_element_type=jnp.float32)
            term = term.astype(jnp.bfloat16).astype(jnp.float32)
            total = term if total is None else total + term
        for span in range(scale_ref.shape[0]):
            rows = slice(span * row_count, (span + 1) * row_count)
            out_ref[rows, :] = (
                hidden_ref[rows, :].astype(jnp.float32) + scale_ref[span:span + 1, :] * total[rows, :]
            )
        result = out_ref[...]
        partial = jnp.broadcast_to(jnp.sum(result * result, axis=1, keepdims=True), squares_ref.shape)

        @pl.when(tile == 0)
        def _():
            squares_ref[...] = partial

        @pl.when(tile > 0)
        def _():
            squares_ref[...] += partial

    @pl.when(tile < tiles_per_half)
    def _():
        accumulate(mine_refs)

    @pl.when(tile >= tiles_per_half)
    def _():
        accumulate(other_refs)


def grouped_out_proj(
    span_index, att_blocks, mine_blocks, other_blocks, hidden, scale, tile_width=1024
):
    group_count = len(att_blocks)
    token_count, head_width = att_blocks[0].shape
    half_width = mine_blocks[0].shape[1]
    span_rows = scale.shape[0]
    tile_width = min(tile_width, half_width)
    tiles_per_half = half_width // tile_width
    att_spec = pl.BlockSpec((token_count, head_width), lambda n, s: (0, 0))
    mine_spec = pl.BlockSpec(
        (head_width, tile_width), lambda n, s: (0, jnp.minimum(n, tiles_per_half - 1))
    )
    other_spec = pl.BlockSpec(
        (head_width, tile_width), lambda n, s: (0, jnp.maximum(n - tiles_per_half, 0))
    )

    def column(n, s):
        return ((n // tiles_per_half + s[0]) % 2) * tiles_per_half + n % tiles_per_half

    out_spec = pl.BlockSpec((token_count, tile_width), lambda n, s: (0, column(n, s)))
    hidden_spec = pl.BlockSpec((token_count, tile_width), lambda n, s: (0, column(n, s)))
    scale_spec = pl.BlockSpec((span_rows, tile_width), lambda n, s: (0, column(n, s)))
    squares_spec = pl.BlockSpec((token_count, 128), lambda n, s: (0, 0))
    tile_count = 2 * tiles_per_half
    flops = 2 * token_count * head_width * group_count * half_width * 2
    moved = 2 * (group_count * token_count * head_width + 2 * group_count * head_width * half_width)
    moved += token_count * 2 * half_width * (4 + 2)
    residual, squares = pl.pallas_call(
        functools.partial(out_proj_kernel, group_count, tiles_per_half, token_count // span_rows),
        out_shape=(
            jax.ShapeDtypeStruct((token_count, 2 * half_width), jnp.float32),
            jax.ShapeDtypeStruct((token_count, 128), jnp.float32),
        ),
        grid_spec=pltpu.PrefetchScalarGridSpec(
            num_scalar_prefetch=1,
            grid=(tile_count,),
            in_specs=[att_spec] * group_count + [mine_spec] * group_count + [other_spec] * group_count
            + [hidden_spec, scale_spec],
            out_specs=[out_spec, squares_spec],
        ),
        cost_estimate=pl.CostEstimate(flops=flops, bytes_accessed=moved, transcendentals=0),
    )(
        jnp.reshape(span_index, (1,)).astype(jnp.int32),
        *att_blocks,
        *mine_blocks,
        *other_blocks,
        hidden,
        scale,
    )
    return residual, squares[:, 0]


def select_row(source, target):
    matches = jnp.arange(source.shape[0], dtype=jnp.int32) == target
    return jnp.sum(jnp.where(matches.reshape((-1,) + (1,) * (source.ndim - 1)), source, 0), axis=0)


def attend(queries, cache_all, fresh_all, cache_seen, fresh_seen):
    row_count, head_count, head_size = queries.shape
    cache_keys = cache_all[:, :, 0].reshape(-1, head_count, head_size)
    cache_vals = cache_all[:, :, 1].reshape(-1, head_count, head_size)
    fresh_keys = fresh_all[:, :, 0].reshape(-1, head_count, head_size)
    fresh_vals = fresh_all[:, :, 1].reshape(-1, head_count, head_size)
    score_scale = 1.0 / math.sqrt(head_size)
    cache_scores = (
        jnp.einsum("qhd,khd->hqk", queries, cache_keys, preferred_element_type=jnp.float32)
        * score_scale
    )
    fresh_scores = (
        jnp.einsum("qhd,khd->hqk", queries, fresh_keys, preferred_element_type=jnp.float32)
        * score_scale
    )
    cache_scores = jnp.where(cache_seen[None, None, :], cache_scores, NEGATIVE)
    fresh_scores = jnp.where(fresh_seen[None, None, :], fresh_scores, NEGATIVE)
    scores = jnp.concatenate([cache_scores, fresh_scores], axis=2)
    row_max = jnp.max(scores, axis=2, keepdims=True)
    exp_terms = jnp.exp(scores - row_max)
    weights = (exp_terms / jnp.sum(exp_terms, axis=2, keepdims=True)).astype(jnp.bfloat16)
    split_at = cache_keys.shape[0]
    attended = jnp.einsum(
        "hqk,khd->qhd", weights[:, :, :split_at], cache_vals, preferred_element_type=jnp.float32
    )
    attended = attended + jnp.einsum(
        "hqk,khd->qhd", weights[:, :, split_at:], fresh_vals, preferred_element_type=jnp.float32
    )
    return attended.astype(jnp.bfloat16).reshape(row_count, head_count * head_size)


def local(
    hidden_in, levels, order, cache_mask, finished, cache_kv, modulation, w_qkv, w_out, w_up, w_down
):
    span_index = lax.axis_index("span")
    tp_rank = lax.axis_index("tp")
    span_count = lax.psum(1, "span")
    tp_count = lax.psum(1, "tp")
    model_width = modulation.shape[2]
    share_width = hidden_in.shape[2]
    local_count = hidden_in.shape[0]
    row_count = hidden_in.shape[1]
    token_count = local_count * row_count
    gather_weights = (
        tp_count * w_out.size * w_out.dtype.itemsize <= WEIGHT_GATHER_BYTES and span_count == 2
    )
    if gather_weights:
        cycle = snake_cycle(tp_count)
        position = jnp.array([cycle.index(t) for t in range(tp_count)], jnp.int32)[tp_rank]
        steps = list(range(tp_count // 2 + 1)) + [-k for k in range(1, (tp_count - 1) // 2 + 1)]
        owners = jnp.array(cycle, jnp.int32)
        gathered = jnp.zeros(hidden_in.shape[:2] + (model_width,), hidden_in.dtype)
        for step, piece in zip(steps, ring_gather(hidden_in, "tp", tp_count)):
            owner = owners[(position - step + tp_count) % tp_count]
            gathered = lax.dynamic_update_slice_in_dim(gathered, piece, owner * share_width, 2)
        gathered_narrow = gathered
        gathered = gathered.astype(jnp.float32)
    else:
        gathered = lax.all_gather(hidden_in, "tp", axis=2, tiled=True).astype(jnp.float32)
    if gather_weights:
        column_part = model_width // span_count
        w_out_part = lax.dynamic_slice_in_dim(w_out, span_index * column_part, column_part, 1)
        mine_blocks = ring_gather(w_out_part, "tp", tp_count)
        other_blocks = [lax.ppermute(b, "span", [(0, 1), (1, 0)]) for b in mine_blocks]
    if gather_weights:
        swap = [(0, 1), (1, 0)]
        up_full = jnp.concatenate([w_up, lax.ppermute(w_up, "span", swap)], axis=1)
        down_full = jnp.concatenate([w_down, lax.ppermute(w_down, "span", swap)], axis=0)
    else:
        up_full, down_full = (
            lax.all_gather(w_up, "span", axis=1, tiled=True),
            lax.all_gather(w_down, "span", axis=0, tiled=True),
        )
    mod_table = modulation.reshape(modulation.shape[0], -1)
    picker = (jnp.arange(mod_table.shape[0], dtype=jnp.int32)[None, :] == levels[:, None]).astype(
        jnp.bfloat16
    )
    mod_rows = jnp.dot(picker, mod_table, preferred_element_type=jnp.float32).reshape(
        local_count, 6, model_width
    )
    attn_in = (normalize(gathered) * mod_rows[:, 1][:, None] + mod_rows[:, 0][:, None]).astype(
        jnp.bfloat16
    )
    per_device = w_qkv.shape[2]
    projected = jnp.dot(
        attn_in.reshape(token_count, model_width),
        w_qkv.reshape(model_width, -1),
        preferred_element_type=jnp.float32,
    )
    projected = projected.astype(jnp.bfloat16).reshape(local_count, row_count, 3, per_device)
    queries = projected[:, :, 0].reshape(local_count, row_count, -1, HEAD_DIM)
    fresh_kv = projected[:, :, 1:]
    cache_all, fresh_all = (
        lax.all_gather(cache_kv, "span", axis=0, tiled=True),
        lax.all_gather(fresh_kv, "span", axis=0, tiled=True),
    )
    positions = jnp.arange(cache_mask.shape[0], dtype=jnp.int32)
    my_spans = span_index * local_count + jnp.arange(local_count, dtype=jnp.int32)
    mask_rows = jax.vmap(lambda target: select_row(cache_mask, target))(my_spans)
    my_order = jax.vmap(lambda target: select_row(order, target))(my_spans)
    cache_seen = jnp.repeat(
        (mask_rows == 1) | (positions[None, :] == finished[0]), row_count, axis=1
    )
    fresh_seen = jnp.repeat(order[None, :] <= my_order[:, None], row_count, axis=1)
    attended = jax.vmap(
        lambda q_rows, c_seen, f_seen: attend(q_rows, cache_all, fresh_all, c_seen, f_seen)
    )(queries, cache_seen, fresh_seen)
    if gather_weights:
        att_blocks = ring_gather(attended.reshape(token_count, per_device), "tp", tp_count)
        residual_rows, square_sums = grouped_out_proj(
            span_index,
            att_blocks,
            mine_blocks,
            other_blocks,
            gathered_narrow.reshape(token_count, model_width),
            mod_rows[:, 2],
        )
        residual_full = residual_rows.reshape(local_count, row_count, model_width)
        inverse = lax.rsqrt(square_sums.reshape(local_count, row_count, 1) / model_width + EPSILON)
        mlp_in = (
            residual_full * inverse * mod_rows[:, 4][:, None] + mod_rows[:, 3][:, None]
        ).astype(jnp.bfloat16)
    else:
        partial_value = jnp.dot(
            attended.reshape(token_count, -1), w_out, preferred_element_type=jnp.float32
        ).reshape(local_count, row_count, model_width)
        attn_part = lax.psum_scatter(
            partial_value.astype(jnp.bfloat16), "tp", scatter_dimension=2, tiled=True
        ).astype(jnp.float32)
        mod_share = lax.dynamic_slice_in_dim(mod_rows, tp_rank * share_width, share_width, 2)
        residual = hidden_in.astype(jnp.float32) + mod_share[:, 2][:, None] * attn_part
        squares = lax.psum(jnp.sum(residual * residual, axis=2), "tp")
        scaled = residual * lax.rsqrt(squares / model_width + EPSILON)[:, :, None]
        mlp_part = (scaled * mod_share[:, 4][:, None] + mod_share[:, 3][:, None]).astype(
            jnp.bfloat16
        )
        mlp_in = lax.all_gather(mlp_part, "tp", axis=2, tiled=True)
    pre_act = jnp.dot(mlp_in, up_full, preferred_element_type=jnp.float32)
    hidden_units = jax.nn.gelu(pre_act).astype(jnp.bfloat16)
    down_terms = jnp.dot(hidden_units, down_full, preferred_element_type=jnp.float32)
    if gather_weights:
        mlp_out = ring_reduce_scatter(
            down_terms.reshape(token_count, model_width), "tp", tp_count
        ).reshape(local_count, row_count, share_width)
    else:
        mlp_out = lax.psum_scatter(
            down_terms.astype(jnp.bfloat16), "tp", scatter_dimension=2, tiled=True
        ).astype(jnp.float32)
    if gather_weights:
        residual = lax.dynamic_slice_in_dim(residual_full, tp_rank * share_width, share_width, 2)
        mod_share = lax.dynamic_slice_in_dim(mod_rows, tp_rank * share_width, share_width, 2)
    result = residual + mod_share[:, 5][:, None] * mlp_out
    return result.astype(jnp.bfloat16)


def solution(mesh):
    placed = (
        P(("rep", "span"), None, "tp"),
        P(("rep", "span")),
        P("rep"),
        P("rep", None),
        P("rep"),
        P(("rep", "span"), None, None, "tp"),
        P(),
        P(None, None, "tp"),
        P("tp", None),
        P(None, ("span", "tp")),
        P(("span", "tp"), None),
    )
    return jax.shard_map(
        local, mesh=mesh, in_specs=placed, out_specs=P(("rep", "span"), None, "tp"), check_vma=False
    )
```

```python
import functools
import math

import jax
import jax.numpy as jnp
from jax import lax
from jax.experimental import pallas as pl
from jax.experimental.pallas import tpu as pltpu
from jax.sharding import PartitionSpec as P

HEAD_DIM = 128


EPSILON = 1e-06
NEGATIVE = -1e30
WEIGHT_GATHER_BYTES = 24 * 2**20


def normalize(values):
    return values * lax.rsqrt(jnp.mean(values * values, axis=-1, keepdims=True) + EPSILON)


def snake_cycle(count):
    return list(range(0, count, 2)) + list(range(count - 1, 0, -2)) if count % 2 == 0 else list(range(count))


def ring_gather(block, axis_name, count):
    cycle = snake_cycle(count)
    ahead = [(cycle[p], cycle[(p + 1) % count]) for p in range(count)]
    behind = [(cycle[p], cycle[(p - 1) % count]) for p in range(count)]
    blocks = [block]
    forward = block
    for _ in range(count // 2):
        forward = lax.ppermute(forward, axis_name, ahead)
        blocks.append(forward)
    backward = block
    for _ in range((count - 1) // 2):
        backward = lax.ppermute(backward, axis_name, behind)
        blocks.append(backward)
    return blocks


def ring_reduce_scatter(terms, axis_name, count):
    token_count, width = terms.shape
    block = width // count
    half = block // 2
    cycle = snake_cycle(count)
    position = jnp.array([cycle.index(t) for t in range(count)], jnp.int32)[lax.axis_index(axis_name)]
    owners = jnp.array(cycle, jnp.int32)
    rounded = terms.astype(jnp.bfloat16)

    def own_part(slot, side):
        start = owners[slot % count] * block + side * half
        return lax.dynamic_slice_in_dim(rounded, start, half, 1).astype(jnp.float32)

    ahead = [(cycle[p], cycle[(p + 1) % count]) for p in range(count)]
    behind = [(cycle[p], cycle[(p - 1) % count]) for p in range(count)]
    forward = own_part(position - 1 + count, 0)
    backward = own_part(position + 1, 1)
    for step in range(count - 1):
        forward = lax.ppermute(forward.astype(jnp.bfloat16), axis_name, ahead).astype(jnp.float32)
        forward = forward + own_part(position - 2 - step + 2 * count, 0)
        backward = lax.ppermute(backward.astype(jnp.bfloat16), axis_name, behind).astype(jnp.float32)
        backward = backward + own_part(position + 2 + step, 1)
    return jnp.concatenate([forward, backward], axis=1)


def out_proj_kernel(group_count, tiles_per_half, row_count, span_ref, *refs):
    att_refs = refs[:group_count]
    mine_refs = refs[group_count:2 * group_count]
    other_refs = refs[2 * group_count:3 * group_count]
    hidden_ref, scale_ref, out_ref, squares_ref = refs[3 * group_count:]
    tile = pl.program_id(0)

    def accumulate(w_refs):
        total = None
        for group in range(group_count):
            term = jnp.dot(att_refs[group][...], w_refs[group][...], preferred_element_type=jnp.float32)
            term = term.astype(jnp.bfloat16).astype(jnp.float32)
            total = term if total is None else total + term
        for span in range(scale_ref.shape[0]):
            rows = slice(span * row_count, (span + 1) * row_count)
            out_ref[rows, :] = (
                hidden_ref[rows, :].astype(jnp.float32) + scale_ref[span:span + 1, :] * total[rows, :]
            )
        result = out_ref[...]
        partial = jnp.broadcast_to(jnp.sum(result * result, axis=1, keepdims=True), squares_ref.shape)

        @pl.when(tile == 0)
        def _():
            squares_ref[...] = partial

        @pl.when(tile > 0)
        def _():
            squares_ref[...] += partial

    @pl.when(tile < tiles_per_half)
    def _():
        accumulate(mine_refs)

    @pl.when(tile >= tiles_per_half)
    def _():
        accumulate(other_refs)


def grouped_out_proj(
    span_index, att_blocks, mine_blocks, other_blocks, hidden, scale, tile_width=1024
):
    group_count = len(att_blocks)
    token_count, head_width = att_blocks[0].shape
    half_width = mine_blocks[0].shape[1]
    span_rows = scale.shape[0]
    tile_width = min(tile_width, half_width)
    tiles_per_half = half_width // tile_width
    att_spec = pl.BlockSpec((token_count, head_width), lambda n, s: (0, 0))
    mine_spec = pl.BlockSpec(
        (head_width, tile_width), lambda n, s: (0, jnp.minimum(n, tiles_per_half - 1))
    )
    other_spec = pl.BlockSpec(
        (head_width, tile_width), lambda n, s: (0, jnp.maximum(n - tiles_per_half, 0))
    )

    def column(n, s):
        return ((n // tiles_per_half + s[0]) % 2) * tiles_per_half + n % tiles_per_half

    out_spec = pl.BlockSpec((token_count, tile_width), lambda n, s: (0, column(n, s)))
    hidden_spec = pl.BlockSpec((token_count, tile_width), lambda n, s: (0, column(n, s)))
    scale_spec = pl.BlockSpec((span_rows, tile_width), lambda n, s: (0, column(n, s)))
    squares_spec = pl.BlockSpec((token_count, 128), lambda n, s: (0, 0))
    tile_count = 2 * tiles_per_half
    flops = 2 * token_count * head_width * group_count * half_width * 2
    moved = 2 * (group_count * token_count * head_width + 2 * group_count * head_width * half_width)
    moved += token_count * 2 * half_width * (4 + 2)
    residual, squares = pl.pallas_call(
        functools.partial(out_proj_kernel, group_count, tiles_per_half, token_count // span_rows),
        out_shape=(
            jax.ShapeDtypeStruct((token_count, 2 * half_width), jnp.float32),
            jax.ShapeDtypeStruct((token_count, 128), jnp.float32),
        ),
        grid_spec=pltpu.PrefetchScalarGridSpec(
            num_scalar_prefetch=1,
            grid=(tile_count,),
            in_specs=[att_spec] * group_count + [mine_spec] * group_count + [other_spec] * group_count
            + [hidden_spec, scale_spec],
            out_specs=[out_spec, squares_spec],
        ),
        cost_estimate=pl.CostEstimate(flops=flops, bytes_accessed=moved, transcendentals=0),
    )(
        jnp.reshape(span_index, (1,)).astype(jnp.int32),
        *att_blocks,
        *mine_blocks,
        *other_blocks,
        hidden,
        scale,
    )
    return residual, squares[:, 0]


def select_row(source, target):
    matches = jnp.arange(source.shape[0], dtype=jnp.int32) == target
    return jnp.sum(jnp.where(matches.reshape((-1,) + (1,) * (source.ndim - 1)), source, 0), axis=0)


def attend(queries, cache_all, fresh_all, cache_seen, fresh_seen):
    row_count, head_count, head_size = queries.shape
    cache_keys = cache_all[:, :, 0].reshape(-1, head_count, head_size)
    cache_vals = cache_all[:, :, 1].reshape(-1, head_count, head_size)
    fresh_keys = fresh_all[:, :, 0].reshape(-1, head_count, head_size)
    fresh_vals = fresh_all[:, :, 1].reshape(-1, head_count, head_size)
    score_scale = 1.0 / math.sqrt(head_size)
    cache_scores = (
        jnp.einsum("qhd,khd->hqk", queries, cache_keys, preferred_element_type=jnp.float32)
        * score_scale
    )
    fresh_scores = (
        jnp.einsum("qhd,khd->hqk", queries, fresh_keys, preferred_element_type=jnp.float32)
        * score_scale
    )
    cache_scores = jnp.where(cache_seen[None, None, :], cache_scores, NEGATIVE)
    fresh_scores = jnp.where(fresh_seen[None, None, :], fresh_scores, NEGATIVE)
    scores = jnp.concatenate([cache_scores, fresh_scores], axis=2)
    row_max = jnp.max(scores, axis=2, keepdims=True)
    exp_terms = jnp.exp(scores - row_max)
    weights = (exp_terms / jnp.sum(exp_terms, axis=2, keepdims=True)).astype(jnp.bfloat16)
    split_at = cache_keys.shape[0]
    attended = jnp.einsum(
        "hqk,khd->qhd", weights[:, :, :split_at], cache_vals, preferred_element_type=jnp.float32
    )
    attended = attended + jnp.einsum(
        "hqk,khd->qhd", weights[:, :, split_at:], fresh_vals, preferred_element_type=jnp.float32
    )
    return attended.astype(jnp.bfloat16).reshape(row_count, head_count * head_size)


def local(
    hidden_in, levels, order, cache_mask, finished, cache_kv, modulation, w_qkv, w_out, w_up, w_down
):
    span_index = lax.axis_index("span")
    tp_rank = lax.axis_index("tp")
    span_count = lax.psum(1, "span")
    tp_count = lax.psum(1, "tp")
    model_width = modulation.shape[2]
    share_width = hidden_in.shape[2]
    local_count = hidden_in.shape[0]
    row_count = hidden_in.shape[1]
    token_count = local_count * row_count
    gather_weights = (
        tp_count * w_out.size * w_out.dtype.itemsize <= WEIGHT_GATHER_BYTES and span_count == 2
    )
    if gather_weights:
        cycle = snake_cycle(tp_count)
        position = jnp.array([cycle.index(t) for t in range(tp_count)], jnp.int32)[tp_rank]
        steps = list(range(tp_count // 2 + 1)) + [-k for k in range(1, (tp_count - 1) // 2 + 1)]
        owners = jnp.array(cycle, jnp.int32)
        gathered = jnp.zeros(hidden_in.shape[:2] + (model_width,), hidden_in.dtype)
        for step, piece in zip(steps, ring_gather(hidden_in, "tp", tp_count)):
            owner = owners[(position - step + tp_count) % tp_count]
            gathered = lax.dynamic_update_slice_in_dim(gathered, piece, owner * share_width, 2)
        gathered_narrow = gathered
        gathered = gathered.astype(jnp.float32)
    else:
        gathered = lax.all_gather(hidden_in, "tp", axis=2, tiled=True).astype(jnp.float32)
    if gather_weights:
        column_part = model_width // span_count
        w_out_part = lax.dynamic_slice_in_dim(w_out, span_index * column_part, column_part, 1)
        mine_blocks = ring_gather(w_out_part, "tp", tp_count)
        other_blocks = [lax.ppermute(b, "span", [(0, 1), (1, 0)]) for b in mine_blocks]
    if gather_weights:
        swap = [(0, 1), (1, 0)]
        up_full = jnp.concatenate([w_up, lax.ppermute(w_up, "span", swap)], axis=1)
        down_full = jnp.concatenate([w_down, lax.ppermute(w_down, "span", swap)], axis=0)
        gathered_narrow, up_full, down_full = lax.optimization_barrier(
            (gathered_narrow, up_full, down_full)
        )
        gathered = gathered_narrow.astype(jnp.float32)
    else:
        up_full, down_full = (
            lax.all_gather(w_up, "span", axis=1, tiled=True),
            lax.all_gather(w_down, "span", axis=0, tiled=True),
        )
    mod_table = modulation.reshape(modulation.shape[0], -1)
    picker = (jnp.arange(mod_table.shape[0], dtype=jnp.int32)[None, :] == levels[:, None]).astype(
        jnp.bfloat16
    )
    mod_rows = jnp.dot(picker, mod_table, preferred_element_type=jnp.float32).reshape(
        local_count, 6, model_width
    )
    attn_in = (normalize(gathered) * mod_rows[:, 1][:, None] + mod_rows[:, 0][:, None]).astype(
        jnp.bfloat16
    )
    per_device = w_qkv.shape[2]
    projected = jnp.dot(
        attn_in.reshape(token_count, model_width),
        w_qkv.reshape(model_width, -1),
        preferred_element_type=jnp.float32,
    )
    projected = projected.astype(jnp.bfloat16).reshape(local_count, row_count, 3, per_device)
    queries = projected[:, :, 0].reshape(local_count, row_count, -1, HEAD_DIM)
    fresh_kv = projected[:, :, 1:]
    cache_all, fresh_all = (
        lax.all_gather(cache_kv, "span", axis=0, tiled=True),
        lax.all_gather(fresh_kv, "span", axis=0, tiled=True),
    )
    positions = jnp.arange(cache_mask.shape[0], dtype=jnp.int32)
    my_spans = span_index * local_count + jnp.arange(local_count, dtype=jnp.int32)
    mask_rows = jax.vmap(lambda target: select_row(cache_mask, target))(my_spans)
    my_order = jax.vmap(lambda target: select_row(order, target))(my_spans)
    cache_seen = jnp.repeat(
        (mask_rows == 1) | (positions[None, :] == finished[0]), row_count, axis=1
    )
    fresh_seen = jnp.repeat(order[None, :] <= my_order[:, None], row_count, axis=1)
    attended = jax.vmap(
        lambda q_rows, c_seen, f_seen: attend(q_rows, cache_all, fresh_all, c_seen, f_seen)
    )(queries, cache_seen, fresh_seen)
    if gather_weights:
        att_blocks = ring_gather(attended.reshape(token_count, per_device), "tp", tp_count)
        residual_rows, square_sums = grouped_out_proj(
            span_index,
            att_blocks,
            mine_blocks,
            other_blocks,
            gathered_narrow.reshape(token_count, model_width),
            mod_rows[:, 2],
        )
        residual_full = residual_rows.reshape(local_count, row_count, model_width)
        inverse = lax.rsqrt(square_sums.reshape(local_count, row_count, 1) / model_width + EPSILON)
        mlp_in = (
            residual_full * inverse * mod_rows[:, 4][:, None] + mod_rows[:, 3][:, None]
        ).astype(jnp.bfloat16)
    else:
        partial_value = jnp.dot(
            attended.reshape(token_count, -1), w_out, preferred_element_type=jnp.float32
        ).reshape(local_count, row_count, model_width)
        attn_part = lax.psum_scatter(
            partial_value.astype(jnp.bfloat16), "tp", scatter_dimension=2, tiled=True
        ).astype(jnp.float32)
        mod_share = lax.dynamic_slice_in_dim(mod_rows, tp_rank * share_width, share_width, 2)
        residual = hidden_in.astype(jnp.float32) + mod_share[:, 2][:, None] * attn_part
        squares = lax.psum(jnp.sum(residual * residual, axis=2), "tp")
        scaled = residual * lax.rsqrt(squares / model_width + EPSILON)[:, :, None]
        mlp_part = (scaled * mod_share[:, 4][:, None] + mod_share[:, 3][:, None]).astype(
            jnp.bfloat16
        )
        mlp_in = lax.all_gather(mlp_part, "tp", axis=2, tiled=True)
    pre_act = jnp.dot(mlp_in, up_full, preferred_element_type=jnp.float32)
    hidden_units = jax.nn.gelu(pre_act).astype(jnp.bfloat16)
    down_terms = jnp.dot(hidden_units, down_full, preferred_element_type=jnp.float32)
    if gather_weights:
        mlp_out = ring_reduce_scatter(
            down_terms.reshape(token_count, model_width), "tp", tp_count
        ).reshape(local_count, row_count, share_width)
    else:
        mlp_out = lax.psum_scatter(
            down_terms.astype(jnp.bfloat16), "tp", scatter_dimension=2, tiled=True
        ).astype(jnp.float32)
    if gather_weights:
        residual = lax.dynamic_slice_in_dim(residual_full, tp_rank * share_width, share_width, 2)
        mod_share = lax.dynamic_slice_in_dim(mod_rows, tp_rank * share_width, share_width, 2)
    result = residual + mod_share[:, 5][:, None] * mlp_out
    return result.astype(jnp.bfloat16)


def solution(mesh):
    placed = (
        P(("rep", "span"), None, "tp"),
        P(("rep", "span")),
        P("rep"),
        P("rep", None),
        P("rep"),
        P(("rep", "span"), None, None, "tp"),
        P(),
        P(None, None, "tp"),
        P("tp", None),
        P(None, ("span", "tp")),
        P(("span", "tp"), None),
    )
    return jax.shard_map(
        local, mesh=mesh, in_specs=placed, out_specs=P(("rep", "span"), None, "tp"), check_vma=False
    )
```

```python
import functools
import math

import jax
import jax.numpy as jnp
from jax import lax
from jax.experimental import pallas as pl
from jax.experimental.pallas import tpu as pltpu
from jax.sharding import PartitionSpec as P

HEAD_DIM = 128


EPSILON = 1e-06
NEGATIVE = -1e30
WEIGHT_GATHER_BYTES = 24 * 2**20


def normalize(values):
    return values * lax.rsqrt(jnp.mean(values * values, axis=-1, keepdims=True) + EPSILON)


def snake_cycle(count):
    return list(range(0, count, 2)) + list(range(count - 1, 0, -2)) if count % 2 == 0 else list(range(count))


def ring_gather(block, axis_name, count):
    cycle = snake_cycle(count)
    ahead = [(cycle[p], cycle[(p + 1) % count]) for p in range(count)]
    behind = [(cycle[p], cycle[(p - 1) % count]) for p in range(count)]
    blocks = [block]
    forward = block
    for _ in range(count // 2):
        forward = lax.ppermute(forward, axis_name, ahead)
        blocks.append(forward)
    backward = block
    for _ in range((count - 1) // 2):
        backward = lax.ppermute(backward, axis_name, behind)
        blocks.append(backward)
    return blocks


def ring_reduce_scatter(terms, axis_name, count):
    token_count, width = terms.shape
    block = width // count
    half = block // 2
    cycle = snake_cycle(count)
    position = jnp.array([cycle.index(t) for t in range(count)], jnp.int32)[lax.axis_index(axis_name)]
    owners = jnp.array(cycle, jnp.int32)
    rounded = terms.astype(jnp.bfloat16)

    def own_part(slot, side):
        start = owners[slot % count] * block + side * half
        return lax.dynamic_slice_in_dim(rounded, start, half, 1).astype(jnp.float32)

    ahead = [(cycle[p], cycle[(p + 1) % count]) for p in range(count)]
    behind = [(cycle[p], cycle[(p - 1) % count]) for p in range(count)]
    forward = own_part(position - 1 + count, 0)
    backward = own_part(position + 1, 1)
    for step in range(count - 1):
        forward = lax.ppermute(forward.astype(jnp.bfloat16), axis_name, ahead).astype(jnp.float32)
        forward = forward + own_part(position - 2 - step + 2 * count, 0)
        backward = lax.ppermute(backward.astype(jnp.bfloat16), axis_name, behind).astype(jnp.float32)
        backward = backward + own_part(position + 2 + step, 1)
    return jnp.concatenate([forward, backward], axis=1)


def out_proj_kernel(group_count, tiles_per_half, row_count, span_ref, *refs):
    att_refs = refs[:group_count]
    mine_refs = refs[group_count:2 * group_count]
    other_refs = refs[2 * group_count:3 * group_count]
    hidden_ref, scale_ref, out_ref, squares_ref = refs[3 * group_count:]
    tile = pl.program_id(0)

    def accumulate(w_refs):
        total = None
        for group in range(group_count):
            term = jnp.dot(att_refs[group][...], w_refs[group][...], preferred_element_type=jnp.float32)
            term = term.astype(jnp.bfloat16).astype(jnp.float32)
            total = term if total is None else total + term
        for span in range(scale_ref.shape[0]):
            rows = slice(span * row_count, (span + 1) * row_count)
            out_ref[rows, :] = (
                hidden_ref[rows, :].astype(jnp.float32) + scale_ref[span:span + 1, :] * total[rows, :]
            )
        result = out_ref[...]
        partial = jnp.broadcast_to(jnp.sum(result * result, axis=1, keepdims=True), squares_ref.shape)

        @pl.when(tile == 0)
        def _():
            squares_ref[...] = partial

        @pl.when(tile > 0)
        def _():
            squares_ref[...] += partial

    @pl.when(tile < tiles_per_half)
    def _():
        accumulate(mine_refs)

    @pl.when(tile >= tiles_per_half)
    def _():
        accumulate(other_refs)


def grouped_out_proj(
    span_index, att_blocks, mine_blocks, other_blocks, hidden, scale, tile_width=1024
):
    group_count = len(att_blocks)
    token_count, head_width = att_blocks[0].shape
    half_width = mine_blocks[0].shape[1]
    span_rows = scale.shape[0]
    tile_width = min(tile_width, half_width)
    tiles_per_half = half_width // tile_width
    att_spec = pl.BlockSpec((token_count, head_width), lambda n, s: (0, 0))
    mine_spec = pl.BlockSpec(
        (head_width, tile_width), lambda n, s: (0, jnp.minimum(n, tiles_per_half - 1))
    )
    other_spec = pl.BlockSpec(
        (head_width, tile_width), lambda n, s: (0, jnp.maximum(n - tiles_per_half, 0))
    )

    def column(n, s):
        return ((n // tiles_per_half + s[0]) % 2) * tiles_per_half + n % tiles_per_half

    out_spec = pl.BlockSpec((token_count, tile_width), lambda n, s: (0, column(n, s)))
    hidden_spec = pl.BlockSpec((token_count, tile_width), lambda n, s: (0, column(n, s)))
    scale_spec = pl.BlockSpec((span_rows, tile_width), lambda n, s: (0, column(n, s)))
    squares_spec = pl.BlockSpec((token_count, 128), lambda n, s: (0, 0))
    tile_count = 2 * tiles_per_half
    flops = 2 * token_count * head_width * group_count * half_width * 2
    moved = 2 * (group_count * token_count * head_width + 2 * group_count * head_width * half_width)
    moved += token_count * 2 * half_width * (4 + 2)
    residual, squares = pl.pallas_call(
        functools.partial(out_proj_kernel, group_count, tiles_per_half, token_count // span_rows),
        out_shape=(
            jax.ShapeDtypeStruct((token_count, 2 * half_width), jnp.float32),
            jax.ShapeDtypeStruct((token_count, 128), jnp.float32),
        ),
        grid_spec=pltpu.PrefetchScalarGridSpec(
            num_scalar_prefetch=1,
            grid=(tile_count,),
            in_specs=[att_spec] * group_count + [mine_spec] * group_count + [other_spec] * group_count
            + [hidden_spec, scale_spec],
            out_specs=[out_spec, squares_spec],
        ),
        cost_estimate=pl.CostEstimate(flops=flops, bytes_accessed=moved, transcendentals=0),
    )(
        jnp.reshape(span_index, (1,)).astype(jnp.int32),
        *att_blocks,
        *mine_blocks,
        *other_blocks,
        hidden,
        scale,
    )
    return residual, squares[:, 0]


def select_row(source, target):
    matches = jnp.arange(source.shape[0], dtype=jnp.int32) == target
    return jnp.sum(jnp.where(matches.reshape((-1,) + (1,) * (source.ndim - 1)), source, 0), axis=0)


def attend(queries, cache_all, fresh_all, cache_seen, fresh_seen):
    row_count, head_count, head_size = queries.shape
    cache_keys = cache_all[:, :, 0].reshape(-1, head_count, head_size)
    cache_vals = cache_all[:, :, 1].reshape(-1, head_count, head_size)
    fresh_keys = fresh_all[:, :, 0].reshape(-1, head_count, head_size)
    fresh_vals = fresh_all[:, :, 1].reshape(-1, head_count, head_size)
    score_scale = 1.0 / math.sqrt(head_size)
    cache_scores = (
        jnp.einsum("qhd,khd->hqk", queries, cache_keys, preferred_element_type=jnp.float32)
        * score_scale
    )
    fresh_scores = (
        jnp.einsum("qhd,khd->hqk", queries, fresh_keys, preferred_element_type=jnp.float32)
        * score_scale
    )
    cache_scores = jnp.where(cache_seen[None, None, :], cache_scores, NEGATIVE)
    fresh_scores = jnp.where(fresh_seen[None, None, :], fresh_scores, NEGATIVE)
    scores = jnp.concatenate([cache_scores, fresh_scores], axis=2)
    row_max = jnp.max(scores, axis=2, keepdims=True)
    exp_terms = jnp.exp(scores - row_max)
    weights = (exp_terms / jnp.sum(exp_terms, axis=2, keepdims=True)).astype(jnp.bfloat16)
    split_at = cache_keys.shape[0]
    attended = jnp.einsum(
        "hqk,khd->qhd", weights[:, :, :split_at], cache_vals, preferred_element_type=jnp.float32
    )
    attended = attended + jnp.einsum(
        "hqk,khd->qhd", weights[:, :, split_at:], fresh_vals, preferred_element_type=jnp.float32
    )
    return attended.astype(jnp.bfloat16).reshape(row_count, head_count * head_size)


def local(
    hidden_in, levels, order, cache_mask, finished, cache_kv, modulation, w_qkv, w_out, w_up, w_down
):
    span_index = lax.axis_index("span")
    tp_rank = lax.axis_index("tp")
    span_count = lax.psum(1, "span")
    tp_count = lax.psum(1, "tp")
    model_width = modulation.shape[2]
    share_width = hidden_in.shape[2]
    local_count = hidden_in.shape[0]
    row_count = hidden_in.shape[1]
    token_count = local_count * row_count
    gather_weights = (
        tp_count * w_out.size * w_out.dtype.itemsize <= WEIGHT_GATHER_BYTES and span_count == 2
    )
    if gather_weights:
        cycle = snake_cycle(tp_count)
        position = jnp.array([cycle.index(t) for t in range(tp_count)], jnp.int32)[tp_rank]
        steps = list(range(tp_count // 2 + 1)) + [-k for k in range(1, (tp_count - 1) // 2 + 1)]
        owners = jnp.array(cycle, jnp.int32)
        gathered = jnp.zeros(hidden_in.shape[:2] + (model_width,), hidden_in.dtype)
        for step, piece in zip(steps, ring_gather(hidden_in, "tp", tp_count)):
            owner = owners[(position - step + tp_count) % tp_count]
            gathered = lax.dynamic_update_slice_in_dim(gathered, piece, owner * share_width, 2)
        gathered_narrow = gathered
        gathered = gathered.astype(jnp.float32)
    else:
        gathered = lax.all_gather(hidden_in, "tp", axis=2, tiled=True).astype(jnp.float32)
    if gather_weights:
        column_part = model_width // span_count
        w_out_part = lax.dynamic_slice_in_dim(w_out, span_index * column_part, column_part, 1)
        mine_blocks = ring_gather(w_out_part, "tp", tp_count)
        other_blocks = [lax.ppermute(b, "span", [(0, 1), (1, 0)]) for b in mine_blocks]
    if gather_weights:
        swap = [(0, 1), (1, 0)]
        up_full = down_full = None
    else:
        up_full, down_full = (
            lax.all_gather(w_up, "span", axis=1, tiled=True),
            lax.all_gather(w_down, "span", axis=0, tiled=True),
        )
    mod_table = modulation.reshape(modulation.shape[0], -1)
    picker = (jnp.arange(mod_table.shape[0], dtype=jnp.int32)[None, :] == levels[:, None]).astype(
        jnp.bfloat16
    )
    mod_rows = jnp.dot(picker, mod_table, preferred_element_type=jnp.float32).reshape(
        local_count, 6, model_width
    )
    attn_in = (normalize(gathered) * mod_rows[:, 1][:, None] + mod_rows[:, 0][:, None]).astype(
        jnp.bfloat16
    )
    per_device = w_qkv.shape[2]
    projected = jnp.dot(
        attn_in.reshape(token_count, model_width),
        w_qkv.reshape(model_width, -1),
        preferred_element_type=jnp.float32,
    )
    projected = projected.astype(jnp.bfloat16).reshape(local_count, row_count, 3, per_device)
    queries = projected[:, :, 0].reshape(local_count, row_count, -1, HEAD_DIM)
    fresh_kv = projected[:, :, 1:]
    cache_all, fresh_all = (
        lax.all_gather(cache_kv, "span", axis=0, tiled=True),
        lax.all_gather(fresh_kv, "span", axis=0, tiled=True),
    )
    positions = jnp.arange(cache_mask.shape[0], dtype=jnp.int32)
    my_spans = span_index * local_count + jnp.arange(local_count, dtype=jnp.int32)
    mask_rows = jax.vmap(lambda target: select_row(cache_mask, target))(my_spans)
    my_order = jax.vmap(lambda target: select_row(order, target))(my_spans)
    cache_seen = jnp.repeat(
        (mask_rows == 1) | (positions[None, :] == finished[0]), row_count, axis=1
    )
    fresh_seen = jnp.repeat(order[None, :] <= my_order[:, None], row_count, axis=1)
    attended = jax.vmap(
        lambda q_rows, c_seen, f_seen: attend(q_rows, cache_all, fresh_all, c_seen, f_seen)
    )(queries, cache_seen, fresh_seen)
    if gather_weights:
        att_blocks = ring_gather(attended.reshape(token_count, per_device), "tp", tp_count)
        last_block, up_late, down_late = lax.optimization_barrier((att_blocks[-1], w_up, w_down))
        att_blocks[-1] = last_block
        swap = [(0, 1), (1, 0)]
        up_full = jnp.concatenate([up_late, lax.ppermute(up_late, "span", swap)], axis=1)
        down_full = jnp.concatenate([down_late, lax.ppermute(down_late, "span", swap)], axis=0)
        residual_rows, square_sums = grouped_out_proj(
            span_index,
            att_blocks,
            mine_blocks,
            other_blocks,
            gathered_narrow.reshape(token_count, model_width),
            mod_rows[:, 2],
        )
        residual_full = residual_rows.reshape(local_count, row_count, model_width)
        inverse = lax.rsqrt(square_sums.reshape(local_count, row_count, 1) / model_width + EPSILON)
        mlp_in = (
            residual_full * inverse * mod_rows[:, 4][:, None] + mod_rows[:, 3][:, None]
        ).astype(jnp.bfloat16)
    else:
        partial_value = jnp.dot(
            attended.reshape(token_count, -1), w_out, preferred_element_type=jnp.float32
        ).reshape(local_count, row_count, model_width)
        attn_part = lax.psum_scatter(
            partial_value.astype(jnp.bfloat16), "tp", scatter_dimension=2, tiled=True
        ).astype(jnp.float32)
        mod_share = lax.dynamic_slice_in_dim(mod_rows, tp_rank * share_width, share_width, 2)
        residual = hidden_in.astype(jnp.float32) + mod_share[:, 2][:, None] * attn_part
        squares = lax.psum(jnp.sum(residual * residual, axis=2), "tp")
        scaled = residual * lax.rsqrt(squares / model_width + EPSILON)[:, :, None]
        mlp_part = (scaled * mod_share[:, 4][:, None] + mod_share[:, 3][:, None]).astype(
            jnp.bfloat16
        )
        mlp_in = lax.all_gather(mlp_part, "tp", axis=2, tiled=True)
    pre_act = jnp.dot(mlp_in, up_full, preferred_element_type=jnp.float32)
    hidden_units = jax.nn.gelu(pre_act).astype(jnp.bfloat16)
    down_terms = jnp.dot(hidden_units, down_full, preferred_element_type=jnp.float32)
    if gather_weights:
        mlp_out = ring_reduce_scatter(
            down_terms.reshape(token_count, model_width), "tp", tp_count
        ).reshape(local_count, row_count, share_width)
    else:
        mlp_out = lax.psum_scatter(
            down_terms.astype(jnp.bfloat16), "tp", scatter_dimension=2, tiled=True
        ).astype(jnp.float32)
    if gather_weights:
        residual = lax.dynamic_slice_in_dim(residual_full, tp_rank * share_width, share_width, 2)
        mod_share = lax.dynamic_slice_in_dim(mod_rows, tp_rank * share_width, share_width, 2)
    result = residual + mod_share[:, 5][:, None] * mlp_out
    return result.astype(jnp.bfloat16)


def solution(mesh):
    placed = (
        P(("rep", "span"), None, "tp"),
        P(("rep", "span")),
        P("rep"),
        P("rep", None),
        P("rep"),
        P(("rep", "span"), None, None, "tp"),
        P(),
        P(None, None, "tp"),
        P("tp", None),
        P(None, ("span", "tp")),
        P(("span", "tp"), None),
    )
    return jax.shard_map(
        local, mesh=mesh, in_specs=placed, out_specs=P(("rep", "span"), None, "tp"), check_vma=False
    )
```

```python
import functools
import math

import jax
import jax.numpy as jnp
from jax import lax
from jax.experimental import pallas as pl
from jax.experimental.pallas import tpu as pltpu
from jax.sharding import PartitionSpec as P

HEAD_DIM = 128


EPSILON = 1e-06
NEGATIVE = -1e30
WEIGHT_GATHER_BYTES = 24 * 2**20


def normalize(values):
    return values * lax.rsqrt(jnp.mean(values * values, axis=-1, keepdims=True) + EPSILON)


def snake_cycle(count):
    return list(range(0, count, 2)) + list(range(count - 1, 0, -2)) if count % 2 == 0 else list(range(count))


def ring_gather(block, axis_name, count):
    cycle = snake_cycle(count)
    ahead = [(cycle[p], cycle[(p + 1) % count]) for p in range(count)]
    behind = [(cycle[p], cycle[(p - 1) % count]) for p in range(count)]
    blocks = [block]
    forward = block
    for _ in range(count // 2):
        forward = lax.ppermute(forward, axis_name, ahead)
        blocks.append(forward)
    backward = block
    for _ in range((count - 1) // 2):
        backward = lax.ppermute(backward, axis_name, behind)
        blocks.append(backward)
    return blocks


def ring_reduce_scatter(terms, axis_name, count):
    token_count, width = terms.shape
    block = width // count
    half = block // 2
    cycle = snake_cycle(count)
    position = jnp.array([cycle.index(t) for t in range(count)], jnp.int32)[lax.axis_index(axis_name)]
    owners = jnp.array(cycle, jnp.int32)
    rounded = terms.astype(jnp.bfloat16)

    def own_part(slot, side):
        start = owners[slot % count] * block + side * half
        return lax.dynamic_slice_in_dim(rounded, start, half, 1).astype(jnp.float32)

    ahead = [(cycle[p], cycle[(p + 1) % count]) for p in range(count)]
    behind = [(cycle[p], cycle[(p - 1) % count]) for p in range(count)]
    forward = own_part(position - 1 + count, 0)
    backward = own_part(position + 1, 1)
    for step in range(count - 1):
        forward = lax.ppermute(forward.astype(jnp.bfloat16), axis_name, ahead).astype(jnp.float32)
        forward = forward + own_part(position - 2 - step + 2 * count, 0)
        backward = lax.ppermute(backward.astype(jnp.bfloat16), axis_name, behind).astype(jnp.float32)
        backward = backward + own_part(position + 2 + step, 1)
    return jnp.concatenate([forward, backward], axis=1)


def out_proj_kernel(group_count, row_count, span_ref, *refs):
    att_refs = refs[:group_count]
    w_refs = refs[group_count:2 * group_count]
    hidden_ref, scale_ref = refs[2 * group_count:2 * group_count + 2]
    out_ref, squares_ref = refs[-2:]
    tile = pl.program_id(0)
    total = None
    for group in range(group_count):
        term = jnp.dot(att_refs[group][...], w_refs[group][...], preferred_element_type=jnp.float32)
        term = term.astype(jnp.bfloat16).astype(jnp.float32)
        total = term if total is None else total + term
    for span in range(scale_ref.shape[0]):
        rows = slice(span * row_count, (span + 1) * row_count)
        out_ref[rows, :] = (
            hidden_ref[rows, :].astype(jnp.float32) + scale_ref[span:span + 1, :] * total[rows, :]
        )
    result = out_ref[...]
    partial = jnp.broadcast_to(jnp.sum(result * result, axis=1, keepdims=True), squares_ref.shape)

    @pl.when(tile == 0)
    def _():
        squares_ref[...] = partial

    @pl.when(tile > 0)
    def _():
        squares_ref[...] += partial


def grouped_out_half(span_index, half, att_blocks, w_blocks, hidden, scale, earlier=None, tile_width=1024):
    group_count = len(att_blocks)
    token_count, head_width = att_blocks[0].shape
    half_width = w_blocks[0].shape[1]
    span_rows = scale.shape[0]
    tile_width = min(tile_width, half_width)
    tiles = half_width // tile_width

    def column(n, s):
        return ((half + s[0]) % 2) * tiles + n

    att_spec = pl.BlockSpec((token_count, head_width), lambda n, s: (0, 0))
    w_spec = pl.BlockSpec((head_width, tile_width), lambda n, s: (0, n))
    tile_spec = pl.BlockSpec((token_count, tile_width), lambda n, s: (0, column(n, s)))
    scale_spec = pl.BlockSpec((span_rows, tile_width), lambda n, s: (0, column(n, s)))
    squares_spec = pl.BlockSpec((token_count, 128), lambda n, s: (0, 0))
    in_specs = [att_spec] * group_count + [w_spec] * group_count + [tile_spec, scale_spec]
    operands = [jnp.reshape(span_index, (1,)).astype(jnp.int32), *att_blocks, *w_blocks, hidden, scale]
    aliases = {}
    if earlier is not None:
        in_specs.append(pl.BlockSpec(memory_space=pl.ANY))
        aliases = {len(operands): 0}
        operands.append(earlier)
    flops = 2 * token_count * head_width * group_count * half_width
    moved = 2 * (group_count * token_count * head_width + group_count * head_width * half_width)
    moved += token_count * half_width * (4 + 2)
    body = functools.partial(out_proj_kernel, group_count, token_count // span_rows)
    if earlier is not None:
        plain = body

        def body(span_ref, *refs):
            plain(span_ref, *refs[:2 * group_count + 2], *refs[2 * group_count + 3:])

    return pl.pallas_call(
        body,
        out_shape=(
            jax.ShapeDtypeStruct((token_count, 2 * half_width), jnp.float32),
            jax.ShapeDtypeStruct((token_count, 128), jnp.float32),
        ),
        grid_spec=pltpu.PrefetchScalarGridSpec(
            num_scalar_prefetch=1,
            grid=(tiles,),
            in_specs=in_specs,
            out_specs=[tile_spec, squares_spec],
        ),
        input_output_aliases=aliases,
        cost_estimate=pl.CostEstimate(flops=flops, bytes_accessed=moved, transcendentals=0),
    )(*operands)


def select_row(source, target):
    matches = jnp.arange(source.shape[0], dtype=jnp.int32) == target
    return jnp.sum(jnp.where(matches.reshape((-1,) + (1,) * (source.ndim - 1)), source, 0), axis=0)


def attend(queries, cache_all, fresh_all, cache_seen, fresh_seen):
    row_count, head_count, head_size = queries.shape
    cache_keys = cache_all[:, :, 0].reshape(-1, head_count, head_size)
    cache_vals = cache_all[:, :, 1].reshape(-1, head_count, head_size)
    fresh_keys = fresh_all[:, :, 0].reshape(-1, head_count, head_size)
    fresh_vals = fresh_all[:, :, 1].reshape(-1, head_count, head_size)
    score_scale = 1.0 / math.sqrt(head_size)
    cache_scores = (
        jnp.einsum("qhd,khd->hqk", queries, cache_keys, preferred_element_type=jnp.float32)
        * score_scale
    )
    fresh_scores = (
        jnp.einsum("qhd,khd->hqk", queries, fresh_keys, preferred_element_type=jnp.float32)
        * score_scale
    )
    cache_scores = jnp.where(cache_seen[None, None, :], cache_scores, NEGATIVE)
    fresh_scores = jnp.where(fresh_seen[None, None, :], fresh_scores, NEGATIVE)
    scores = jnp.concatenate([cache_scores, fresh_scores], axis=2)
    row_max = jnp.max(scores, axis=2, keepdims=True)
    exp_terms = jnp.exp(scores - row_max)
    weights = (exp_terms / jnp.sum(exp_terms, axis=2, keepdims=True)).astype(jnp.bfloat16)
    split_at = cache_keys.shape[0]
    attended = jnp.einsum(
        "hqk,khd->qhd", weights[:, :, :split_at], cache_vals, preferred_element_type=jnp.float32
    )
    attended = attended + jnp.einsum(
        "hqk,khd->qhd", weights[:, :, split_at:], fresh_vals, preferred_element_type=jnp.float32
    )
    return attended.astype(jnp.bfloat16).reshape(row_count, head_count * head_size)


def local(
    hidden_in, levels, order, cache_mask, finished, cache_kv, modulation, w_qkv, w_out, w_up, w_down
):
    span_index = lax.axis_index("span")
    tp_rank = lax.axis_index("tp")
    span_count = lax.psum(1, "span")
    tp_count = lax.psum(1, "tp")
    model_width = modulation.shape[2]
    share_width = hidden_in.shape[2]
    local_count = hidden_in.shape[0]
    row_count = hidden_in.shape[1]
    token_count = local_count * row_count
    gather_weights = (
        tp_count * w_out.size * w_out.dtype.itemsize <= WEIGHT_GATHER_BYTES and span_count == 2
    )
    if gather_weights:
        cycle = snake_cycle(tp_count)
        position = jnp.array([cycle.index(t) for t in range(tp_count)], jnp.int32)[tp_rank]
        steps = list(range(tp_count // 2 + 1)) + [-k for k in range(1, (tp_count - 1) // 2 + 1)]
        owners = jnp.array(cycle, jnp.int32)
        gathered = jnp.zeros(hidden_in.shape[:2] + (model_width,), hidden_in.dtype)
        for step, piece in zip(steps, ring_gather(hidden_in, "tp", tp_count)):
            owner = owners[(position - step + tp_count) % tp_count]
            gathered = lax.dynamic_update_slice_in_dim(gathered, piece, owner * share_width, 2)
        gathered_narrow = gathered
        gathered = gathered.astype(jnp.float32)
    else:
        gathered = lax.all_gather(hidden_in, "tp", axis=2, tiled=True).astype(jnp.float32)
    if gather_weights:
        column_part = model_width // span_count
        w_out_part = lax.dynamic_slice_in_dim(w_out, span_index * column_part, column_part, 1)
        mine_blocks = ring_gather(w_out_part, "tp", tp_count)
        other_blocks = [lax.ppermute(b, "span", [(0, 1), (1, 0)]) for b in mine_blocks]
    up_full, down_full = (
        lax.all_gather(w_up, "span", axis=1, tiled=True),
        lax.all_gather(w_down, "span", axis=0, tiled=True),
    )
    mod_table = modulation.reshape(modulation.shape[0], -1)
    picker = (jnp.arange(mod_table.shape[0], dtype=jnp.int32)[None, :] == levels[:, None]).astype(
        jnp.bfloat16
    )
    mod_rows = jnp.dot(picker, mod_table, preferred_element_type=jnp.float32).reshape(
        local_count, 6, model_width
    )
    attn_in = (normalize(gathered) * mod_rows[:, 1][:, None] + mod_rows[:, 0][:, None]).astype(
        jnp.bfloat16
    )
    per_device = w_qkv.shape[2]
    projected = jnp.dot(
        attn_in.reshape(token_count, model_width),
        w_qkv.reshape(model_width, -1),
        preferred_element_type=jnp.float32,
    )
    projected = projected.astype(jnp.bfloat16).reshape(local_count, row_count, 3, per_device)
    queries = projected[:, :, 0].reshape(local_count, row_count, -1, HEAD_DIM)
    fresh_kv = projected[:, :, 1:]
    cache_all, fresh_all = (
        lax.all_gather(cache_kv, "span", axis=0, tiled=True),
        lax.all_gather(fresh_kv, "span", axis=0, tiled=True),
    )
    positions = jnp.arange(cache_mask.shape[0], dtype=jnp.int32)
    my_spans = span_index * local_count + jnp.arange(local_count, dtype=jnp.int32)
    mask_rows = jax.vmap(lambda target: select_row(cache_mask, target))(my_spans)
    my_order = jax.vmap(lambda target: select_row(order, target))(my_spans)
    cache_seen = jnp.repeat(
        (mask_rows == 1) | (positions[None, :] == finished[0]), row_count, axis=1
    )
    fresh_seen = jnp.repeat(order[None, :] <= my_order[:, None], row_count, axis=1)
    attended = jax.vmap(
        lambda q_rows, c_seen, f_seen: attend(q_rows, cache_all, fresh_all, c_seen, f_seen)
    )(queries, cache_seen, fresh_seen)
    if gather_weights:
        att_blocks = ring_gather(attended.reshape(token_count, per_device), "tp", tp_count)
        hidden_rows = gathered_narrow.reshape(token_count, model_width)
        first, first_squares = grouped_out_half(
            span_index, 0, att_blocks, mine_blocks, hidden_rows, mod_rows[:, 2]
        )
        residual_rows, second_squares = grouped_out_half(
            span_index, 1, att_blocks, other_blocks, hidden_rows, mod_rows[:, 2], earlier=first
        )
        square_sums = first_squares[:, 0] + second_squares[:, 0]
        residual_full = residual_rows.reshape(local_count, row_count, model_width)
        inverse = lax.rsqrt(square_sums.reshape(local_count, row_count, 1) / model_width + EPSILON)
        mlp_in = (
            residual_full * inverse * mod_rows[:, 4][:, None] + mod_rows[:, 3][:, None]
        ).astype(jnp.bfloat16)
    else:
        partial_value = jnp.dot(
            attended.reshape(token_count, -1), w_out, preferred_element_type=jnp.float32
        ).reshape(local_count, row_count, model_width)
        attn_part = lax.psum_scatter(
            partial_value.astype(jnp.bfloat16), "tp", scatter_dimension=2, tiled=True
        ).astype(jnp.float32)
        mod_share = lax.dynamic_slice_in_dim(mod_rows, tp_rank * share_width, share_width, 2)
        residual = hidden_in.astype(jnp.float32) + mod_share[:, 2][:, None] * attn_part
        squares = lax.psum(jnp.sum(residual * residual, axis=2), "tp")
        scaled = residual * lax.rsqrt(squares / model_width + EPSILON)[:, :, None]
        mlp_part = (scaled * mod_share[:, 4][:, None] + mod_share[:, 3][:, None]).astype(
            jnp.bfloat16
        )
        mlp_in = lax.all_gather(mlp_part, "tp", axis=2, tiled=True)
    pre_act = jnp.dot(mlp_in, up_full, preferred_element_type=jnp.float32)
    hidden_units = jax.nn.gelu(pre_act).astype(jnp.bfloat16)
    down_terms = jnp.dot(hidden_units, down_full, preferred_element_type=jnp.float32)
    if gather_weights:
        mlp_out = ring_reduce_scatter(
            down_terms.reshape(token_count, model_width), "tp", tp_count
        ).reshape(local_count, row_count, share_width)
    else:
        mlp_out = lax.psum_scatter(
            down_terms.astype(jnp.bfloat16), "tp", scatter_dimension=2, tiled=True
        ).astype(jnp.float32)
    if gather_weights:
        residual = lax.dynamic_slice_in_dim(residual_full, tp_rank * share_width, share_width, 2)
        mod_share = lax.dynamic_slice_in_dim(mod_rows, tp_rank * share_width, share_width, 2)
    result = residual + mod_share[:, 5][:, None] * mlp_out
    return result.astype(jnp.bfloat16)


def solution(mesh):
    placed = (
        P(("rep", "span"), None, "tp"),
        P(("rep", "span")),
        P("rep"),
        P("rep", None),
        P("rep"),
        P(("rep", "span"), None, None, "tp"),
        P(),
        P(None, None, "tp"),
        P("tp", None),
        P(None, ("span", "tp")),
        P(("span", "tp"), None),
    )
    return jax.shard_map(
        local, mesh=mesh, in_specs=placed, out_specs=P(("rep", "span"), None, "tp"), check_vma=False
    )
```
